32 devices in a mesh: groups: 2 (over y), seq: 4 (over z), chan: 2 (over x), pair: 2 (over core).
Axes of the slice: x: 2, y: 2, z: 4, core: 2. Of those that a mesh axis runs over, the one named last changes fastest.
Arguments:
- tokens: int32 [1024], P(('groups', 'seq')), parts along dimension 0, may hold values from 0 to 4
- kmer_table: bfloat16 [4, 5, 2048], replicated, may hold values from -3 to 3
- norm_gain: float32 [2048], replicated, may hold values from 0.3 to 2, as said below
- in_proj: bfloat16 [2048, 3, 2048], P(None, None, ('chan', 'pair')), may hold values from -0.125 to 0.125
- long_filter: float32 [4, 4, 128, 512], P(('chan', 'pair'), 'seq'), may hold values from -1 to 1, as said below
- out_proj: bfloat16 [2048, 2048], P(None, ('chan', 'pair')), may hold values from -0.125 to 0.125
- cotangent: bfloat16 [1024, 2048], P(('groups', 'seq'), ('chan', 'pair')), parts along dimension 0, may hold values from -6 to 6
Outputs:
- block_out: bfloat16 [1024, 2048], P(('groups', 'seq'), ('chan', 'pair')), parts along dimension 0
- filter_grad: float32 [8, 4, 128, 512], P(('groups', 'chan', 'pair'), 'seq'), parts along dimension 0
- kmer_grad: float32 [8, 5, 2048], P('groups', None, ('chan', 'pair')), parts along dimension 0
- gain_grad: float32 [4096], P(('groups', 'chan', 'pair')), parts along dimension 0
The draws below stay inside these ranges and needn't reach their ends.
There are 2 independent parts, one for each index of `groups`. The reference program is written for one: setup_inputs(seed, part) draws one part's arguments, and reference() takes and returns one part's arrays. A program takes and returns all parts, laid end to end along the dimension named above; an argument that names none is the same for every part. Nothing has to cross between parts.
Inputs may be any that keep to these rules, and one draw needn't show every extreme that they name: `tokens`: nucleotide ids: 0 to 3 for A, C, G, T and 4 for N. `long_filter`: a causal filter for each channel. `norm_gain`: a positive gain for each channel.
All inputs are finite; a program needn't handle non-finite values.
Results may differ from the reference program's by a relative error of at most 0.0072.
Values may be sent and summed in bfloat16 or wider, within the bound.
No kernel may reach another device: no remote copies, remote signals or barrier semaphores. Data moves between devices by JAX's collectives and lax.ppermute only.
A program may use at most 128 MiB of HBM per device.

```python
import math
import jax
import jax.numpy as jnp
from jax import lax

D = 2048
KMER = 4
ALPHA = 5
SHARDS = 4
CG = 4
CH = 128
L = 512


def draw_long_filter(key, part):
    rate_key, noise_key = jax.random.split(jax.random.fold_in(key, 11))
    log_rate = jax.random.uniform(rate_key, (D, 1), jnp.float32, math.log(0.5 / L), math.log(1.0 / 40.0))
    decay_rate = jnp.exp(log_rate)
    positions = jnp.arange(L, dtype=jnp.float32)[None, :]
    envelope = jnp.exp(-decay_rate * positions) * jnp.sqrt(2.0 * decay_rate)
    noise_part = jnp.clip(jax.random.normal(noise_key, (D, L), jnp.float32), -4.0, 4.0)
    return (noise_part * envelope).reshape(CG, SHARDS, CH, L).astype(jnp.float32)


def draw_norm_gain(key, part):
    ramp_part = 0.5 + jnp.arange(D, dtype=jnp.float32) / D
    factor = jax.random.uniform(jax.random.fold_in(key, 23), (D,), jnp.float32, 0.75, 1.25)
    return (ramp_part * factor).astype(jnp.float32)


def with_ends(entries, rng, smallest, largest):
    place = [jax.random.randint(jax.random.fold_in(rng, axis), (), 0, length) for axis, length in enumerate(entries.shape)]
    main_axis = entries.shape.index(max(entries.shape))
    neighbour = place[:main_axis] + [(place[main_axis] + 1) % entries.shape[main_axis]] + place[main_axis + 1:]
    return entries.at[tuple(place)].set(smallest).at[tuple(neighbour)].set(largest)


def shard_levels(rng, dims, shards, low, high):
    loudness, own = 1.0, jax.random.fold_in(rng, 6)
    for dim, blocks in shards:
        draws = jnp.exp(jax.random.uniform(jax.random.fold_in(own, dim), (blocks,), jnp.float32, low / len(shards), high / len(shards)))
        loudness = loudness * jnp.repeat(draws, dims[dim] // blocks).reshape([-1 if axis == dim else 1 for axis in range(len(dims))])
    return loudness


def centred(own_key, extent, deviation, most, pieces=(), kind=jnp.bfloat16):
    loudness = shard_levels(own_key, extent, pieces, -0.22, 0.18) if pieces else 1.0
    result = jax.random.normal(own_key, extent, jnp.float32) * deviation * loudness
    return jnp.minimum(jnp.maximum(result, -most), most).astype(kind)


def setup_inputs(seed: int = 0, part: int = 0) -> dict:
    seeds = jax.random.split(jax.random.key(seed), 8)
    part_keys = jax.random.split(jax.random.fold_in(seeds[7], part), 8)
    return {
        "tokens": with_ends(jax.random.randint(part_keys[0], (L,), 0, 5), jax.random.fold_in(part_keys[0], 1), 0, 4).astype(jnp.int32),
        "kmer_table": centred(seeds[1], (KMER, ALPHA, D), 0.5, 3.0),
        "norm_gain": draw_norm_gain(jax.random.fold_in(seeds[7], 71), part),
        "in_proj": centred(seeds[3], (D, 3, D), D ** -0.5, 0.125, ((2, 4),)),
        "long_filter": draw_long_filter(jax.random.fold_in(seeds[7], 71), part),
        "out_proj": centred(seeds[5], (D, D), D ** -0.5, 0.125, ((1, 4),)),
        "cotangent": centred(part_keys[6], (L, D), 1.0, 6.0, ((0, 4), (1, 4))),
    }


NORM_EPSILON = 1e-05
PRECISE = lax.Precision.HIGHEST

def flip_pairs(values):
    return values.reshape(values.shape[0], values.shape[1] // 2, 2)[:, :, ::-1].reshape(values.shape)

def reference(tokens, kmer_table, norm_gain, in_proj, long_filter, out_proj, cotangent):
    kmer_len, letter_count, model_width = kmer_table.shape
    length = tokens.shape[0]
    total_len = 2 * length
    padded = jnp.concatenate([jnp.full((kmer_len - 1,), -1, jnp.int32), tokens.astype(jnp.int32)])
    letters = jnp.arange(letter_count, dtype=jnp.int32)
    columns = []
    for shift_back in range(kmer_len):
        window = padded[kmer_len - 1 - shift_back:kmer_len - 1 - shift_back + length]
        columns.append(window[:, None] == letters[None, :])
    onehot = jnp.concatenate(columns, axis=1).astype(jnp.bfloat16)
    embedded = jnp.dot(onehot, kmer_table.reshape(kmer_len * letter_count, model_width), preferred_element_type=jnp.float32)
    inv_rms = lax.rsqrt(lax.optimization_barrier(jnp.mean(embedded * embedded, axis=1, keepdims=True)) + NORM_EPSILON)
    normed = embedded * inv_rms
    hidden = (normed * norm_gain[None, :]).astype(jnp.bfloat16)
    projected = jnp.dot(hidden, in_proj.reshape(model_width, 3 * model_width), preferred_element_type=jnp.float32)
    projected = projected.reshape(length, 3, model_width)
    query_part = projected[:, 0]
    key_part = projected[:, 1]
    value_part = projected[:, 2]
    mixed = (key_part * value_part).astype(jnp.bfloat16)
    filter_cols = long_filter.reshape(model_width, length).T
    spec_s = jnp.fft.rfft(mixed.astype(jnp.float32), n=total_len, axis=0)
    spec_h = jnp.fft.rfft(filter_cols, n=total_len, axis=0)
    spec_g = spec_h + jnp.conj(flip_pairs(spec_h))
    conv_out = jnp.fft.irfft(spec_g * spec_s, n=total_len, axis=0)[:length].astype(jnp.bfloat16)
    gated = (query_part * conv_out.astype(jnp.float32)).astype(jnp.bfloat16)
    block_out = (embedded + jnp.dot(gated, out_proj, preferred_element_type=jnp.float32)).astype(jnp.bfloat16)
    grad_scale = 1.0 / math.sqrt(length)
    d_gated = jnp.dot(cotangent, out_proj.T, preferred_element_type=jnp.float32) * grad_scale
    d_conv = (d_gated * query_part).astype(jnp.bfloat16)
    d_query = d_gated * conv_out.astype(jnp.float32)
    spec_d = jnp.fft.rfft(d_conv.astype(jnp.float32), n=total_len, axis=0)
    d_mixed = jnp.fft.irfft(jnp.conj(spec_g) * spec_d, n=total_len, axis=0)[:length].astype(jnp.bfloat16)
    cross_spec = jnp.conj(spec_s) * spec_d
    filter_cols_grad = jnp.fft.irfft(cross_spec + flip_pairs(jnp.conj(cross_spec)), n=total_len, axis=0)[:length]
    filter_grad = filter_cols_grad.T.reshape(long_filter.shape)
    d_key = d_mixed.astype(jnp.float32) * value_part
    d_value = d_mixed.astype(jnp.float32) * key_part
    d_proj = jnp.stack([d_query, d_key, d_value], axis=1).astype(jnp.bfloat16)
    d_hidden = jnp.dot(d_proj.reshape(length, 3 * model_width), in_proj.reshape(model_width, 3 * model_width).T, preferred_element_type=jnp.float32)
    gain_grad = lax.optimization_barrier(jnp.sum(d_hidden * normed, axis=0))
    scaled = norm_gain[None, :] * d_hidden
    row_stat = lax.optimization_barrier(jnp.mean(scaled * normed, axis=1, keepdims=True))
    d_embedded = inv_rms * (scaled - normed * row_stat) + cotangent.astype(jnp.float32) * grad_scale
    kmer_flat = jnp.dot(onehot.astype(jnp.float32).T, d_embedded, precision=PRECISE)
    kmer_grad = kmer_flat.reshape(kmer_len, letter_count, model_width)
    return (block_out, filter_grad, kmer_grad, gain_grad)
```

```python
import math

import jax
import jax.numpy as jnp
from jax import lax
from jax.sharding import PartitionSpec as P

NORM_EPSILON = 1e-05
PRECISE = lax.Precision.HIGHEST
TRANSFORM_PRECISION = lax.Precision.HIGH


def from_behind(value, axis, steps):
    count = lax.axis_size(axis)
    first, last = (max(0, -steps), min(count, count - steps))
    return lax.ppermute(value, axis, [(source, source + steps) for source in range(first, last)])


def dft_matrix(length):
    total = 2 * length
    t = lax.optimization_barrier(lax.broadcasted_iota(jnp.int32, (length, 1), 0))
    j = lax.broadcasted_iota(jnp.int32, (1, total), 1)
    k = jnp.where(j < length, j, j - length)
    k = jnp.where(j == length, length, k)
    idx = (t * k) % total
    idx = jnp.where(j > length, (idx + 3 * total // 4) % total, idx)
    idx = jnp.where(idx >= length, idx - total, idx)
    return lax.optimization_barrier(jnp.cos(idx.astype(jnp.float32) * (2.0 * math.pi / total)))


def forward_dft(signal, dft):
    return jnp.dot(signal.astype(jnp.float32), dft, precision=TRANSFORM_PRECISION)


def inverse_dft(spec, dft):
    length = dft.shape[0]
    total = 2 * length
    col = lax.broadcasted_iota(jnp.int32, (1, total), 1)
    weight = jnp.where(col % length == 0, 1.0 / total, 2.0 / total).astype(jnp.float32)
    return lax.dot_general(
        spec * weight, dft, (((1,), (1,)), ((), ())), precision=TRANSFORM_PRECISION
    )


def halves(spec):
    length = spec.shape[1] // 2
    return spec[:, :length], spec[:, length:]


def first_col(shape):
    return lax.broadcasted_iota(jnp.int32, shape, 1) == 0


def cmul(ga, gb, xa, xb, conj_g):
    edge = first_col(ga.shape)
    sign = -1.0 if conj_g else 1.0
    ya = ga * xa - sign * (gb * xb)
    yb = ga * xb + sign * (gb * xa)
    ya = jnp.where(edge, ga * xa, ya)
    yb = jnp.where(edge, gb * xb, yb)
    return jnp.concatenate([ya, yb], axis=1)


def pair_flip(values):
    rows = lax.broadcasted_iota(jnp.int32, values.shape, 0)
    up = jnp.roll(values, -1, axis=0)
    down = jnp.roll(values, 1, axis=0)
    return jnp.where(rows % 2 == 0, up, down)


def add_conj_flip(spec):
    a, b = halves(spec)
    fa, fb = halves(pair_flip(spec))
    edge = first_col(a.shape)
    return jnp.concatenate([a + fa, jnp.where(edge, b + fb, b - fb)], axis=1)


def per_device(tokens, kmer_table, norm_gain, in_proj, long_filter, out_proj, cotangent):
    row_count = tokens.shape[0]
    kmer_len, letter_count, model_width = kmer_table.shape
    local_width = in_proj.shape[2]
    length = row_count * lax.axis_size("seq")
    group_index = lax.axis_index(("chan", "pair"))
    rim_width = kmer_len - 1
    before = from_behind(tokens[row_count - rim_width :] + 1, "seq", 1) - 1
    extended = jnp.concatenate([before, tokens])
    letters = jnp.arange(letter_count, dtype=jnp.int32)
    columns = []
    for shift_back in range(kmer_len):
        window = extended[rim_width - shift_back : rim_width - shift_back + row_count]
        columns.append(window[:, None] == letters[None, :])
    onehot_t = jnp.concatenate(columns, axis=1).T.astype(jnp.bfloat16)
    table_t = kmer_table.reshape(kmer_len * letter_count, model_width).T
    embedded = jnp.dot(table_t, onehot_t, preferred_element_type=jnp.float32)
    inv_rms = lax.rsqrt(jnp.mean(embedded * embedded, axis=0, keepdims=True) + NORM_EPSILON)
    normed = embedded * inv_rms
    hidden = (normed * norm_gain[:, None]).astype(jnp.bfloat16)
    projected = jnp.einsum("dr,dmc->mcr", hidden, in_proj, preferred_element_type=jnp.float32)
    query_part = projected[0]
    key_part = projected[1]
    value_part = projected[2]
    mixed_in = (key_part * value_part).astype(jnp.bfloat16)
    dft = dft_matrix(length)
    filter_rows = long_filter.reshape(long_filter.shape[2], long_filter.shape[3])
    spec_g = add_conj_flip(forward_dft(filter_rows, dft))
    ga, gb = halves(spec_g)
    mixed_cols = lax.all_to_all(mixed_in, "seq", split_axis=0, concat_axis=1, tiled=True)
    spec_s = forward_dft(mixed_cols, dft)
    sa, sb = halves(spec_s)
    conv_cols = inverse_dft(cmul(ga, gb, sa, sb, False), dft).astype(jnp.bfloat16)
    conv_rows = lax.all_to_all(conv_cols, "seq", split_axis=1, concat_axis=0, tiled=True)
    gated_rows = (query_part * conv_rows.astype(jnp.float32)).astype(jnp.bfloat16)
    weight_rows = out_proj
    mixed_out = jnp.einsum(
        "cr,cd->rd",
        lax.all_gather(gated_rows, ("chan", "pair"), axis=0, tiled=True),
        weight_rows,
        preferred_element_type=jnp.float32,
    )
    own_rows = lax.dynamic_slice_in_dim(embedded, group_index * local_width, local_width, 0)
    block_out = (mixed_out + own_rows.T).astype(jnp.bfloat16)
    grad_scale = 1.0 / math.sqrt(length)
    d_gated = (
        lax.psum_scatter(
            jnp.einsum("cd,rd->cr", weight_rows, cotangent, preferred_element_type=jnp.float32),
            ("chan", "pair"),
            scatter_dimension=0,
            tiled=True,
        )
        * grad_scale
    )
    d_conv = (d_gated * query_part).astype(jnp.bfloat16)
    d_query = d_gated * conv_rows.astype(jnp.float32)
    d_cols = lax.all_to_all(d_conv, "seq", split_axis=0, concat_axis=1, tiled=True)
    spec_d = forward_dft(d_cols, dft)
    da, db = halves(spec_d)
    d_mixed_cols = inverse_dft(cmul(ga, gb, da, db, True), dft).astype(jnp.bfloat16)
    d_mixed = lax.all_to_all(d_mixed_cols, "seq", split_axis=1, concat_axis=0, tiled=True)
    cross = cmul(sa, sb, da, db, True)
    filter_grad = inverse_dft(add_conj_flip(cross), dft)
    d_key = d_mixed.astype(jnp.float32) * value_part
    d_value = d_mixed.astype(jnp.float32) * key_part
    d_proj = jnp.stack([d_query, d_key, d_value]).astype(jnp.bfloat16)
    normed_local = lax.dynamic_slice_in_dim(normed, group_index * local_width, local_width, 0)
    cot_scaled = cotangent.T.astype(jnp.float32) * grad_scale
    d_full = lax.psum(
        jnp.einsum("dmc,mcr->dr", in_proj, d_proj, preferred_element_type=jnp.float32),
        ("chan", "pair"),
    )
    scaled_full = norm_gain[:, None] * d_full
    row_stat = jnp.mean(scaled_full * normed, axis=0, keepdims=True)
    scaled = lax.dynamic_slice_in_dim(scaled_full, group_index * local_width, local_width, 0)
    d_embedded = inv_rms * (scaled - normed_local * row_stat) + cot_scaled
    d_hidden = lax.dynamic_slice_in_dim(d_full, group_index * local_width, local_width, 0)
    gain_part = jnp.sum(d_hidden * normed_local, axis=1)
    table_part = jnp.einsum(
        "kr,cr->kc", onehot_t.astype(jnp.float32), d_embedded, precision=PRECISE
    )
    summed = lax.psum(jnp.concatenate([table_part, gain_part[None, :]], axis=0), "seq")
    kmer_grad = summed[: kmer_len * letter_count]
    gain_grad = summed[kmer_len * letter_count]
    return (
        block_out,
        filter_grad.reshape(long_filter.shape),
        kmer_grad.reshape(kmer_len, letter_count, local_width),
        gain_grad,
    )


def solution(mesh):
    in_specs = (
        P(("groups", "seq")),
        P(),
        P(),
        P(None, None, ("chan", "pair")),
        P(("chan", "pair"), "seq", None, None),
        P(None, ("chan", "pair")),
        P(("groups", "seq"), ("chan", "pair")),
    )
    out_specs = (
        P(("groups", "seq"), ("chan", "pair")),
        P(("groups", "chan", "pair"), "seq", None, None),
        P("groups", None, ("chan", "pair")),
        P(("groups", "chan", "pair")),
    )
    return jax.shard_map(
        per_device, mesh=mesh, in_specs=in_specs, out_specs=out_specs, check_vma=False
    )
```

```python
import math

import jax
import jax.numpy as jnp
from jax import lax
from jax.sharding import PartitionSpec as P

NORM_EPSILON = 1e-05
PRECISE = lax.Precision.HIGHEST
TRANSFORM_PRECISION = lax.Precision.HIGH


def from_behind(value, axis, steps):
    count = lax.axis_size(axis)
    first, last = (max(0, -steps), min(count, count - steps))
    return lax.ppermute(value, axis, [(source, source + steps) for source in range(first, last)])


def dft_matrix(length):
    total = 2 * length
    inner_len = 32 if length % 32 == 0 else 1
    outer_len = length // inner_len
    j = lax.broadcasted_iota(jnp.int32, (1, total), 1)
    k = jnp.where(j < length, j, j - length)
    k = jnp.where(j == length, length, k)
    phase = jnp.where(j > length, 3 * total // 4, 0)
    scale = 2.0 * math.pi / total

    def angle(idx):
        idx = idx % total
        idx = jnp.where(idx >= length, idx - total, idx)
        return idx.astype(jnp.float32) * scale

    outer = lax.optimization_barrier(lax.broadcasted_iota(jnp.int32, (outer_len, 1), 0))
    inner = lax.optimization_barrier(lax.broadcasted_iota(jnp.int32, (inner_len, 1), 0))
    alpha = angle(outer * inner_len * k)
    beta = angle(inner * k + phase)
    ca, sa = jnp.cos(alpha), jnp.sin(alpha)
    cb, sb = jnp.cos(beta), jnp.sin(beta)
    table = ca[:, None, :] * cb[None, :, :] - sa[:, None, :] * sb[None, :, :]
    return lax.optimization_barrier(table.reshape(length, total))


def xor_exchange(x, axis, step):
    count = lax.axis_size(axis)
    return lax.ppermute(x, axis, [(i, i ^ step) for i in range(count)])


def reduce_scatter_cp(x):
    chans, pairs = lax.axis_size("chan"), lax.axis_size("pair")
    rest = x.shape[1:]
    block = x.shape[0] // (chans * pairs)
    y = x.reshape((chans, pairs, block) + rest)
    me, step = lax.axis_index("pair"), pairs // 2
    while step >= 1:
        bit = (me // step) % 2
        split = y.reshape((chans, 2, step, block) + rest)
        y = jnp.take(split, bit, axis=1) + xor_exchange(jnp.take(split, 1 - bit, axis=1), "pair", step)
        step //= 2
    y = y.reshape((chans, block) + rest)
    me, step = lax.axis_index("chan"), chans // 2
    while step >= 1:
        bit = (me // step) % 2
        split = y.reshape((2, step, block) + rest)
        y = jnp.take(split, bit, axis=0) + xor_exchange(jnp.take(split, 1 - bit, axis=0), "chan", step)
        step //= 2
    return y.reshape((block,) + rest)


def ordered(mine, other, first, axis):
    return jnp.concatenate(
        [jnp.where(first, mine, other), jnp.where(first, other, mine)], axis=axis
    )


def all_gather_cp(x):
    chans, pairs = lax.axis_size("chan"), lax.axis_size("pair")
    y = x[None]
    me, step = lax.axis_index("chan"), 1
    while step < chans:
        y = ordered(y, xor_exchange(y, "chan", step), (me // step) % 2 == 0, 0)
        step *= 2
    y = y[:, None]
    me, step = lax.axis_index("pair"), 1
    while step < pairs:
        y = ordered(y, xor_exchange(y, "pair", step), (me // step) % 2 == 0, 1)
        step *= 2
    return y.reshape((chans * pairs * x.shape[0],) + x.shape[1:])


def psum_seq(x):
    count = lax.axis_size("seq")
    step = 1
    while step < count:
        x = x + xor_exchange(x, "seq", step)
        step *= 2
    return x


def forward_dft(signal, dft):
    return jnp.dot(signal.astype(jnp.float32), dft, precision=TRANSFORM_PRECISION)


def inverse_dft(spec, dft):
    length = dft.shape[0]
    total = 2 * length
    col = lax.broadcasted_iota(jnp.int32, (1, total), 1)
    weight = jnp.where(col % length == 0, 1.0 / total, 2.0 / total).astype(jnp.float32)
    return lax.dot_general(
        spec * weight, dft, (((1,), (1,)), ((), ())), precision=TRANSFORM_PRECISION
    )


def halves(spec):
    length = spec.shape[1] // 2
    return spec[:, :length], spec[:, length:]


def first_col(shape):
    return lax.broadcasted_iota(jnp.int32, shape, 1) == 0


def cmul(ga, gb, xa, xb, conj_g):
    edge = first_col(ga.shape)
    sign = -1.0 if conj_g else 1.0
    ya = ga * xa - sign * (gb * xb)
    yb = ga * xb + sign * (gb * xa)
    ya = jnp.where(edge, ga * xa, ya)
    yb = jnp.where(edge, gb * xb, yb)
    return jnp.concatenate([ya, yb], axis=1)


def pair_flip(values):
    rows = lax.broadcasted_iota(jnp.int32, values.shape, 0)
    up = jnp.roll(values, -1, axis=0)
    down = jnp.roll(values, 1, axis=0)
    return jnp.where(rows % 2 == 0, up, down)


def add_conj_flip(spec):
    a, b = halves(spec)
    fa, fb = halves(pair_flip(spec))
    edge = first_col(a.shape)
    return jnp.concatenate([a + fa, jnp.where(edge, b + fb, b - fb)], axis=1)


def norm_gain_local(norm_gain, group_index, local_width):
    return lax.dynamic_slice_in_dim(norm_gain, group_index * local_width, local_width, 0)


def per_device(tokens, kmer_table, norm_gain, in_proj, long_filter, out_proj, cotangent):
    row_count = tokens.shape[0]
    kmer_len, letter_count, model_width = kmer_table.shape
    local_width = in_proj.shape[2]
    length = row_count * lax.axis_size("seq")
    group_index = lax.axis_index(("chan", "pair"))
    rim_width = kmer_len - 1
    before = from_behind(tokens[row_count - rim_width :] + 1, "seq", 1) - 1
    extended = jnp.concatenate([before, tokens])
    letters = jnp.arange(letter_count, dtype=jnp.int32)
    columns = []
    for shift_back in range(kmer_len):
        window = extended[rim_width - shift_back : rim_width - shift_back + row_count]
        columns.append(window[:, None] == letters[None, :])
    onehot_t = jnp.concatenate(columns, axis=1).T.astype(jnp.bfloat16)
    table_t = kmer_table.reshape(kmer_len * letter_count, model_width).T
    embedded = jnp.dot(table_t, onehot_t, preferred_element_type=jnp.float32)
    inv_rms = lax.rsqrt(jnp.mean(embedded * embedded, axis=0, keepdims=True) + NORM_EPSILON)
    normed = embedded * inv_rms
    scaled_normed = normed * norm_gain[:, None]
    hidden = scaled_normed.astype(jnp.bfloat16)
    projected = jnp.einsum("dr,dmc->mcr", hidden, in_proj, preferred_element_type=jnp.float32)
    residual = (scaled_normed - hidden.astype(jnp.float32)).astype(jnp.bfloat16)
    unrounded = projected + jnp.einsum(
        "dr,dmc->mcr", residual, in_proj, preferred_element_type=jnp.float32
    )
    query_part = projected[0]
    key_part = projected[1]
    value_part = projected[2]
    mixed_in = (key_part * value_part).astype(jnp.bfloat16)
    dft = dft_matrix(length)
    filter_rows = long_filter.reshape(long_filter.shape[2], long_filter.shape[3])
    spec_g = add_conj_flip(forward_dft(filter_rows, dft))
    ga, gb = halves(spec_g)
    mixed_cols = lax.all_to_all(mixed_in, "seq", split_axis=0, concat_axis=1, tiled=True)
    spec_s = forward_dft(mixed_cols, dft)
    sa, sb = halves(spec_s)
    conv_cols = inverse_dft(cmul(ga, gb, sa, sb, False), dft).astype(jnp.bfloat16)
    conv_rows = lax.all_to_all(conv_cols, "seq", split_axis=1, concat_axis=0, tiled=True)
    gated_rows = (query_part * conv_rows.astype(jnp.float32)).astype(jnp.bfloat16)
    weight_rows = out_proj
    mixed_out = jnp.einsum(
        "cr,cd->rd",
        all_gather_cp(gated_rows),
        weight_rows,
        preferred_element_type=jnp.float32,
    )
    own_rows = lax.dynamic_slice_in_dim(embedded, group_index * local_width, local_width, 0)
    block_out = (mixed_out + own_rows.T).astype(jnp.bfloat16)
    grad_scale = 1.0 / math.sqrt(length)
    d_gated = (
        reduce_scatter_cp(
            jnp.einsum("cd,rd->cr", weight_rows, cotangent, preferred_element_type=jnp.float32)
        )
        * grad_scale
    )
    d_conv = (d_gated * query_part).astype(jnp.bfloat16)
    d_query = d_gated * conv_rows.astype(jnp.float32)
    d_cols = lax.all_to_all(d_conv, "seq", split_axis=0, concat_axis=1, tiled=True)
    spec_d = forward_dft(d_cols, dft)
    da, db = halves(spec_d)
    d_mixed_cols = inverse_dft(cmul(ga, gb, da, db, True), dft).astype(jnp.bfloat16)
    d_mixed = lax.all_to_all(d_mixed_cols, "seq", split_axis=1, concat_axis=0, tiled=True)
    cross = cmul(sa, sb, da, db, True)
    filter_grad = inverse_dft(add_conj_flip(cross), dft)
    d_key = d_mixed.astype(jnp.float32) * value_part
    d_value = d_mixed.astype(jnp.float32) * key_part
    d_proj = jnp.stack([d_query, d_key, d_value]).astype(jnp.bfloat16)
    normed_local = lax.dynamic_slice_in_dim(normed, group_index * local_width, local_width, 0)
    cot_scaled = cotangent.T.astype(jnp.float32) * grad_scale
    d_full = jnp.einsum("dmc,mcr->dr", in_proj, d_proj, preferred_element_type=jnp.float32)
    stat_part = jnp.sum(d_proj.astype(jnp.float32) * unrounded, axis=(0, 1))
    stat_rows = jnp.zeros((8, row_count), jnp.float32).at[0].set(stat_part)
    groups = lax.axis_size("chan") * lax.axis_size("pair")
    payload = jnp.concatenate(
        [
            d_full.reshape(groups, local_width, row_count),
            jnp.broadcast_to(stat_rows[None], (groups, 8, row_count)),
        ],
        axis=1,
    ).reshape(groups * (local_width + 8), row_count)
    reduced = reduce_scatter_cp(payload)
    d_hidden = reduced[:local_width]
    row_stat = reduced[local_width : local_width + 1] / model_width
    scaled = norm_gain_local(norm_gain, group_index, local_width)[:, None] * d_hidden
    d_embedded = inv_rms * (scaled - normed_local * row_stat) + cot_scaled
    gain_part = jnp.sum(d_hidden * normed_local, axis=1)
    table_part = jnp.einsum(
        "kr,cr->kc", onehot_t.astype(jnp.float32), d_embedded, precision=PRECISE
    )
    summed = psum_seq(jnp.concatenate([table_part, gain_part[None, :]], axis=0))
    kmer_grad = summed[: kmer_len * letter_count]
    gain_grad = summed[kmer_len * letter_count]
    return (
        block_out,
        filter_grad.reshape(long_filter.shape),
        kmer_grad.reshape(kmer_len, letter_count, local_width),
        gain_grad,
    )


def solution(mesh):
    in_specs = (
        P(("groups", "seq")),
        P(),
        P(),
        P(None, None, ("chan", "pair")),
        P(("chan", "pair"), "seq", None, None),
        P(None, ("chan", "pair")),
        P(("groups", "seq"), ("chan", "pair")),
    )
    out_specs = (
        P(("groups", "seq"), ("chan", "pair")),
        P(("groups", "chan", "pair"), "seq", None, None),
        P("groups", None, ("chan", "pair")),
        P(("groups", "chan", "pair")),
    )
    return jax.shard_map(
        per_device, mesh=mesh, in_specs=in_specs, out_specs=out_specs, check_vma=False
    )
```

```python
import math

import jax
import jax.numpy as jnp
from jax import lax
from jax.sharding import PartitionSpec as P

NORM_EPSILON = 1e-05
PRECISE = lax.Precision.HIGHEST
TRANSFORM_PRECISION = lax.Precision.HIGH


def from_behind(value, axis, steps):
    count = lax.axis_size(axis)
    first, last = (max(0, -steps), min(count, count - steps))
    return lax.ppermute(value, axis, [(source, source + steps) for source in range(first, last)])


def dft_matrix(length):
    total = 2 * length
    inner_len = 32 if length % 32 == 0 else 1
    outer_len = length // inner_len
    j = lax.broadcasted_iota(jnp.int32, (1, total), 1)
    k = jnp.where(j < length, j, j - length)
    k = jnp.where(j == length, length, k)
    phase = jnp.where(j > length, 3 * total // 4, 0)
    scale = 2.0 * math.pi / total

    def angle(idx):
        idx = idx % total
        idx = jnp.where(idx >= length, idx - total, idx)
        return idx.astype(jnp.float32) * scale

    outer = lax.optimization_barrier(lax.broadcasted_iota(jnp.int32, (outer_len, 1), 0))
    inner = lax.optimization_barrier(lax.broadcasted_iota(jnp.int32, (inner_len, 1), 0))
    alpha = angle(outer * inner_len * k)
    beta = angle(inner * k + phase)
    ca, sa = jnp.cos(alpha), jnp.sin(alpha)
    cb, sb = jnp.cos(beta), jnp.sin(beta)
    table = ca[:, None, :] * cb[None, :, :] - sa[:, None, :] * sb[None, :, :]
    return lax.optimization_barrier(table.reshape(length, total))


def xor_exchange(x, axis, step):
    count = lax.axis_size(axis)
    return lax.ppermute(x, axis, [(i, i ^ step) for i in range(count)])


def reduce_scatter_lanes(x, width):
    for axis, inner in (("pair", lax.axis_size("chan")), ("chan", 1)):
        me, step = lax.axis_index(axis), lax.axis_size(axis) // 2
        while step >= 1:
            half = step * inner * width
            low = (me // step) % 2 == 0
            lo, hi = x[:, :half], x[:, half : 2 * half]
            keep = jnp.where(low, lo, hi)
            send = jnp.where(low, hi, lo)
            x = keep + xor_exchange(send, axis, step)
            step //= 2
    return x


def pair_major(blocks):
    chans, pairs = lax.axis_size("chan"), lax.axis_size("pair")
    return [blocks[c * pairs + p] for p in range(pairs) for c in range(chans)]


def ordered(mine, other, first, axis):
    return jnp.concatenate(
        [jnp.where(first, mine, other), jnp.where(first, other, mine)], axis=axis
    )


def all_gather_cp(x):
    chans, pairs = lax.axis_size("chan"), lax.axis_size("pair")
    y = x[None]
    me, step = lax.axis_index("chan"), 1
    while step < chans:
        y = ordered(y, xor_exchange(y, "chan", step), (me // step) % 2 == 0, 0)
        step *= 2
    y = y[:, None]
    me, step = lax.axis_index("pair"), 1
    while step < pairs:
        y = ordered(y, xor_exchange(y, "pair", step), (me // step) % 2 == 0, 1)
        step *= 2
    return y.reshape((chans * pairs * x.shape[0],) + x.shape[1:])


def psum_seq(x):
    count = lax.axis_size("seq")
    step = 1
    while step < count:
        x = x + xor_exchange(x, "seq", step)
        step *= 2
    return x


def forward_dft(signal, dft):
    return jnp.dot(signal.astype(jnp.float32), dft, precision=TRANSFORM_PRECISION)


def inverse_dft(spec, dft):
    length = dft.shape[0]
    total = 2 * length
    col = lax.broadcasted_iota(jnp.int32, (1, total), 1)
    weight = jnp.where(col % length == 0, 1.0 / total, 2.0 / total).astype(jnp.float32)
    return lax.dot_general(
        spec * weight, dft, (((1,), (1,)), ((), ())), precision=TRANSFORM_PRECISION
    )


def halves(spec):
    length = spec.shape[1] // 2
    return spec[:, :length], spec[:, length:]


def first_col(shape):
    return lax.broadcasted_iota(jnp.int32, shape, 1) == 0


def cmul(ga, gb, xa, xb, conj_g):
    edge = first_col(ga.shape)
    sign = -1.0 if conj_g else 1.0
    ya = ga * xa - sign * (gb * xb)
    yb = ga * xb + sign * (gb * xa)
    ya = jnp.where(edge, ga * xa, ya)
    yb = jnp.where(edge, gb * xb, yb)
    return jnp.concatenate([ya, yb], axis=1)


def pair_flip(values):
    rows = lax.broadcasted_iota(jnp.int32, values.shape, 0)
    up = jnp.roll(values, -1, axis=0)
    down = jnp.roll(values, 1, axis=0)
    return jnp.where(rows % 2 == 0, up, down)


def add_conj_flip(spec):
    a, b = halves(spec)
    fa, fb = halves(pair_flip(spec))
    edge = first_col(a.shape)
    return jnp.concatenate([a + fa, jnp.where(edge, b + fb, b - fb)], axis=1)


def norm_gain_local(norm_gain, group_index, local_width):
    return lax.dynamic_slice_in_dim(norm_gain, group_index * local_width, local_width, 0)


def per_device(tokens, kmer_table, norm_gain, in_proj, long_filter, out_proj, cotangent):
    row_count = tokens.shape[0]
    kmer_len, letter_count, model_width = kmer_table.shape
    local_width = in_proj.shape[2]
    length = row_count * lax.axis_size("seq")
    group_index = lax.axis_index(("chan", "pair"))
    rim_width = kmer_len - 1
    before = from_behind(tokens[row_count - rim_width :] + 1, "seq", 1) - 1
    extended = jnp.concatenate([before, tokens])
    letters = jnp.arange(letter_count, dtype=jnp.int32)
    columns = []
    for shift_back in range(kmer_len):
        window = extended[rim_width - shift_back : rim_width - shift_back + row_count]
        columns.append(window[:, None] == letters[None, :])
    onehot_t = jnp.concatenate(columns, axis=1).T.astype(jnp.bfloat16)
    table_t = kmer_table.reshape(kmer_len * letter_count, model_width).T
    embedded = jnp.dot(table_t, onehot_t, preferred_element_type=jnp.float32)
    inv_rms = lax.rsqrt(jnp.mean(embedded * embedded, axis=0, keepdims=True) + NORM_EPSILON)
    normed = embedded * inv_rms
    scaled_normed = normed * norm_gain[:, None]
    hidden = scaled_normed.astype(jnp.bfloat16)
    projected = jnp.einsum("dr,dmc->mcr", hidden, in_proj, preferred_element_type=jnp.float32)
    residual = (scaled_normed - hidden.astype(jnp.float32)).astype(jnp.bfloat16)
    unrounded = projected + jnp.einsum(
        "dr,dmc->mcr", residual, in_proj, preferred_element_type=jnp.float32
    )
    query_part = projected[0]
    key_part = projected[1]
    value_part = projected[2]
    mixed_in = (key_part * value_part).astype(jnp.bfloat16)
    grad_scale = 1.0 / math.sqrt(length)
    groups = lax.axis_size("chan") * lax.axis_size("pair")
    gated_partial = jnp.einsum("rd,cd->rc", cotangent, out_proj, preferred_element_type=jnp.float32)
    gated_blocks = [gated_partial[:, g * local_width : (g + 1) * local_width] for g in range(groups)]
    d_gated = (
        reduce_scatter_lanes(jnp.concatenate(pair_major(gated_blocks), axis=1), local_width).T
        * grad_scale
    )
    dft = dft_matrix(length)
    filter_rows = long_filter.reshape(long_filter.shape[2], long_filter.shape[3])
    spec_g = add_conj_flip(forward_dft(filter_rows, dft))
    ga, gb = halves(spec_g)
    d_conv = (d_gated * query_part).astype(jnp.bfloat16)
    both_cols = lax.all_to_all(
        jnp.stack([mixed_in, d_conv]), "seq", split_axis=1, concat_axis=2, tiled=True
    )
    mixed_cols, d_cols = both_cols[0], both_cols[1]
    spec_s = forward_dft(mixed_cols, dft)
    sa, sb = halves(spec_s)
    conv_cols = inverse_dft(cmul(ga, gb, sa, sb, False), dft).astype(jnp.bfloat16)
    spec_d = forward_dft(d_cols, dft)
    da, db = halves(spec_d)
    d_mixed_cols = inverse_dft(cmul(ga, gb, da, db, True), dft).astype(jnp.bfloat16)
    both_rows = lax.all_to_all(
        jnp.stack([conv_cols, d_mixed_cols]), "seq", split_axis=2, concat_axis=1, tiled=True
    )
    conv_rows, d_mixed = both_rows[0], both_rows[1]
    gated_rows = (query_part * conv_rows.astype(jnp.float32)).astype(jnp.bfloat16)
    weight_rows = out_proj
    mixed_out = jnp.einsum(
        "cr,cd->rd",
        all_gather_cp(gated_rows),
        weight_rows,
        preferred_element_type=jnp.float32,
    )
    own_rows = lax.dynamic_slice_in_dim(embedded, group_index * local_width, local_width, 0)
    block_out = (mixed_out + own_rows.T).astype(jnp.bfloat16)
    d_query = d_gated * conv_rows.astype(jnp.float32)
    cross = cmul(sa, sb, da, db, True)
    filter_grad = inverse_dft(add_conj_flip(cross), dft)
    d_key = d_mixed.astype(jnp.float32) * value_part
    d_value = d_mixed.astype(jnp.float32) * key_part
    d_proj = jnp.stack([d_query, d_key, d_value]).astype(jnp.bfloat16)
    normed_local = lax.dynamic_slice_in_dim(normed, group_index * local_width, local_width, 0)
    d_full = jnp.einsum("mcr,dmc->rd", d_proj, in_proj, preferred_element_type=jnp.float32)
    stat_part = jnp.sum(d_proj.astype(jnp.float32) * unrounded, axis=(0, 1))
    stat_block = jnp.broadcast_to(stat_part[:, None], (row_count, 128))
    hidden_blocks = [
        jnp.concatenate([d_full[:, g * local_width : (g + 1) * local_width], stat_block], axis=1)
        for g in range(groups)
    ]
    reduced = reduce_scatter_lanes(
        jnp.concatenate(pair_major(hidden_blocks), axis=1), local_width + 128
    )
    d_hidden = reduced[:, :local_width]
    row_stat = reduced[:, local_width : local_width + 1] / model_width
    gain_local = norm_gain_local(norm_gain, group_index, local_width)
    normed_rows = normed_local.T
    d_embedded = inv_rms.T * (gain_local[None, :] * d_hidden - normed_rows * row_stat) + (
        cotangent.astype(jnp.float32) * grad_scale
    )
    gain_part = jnp.sum(d_hidden * normed_rows, axis=0)
    table_part = jnp.einsum(
        "kr,rc->kc", onehot_t.astype(jnp.float32), d_embedded, precision=PRECISE
    )
    summed = psum_seq(jnp.concatenate([table_part, gain_part[None, :]], axis=0))
    kmer_grad = summed[: kmer_len * letter_count]
    gain_grad = summed[kmer_len * letter_count]
    return (
        block_out,
        filter_grad.reshape(long_filter.shape),
        kmer_grad.reshape(kmer_len, letter_count, local_width),
        gain_grad,
    )


def solution(mesh):
    in_specs = (
        P(("groups", "seq")),
        P(),
        P(),
        P(None, None, ("chan", "pair")),
        P(("chan", "pair"), "seq", None, None),
        P(None, ("chan", "pair")),
        P(("groups", "seq"), ("chan", "pair")),
    )
    out_specs = (
        P(("groups", "seq"), ("chan", "pair")),
        P(("groups", "chan", "pair"), "seq", None, None),
        P("groups", None, ("chan", "pair")),
        P(("groups", "chan", "pair")),
    )
    return jax.shard_map(
        per_device, mesh=mesh, in_specs=in_specs, out_specs=out_specs, check_vma=False
    )
```

```python
import math

import jax
import jax.numpy as jnp
from jax import lax
from jax.sharding import PartitionSpec as P

NORM_EPSILON = 1e-05
PRECISE = lax.Precision.HIGHEST
TRANSFORM_PRECISION = lax.Precision.HIGH


def from_behind(value, axis, steps):
    count = lax.axis_size(axis)
    first, last = (max(0, -steps), min(count, count - steps))
    return lax.ppermute(value, axis, [(source, source + steps) for source in range(first, last)])


def dft_matrix(length):
    total = 2 * length
    inner_len = 32 if length % 32 == 0 else 1
    outer_len = length // inner_len
    j = lax.broadcasted_iota(jnp.int32, (1, total), 1)
    k = jnp.where(j < length, j, j - length)
    k = jnp.where(j == length, length, k)
    phase = jnp.where(j > length, 3 * total // 4, 0)
    scale = 2.0 * math.pi / total

    def angle(idx):
        idx = idx % total
        idx = jnp.where(idx >= length, idx - total, idx)
        return idx.astype(jnp.float32) * scale

    outer = lax.optimization_barrier(lax.broadcasted_iota(jnp.int32, (outer_len, 1), 0))
    inner = lax.optimization_barrier(lax.broadcasted_iota(jnp.int32, (inner_len, 1), 0))
    alpha = angle(outer * inner_len * k)
    beta = angle(inner * k + phase)
    ca, sa = jnp.cos(alpha), jnp.sin(alpha)
    cb, sb = jnp.cos(beta), jnp.sin(beta)
    table = ca[:, None, :] * cb[None, :, :] - sa[:, None, :] * sb[None, :, :]
    return lax.optimization_barrier(table.reshape(length, total))


def xor_exchange(x, axis, step):
    count = lax.axis_size(axis)
    return lax.ppermute(x, axis, [(i, i ^ step) for i in range(count)])


def reduce_scatter_lanes(x, width):
    for axis, inner in (("pair", lax.axis_size("chan")), ("chan", 1)):
        me, step = lax.axis_index(axis), lax.axis_size(axis) // 2
        while step >= 1:
            half = step * inner * width
            low = (me // step) % 2 == 0
            lo, hi = x[:, :half], x[:, half : 2 * half]
            keep = jnp.where(low, lo, hi)
            send = jnp.where(low, hi, lo)
            x = keep + xor_exchange(send, axis, step)
            step //= 2
    return x


def pair_major(blocks):
    chans, pairs = lax.axis_size("chan"), lax.axis_size("pair")
    return [blocks[c * pairs + p] for p in range(pairs) for c in range(chans)]


def ordered(mine, other, first, axis):
    return jnp.concatenate(
        [jnp.where(first, mine, other), jnp.where(first, other, mine)], axis=axis
    )


def all_gather_cp(x):
    chans, pairs = lax.axis_size("chan"), lax.axis_size("pair")
    y = x[None]
    me, step = lax.axis_index("chan"), 1
    while step < chans:
        y = ordered(y, xor_exchange(y, "chan", step), (me // step) % 2 == 0, 0)
        step *= 2
    y = y[:, None]
    me, step = lax.axis_index("pair"), 1
    while step < pairs:
        y = ordered(y, xor_exchange(y, "pair", step), (me // step) % 2 == 0, 1)
        step *= 2
    return y.reshape((chans * pairs * x.shape[0],) + x.shape[1:])


def group_exchange(x, axes, count, offset):
    return lax.ppermute(x, axes, [(i, i ^ offset) for i in range(count)])


def reduce_blocks_cp(x, width):
    axes = ("chan", "pair")
    count = lax.axis_size("chan") * lax.axis_size("pair")
    me = lax.axis_index(axes)
    blocks = [x[:, g * width : (g + 1) * width] for g in range(count)]

    def pick(index):
        out = blocks[0]
        for g in range(1, count):
            out = jnp.where(index == g, blocks[g], out)
        return out

    total = pick(me)
    for offset in range(1, count):
        total = total + group_exchange(pick(me ^ offset), axes, count, offset)
    return total


def sum_over_seq(x):
    count = lax.axis_size("seq")
    me = lax.axis_index("seq")
    if count > 4:
        step = 1
        while step < count:
            x = x + xor_exchange(x, "seq", step)
            step *= 2
        return x
    got = [x] + [group_exchange(x, "seq", count, offset) for offset in range(1, count)]
    total = None
    for source in range(count):
        piece = got[0]
        for offset in range(1, count):
            piece = jnp.where((me ^ source) == offset, got[offset], piece)
        total = piece if total is None else total + piece
    return total


def forward_dft(signal, dft):
    return jnp.dot(signal.astype(jnp.float32), dft, precision=TRANSFORM_PRECISION)


def inverse_dft(spec, dft):
    length = dft.shape[0]
    total = 2 * length
    col = lax.broadcasted_iota(jnp.int32, (1, total), 1)
    weight = jnp.where(col % length == 0, 1.0 / total, 2.0 / total).astype(jnp.float32)
    return lax.dot_general(
        spec * weight, dft, (((1,), (1,)), ((), ())), precision=TRANSFORM_PRECISION
    )


def halves(spec):
    length = spec.shape[1] // 2
    return spec[:, :length], spec[:, length:]


def first_col(shape):
    return lax.broadcasted_iota(jnp.int32, shape, 1) == 0


def cmul(ga, gb, xa, xb, conj_g):
    edge = first_col(ga.shape)
    sign = -1.0 if conj_g else 1.0
    ya = ga * xa - sign * (gb * xb)
    yb = ga * xb + sign * (gb * xa)
    ya = jnp.where(edge, ga * xa, ya)
    yb = jnp.where(edge, gb * xb, yb)
    return jnp.concatenate([ya, yb], axis=1)


def pair_flip(values):
    rows = lax.broadcasted_iota(jnp.int32, values.shape, 0)
    up = jnp.roll(values, -1, axis=0)
    down = jnp.roll(values, 1, axis=0)
    return jnp.where(rows % 2 == 0, up, down)


def add_conj_flip(spec):
    a, b = halves(spec)
    fa, fb = halves(pair_flip(spec))
    edge = first_col(a.shape)
    return jnp.concatenate([a + fa, jnp.where(edge, b + fb, b - fb)], axis=1)


def norm_gain_local(norm_gain, group_index, local_width):
    return lax.dynamic_slice_in_dim(norm_gain, group_index * local_width, local_width, 0)


def per_device(tokens, kmer_table, norm_gain, in_proj, long_filter, out_proj, cotangent):
    row_count = tokens.shape[0]
    kmer_len, letter_count, model_width = kmer_table.shape
    local_width = in_proj.shape[2]
    length = row_count * lax.axis_size("seq")
    group_index = lax.axis_index(("chan", "pair"))
    rim_width = kmer_len - 1
    before = from_behind(tokens[row_count - rim_width :] + 1, "seq", 1) - 1
    extended = jnp.concatenate([before, tokens])
    letters = jnp.arange(letter_count, dtype=jnp.int32)
    columns = []
    for shift_back in range(kmer_len):
        window = extended[rim_width - shift_back : rim_width - shift_back + row_count]
        columns.append(window[:, None] == letters[None, :])
    onehot_t = jnp.concatenate(columns, axis=1).T.astype(jnp.bfloat16)
    table_t = kmer_table.reshape(kmer_len * letter_count, model_width).T
    embedded = jnp.dot(table_t, onehot_t, preferred_element_type=jnp.float32)
    inv_rms = lax.rsqrt(jnp.mean(embedded * embedded, axis=0, keepdims=True) + NORM_EPSILON)
    normed = embedded * inv_rms
    scaled_normed = normed * norm_gain[:, None]
    hidden = scaled_normed.astype(jnp.bfloat16)
    projected = jnp.einsum("dr,dmc->mcr", hidden, in_proj, preferred_element_type=jnp.float32)
    residual = (scaled_normed - hidden.astype(jnp.float32)).astype(jnp.bfloat16)
    unrounded = projected + jnp.einsum(
        "dr,dmc->mcr", residual, in_proj, preferred_element_type=jnp.float32
    )
    query_part = projected[0]
    key_part = projected[1]
    value_part = projected[2]
    mixed_in = (key_part * value_part).astype(jnp.bfloat16)
    grad_scale = 1.0 / math.sqrt(length)
    groups = lax.axis_size("chan") * lax.axis_size("pair")
    gated_partial = jnp.einsum("rd,cd->rc", cotangent, out_proj, preferred_element_type=jnp.float32)
    gated_blocks = [gated_partial[:, g * local_width : (g + 1) * local_width] for g in range(groups)]
    d_gated = (
        reduce_scatter_lanes(jnp.concatenate(pair_major(gated_blocks), axis=1), local_width).T
        * grad_scale
    )
    dft = dft_matrix(length)
    filter_rows = long_filter.reshape(long_filter.shape[2], long_filter.shape[3])
    spec_g = add_conj_flip(forward_dft(filter_rows, dft))
    ga, gb = halves(spec_g)
    d_conv = (d_gated * query_part).astype(jnp.bfloat16)
    both_cols = lax.all_to_all(
        jnp.stack([mixed_in, d_conv]), "seq", split_axis=1, concat_axis=2, tiled=True
    )
    mixed_cols, d_cols = both_cols[0], both_cols[1]
    spec_s = forward_dft(mixed_cols, dft)
    sa, sb = halves(spec_s)
    conv_cols = inverse_dft(cmul(ga, gb, sa, sb, False), dft).astype(jnp.bfloat16)
    spec_d = forward_dft(d_cols, dft)
    da, db = halves(spec_d)
    d_mixed_cols = inverse_dft(cmul(ga, gb, da, db, True), dft).astype(jnp.bfloat16)
    both_rows = lax.all_to_all(
        jnp.stack([conv_cols, d_mixed_cols]), "seq", split_axis=2, concat_axis=1, tiled=True
    )
    conv_rows, d_mixed = both_rows[0], both_rows[1]
    gated_rows = (query_part * conv_rows.astype(jnp.float32)).astype(jnp.bfloat16)
    weight_rows = out_proj
    mixed_out = jnp.einsum(
        "cr,cd->rd",
        all_gather_cp(gated_rows),
        weight_rows,
        preferred_element_type=jnp.float32,
    )
    own_rows = lax.dynamic_slice_in_dim(embedded, group_index * local_width, local_width, 0)
    block_out = (mixed_out + own_rows.T).astype(jnp.bfloat16)
    d_query = d_gated * conv_rows.astype(jnp.float32)
    cross = cmul(sa, sb, da, db, True)
    filter_grad = inverse_dft(add_conj_flip(cross), dft)
    d_key = d_mixed.astype(jnp.float32) * value_part
    d_value = d_mixed.astype(jnp.float32) * key_part
    d_proj = jnp.stack([d_query, d_key, d_value]).astype(jnp.bfloat16)
    d_full = jnp.einsum("mcr,dmc->rd", d_proj, in_proj, preferred_element_type=jnp.float32)
    stat_part = jnp.sum(d_proj.astype(jnp.float32) * unrounded, axis=(0, 1))
    onehot_rows = onehot_t.T.astype(jnp.float32)
    weights = onehot_rows * inv_rms.T
    direct = jnp.einsum("rk,rd->kd", weights, d_full, precision=PRECISE)
    centred = jnp.einsum("rk,dr->kd", weights * stat_part[:, None], normed, precision=PRECISE)
    table_all = norm_gain[None, :] * direct - centred / model_width
    gain_all = jnp.einsum("rd,dr->d", d_full, normed, precision=PRECISE)
    partial = jnp.concatenate([table_all, gain_all[None, :]], axis=0)
    own_block = reduce_blocks_cp(partial, local_width)
    cot_table = jnp.einsum(
        "rk,rc->kc", onehot_rows, cotangent.astype(jnp.float32) * grad_scale, precision=PRECISE
    )
    own_block = own_block + jnp.concatenate(
        [cot_table, jnp.zeros((1, local_width), jnp.float32)], axis=0
    )
    summed = sum_over_seq(own_block)
    kmer_grad = summed[: kmer_len * letter_count]
    gain_grad = summed[kmer_len * letter_count]
    return (
        block_out,
        filter_grad.reshape(long_filter.shape),
        kmer_grad.reshape(kmer_len, letter_count, local_width),
        gain_grad,
    )


def solution(mesh):
    in_specs = (
        P(("groups", "seq")),
        P(),
        P(),
        P(None, None, ("chan", "pair")),
        P(("chan", "pair"), "seq", None, None),
        P(None, ("chan", "pair")),
        P(("groups", "seq"), ("chan", "pair")),
    )
    out_specs = (
        P(("groups", "seq"), ("chan", "pair")),
        P(("groups", "chan", "pair"), "seq", None, None),
        P("groups", None, ("chan", "pair")),
        P(("groups", "chan", "pair")),
    )
    return jax.shard_map(
        per_device, mesh=mesh, in_specs=in_specs, out_specs=out_specs, check_vma=False
    )
```

```python
import math

import jax
import jax.numpy as jnp
from jax import lax
from jax.sharding import PartitionSpec as P

NORM_EPSILON = 1e-05
PRECISE = lax.Precision.HIGHEST
TRANSFORM_PRECISION = lax.Precision.HIGH


def from_behind(value, axis, steps):
    count = lax.axis_size(axis)
    first, last = (max(0, -steps), min(count, count - steps))
    return lax.ppermute(value, axis, [(source, source + steps) for source in range(first, last)])


def dft_matrix(length):
    total = 2 * length
    inner_len = 32 if length % 32 == 0 else 1
    outer_len = length // inner_len
    j = lax.broadcasted_iota(jnp.int32, (1, total), 1)
    k = jnp.where(j < length, j, j - length)
    k = jnp.where(j == length, length, k)
    phase = jnp.where(j > length, 3 * total // 4, 0)
    scale = 2.0 * math.pi / total

    def angle(idx):
        idx = idx % total
        idx = jnp.where(idx >= length, idx - total, idx)
        return idx.astype(jnp.float32) * scale

    outer = lax.optimization_barrier(lax.broadcasted_iota(jnp.int32, (outer_len, 1), 0))
    inner = lax.optimization_barrier(lax.broadcasted_iota(jnp.int32, (inner_len, 1), 0))
    alpha = angle(outer * inner_len * k)
    beta = angle(inner * k + phase)
    ca, sa = jnp.cos(alpha), jnp.sin(alpha)
    cb, sb = jnp.cos(beta), jnp.sin(beta)
    table = ca[:, None, :] * cb[None, :, :] - sa[:, None, :] * sb[None, :, :]
    return lax.optimization_barrier(table.reshape(length, total))


def xor_exchange(x, axis, step):
    count = lax.axis_size(axis)
    return lax.ppermute(x, axis, [(i, i ^ step) for i in range(count)])


def reduce_scatter_lanes(x, width):
    for axis, inner in (("pair", lax.axis_size("chan")), ("chan", 1)):
        me, step = lax.axis_index(axis), lax.axis_size(axis) // 2
        while step >= 1:
            half = step * inner * width
            low = (me // step) % 2 == 0
            lo, hi = x[:, :half], x[:, half : 2 * half]
            keep = jnp.where(low, lo, hi)
            send = jnp.where(low, hi, lo)
            x = keep + xor_exchange(send, axis, step)
            step //= 2
    return x


def pair_major(blocks):
    chans, pairs = lax.axis_size("chan"), lax.axis_size("pair")
    return [blocks[c * pairs + p] for p in range(pairs) for c in range(chans)]


def ordered(mine, other, first, axis):
    return jnp.concatenate(
        [jnp.where(first, mine, other), jnp.where(first, other, mine)], axis=axis
    )


def all_gather_cp(x):
    chans, pairs = lax.axis_size("chan"), lax.axis_size("pair")
    y = x[None]
    me, step = lax.axis_index("chan"), 1
    while step < chans:
        y = ordered(y, xor_exchange(y, "chan", step), (me // step) % 2 == 0, 0)
        step *= 2
    y = y[:, None]
    me, step = lax.axis_index("pair"), 1
    while step < pairs:
        y = ordered(y, xor_exchange(y, "pair", step), (me // step) % 2 == 0, 1)
        step *= 2
    return y.reshape((chans * pairs * x.shape[0],) + x.shape[1:])


def group_exchange(x, axes, count, offset):
    return lax.ppermute(x, axes, [(i, i ^ offset) for i in range(count)])


def reduce_blocks_cp(x, width):
    axes = ("chan", "pair")
    count = lax.axis_size("chan") * lax.axis_size("pair")
    me = lax.axis_index(axes)
    blocks = [x[:, g * width : (g + 1) * width] for g in range(count)]

    def pick(index):
        out = blocks[0]
        for g in range(1, count):
            out = jnp.where(index == g, blocks[g], out)
        return out

    total = pick(me)
    for offset in range(1, count):
        total = total + group_exchange(pick(me ^ offset), axes, count, offset)
    return total


def sum_over_seq(x):
    count = lax.axis_size("seq")
    me = lax.axis_index("seq")
    if count > 4:
        step = 1
        while step < count:
            x = x + xor_exchange(x, "seq", step)
            step *= 2
        return x
    got = [x] + [group_exchange(x, "seq", count, offset) for offset in range(1, count)]
    total = None
    for source in range(count):
        piece = got[0]
        for offset in range(1, count):
            piece = jnp.where((me ^ source) == offset, got[offset], piece)
        total = piece if total is None else total + piece
    return total


def all_to_all_seq(x, split_axis, concat_axis):
    count = lax.axis_size("seq")
    if count > 4:
        return lax.all_to_all(x, "seq", split_axis=split_axis, concat_axis=concat_axis, tiled=True)
    me = lax.axis_index("seq")
    width = x.shape[split_axis] // count
    blocks = [lax.slice_in_dim(x, j * width, (j + 1) * width, axis=split_axis) for j in range(count)]

    def pick(index):
        out = blocks[0]
        for j in range(1, count):
            out = jnp.where(index == j, blocks[j], out)
        return out

    got = [pick(me)] + [
        group_exchange(pick(me ^ offset), "seq", count, offset) for offset in range(1, count)
    ]
    pieces = []
    for source in range(count):
        piece = got[0]
        for offset in range(1, count):
            piece = jnp.where((me ^ source) == offset, got[offset], piece)
        pieces.append(piece)
    return jnp.concatenate(pieces, axis=concat_axis)


def forward_dft(signal, dft):
    return jnp.dot(signal.astype(jnp.float32), dft, precision=TRANSFORM_PRECISION)


def inverse_dft(spec, dft):
    length = dft.shape[0]
    total = 2 * length
    col = lax.broadcasted_iota(jnp.int32, (1, total), 1)
    weight = jnp.where(col % length == 0, 1.0 / total, 2.0 / total).astype(jnp.float32)
    return lax.dot_general(
        spec * weight, dft, (((1,), (1,)), ((), ())), precision=TRANSFORM_PRECISION
    )


def halves(spec):
    length = spec.shape[1] // 2
    return spec[:, :length], spec[:, length:]


def first_col(shape):
    return lax.broadcasted_iota(jnp.int32, shape, 1) == 0


def cmul(ga, gb, xa, xb, conj_g):
    edge = first_col(ga.shape)
    sign = -1.0 if conj_g else 1.0
    ya = ga * xa - sign * (gb * xb)
    yb = ga * xb + sign * (gb * xa)
    ya = jnp.where(edge, ga * xa, ya)
    yb = jnp.where(edge, gb * xb, yb)
    return jnp.concatenate([ya, yb], axis=1)


def pair_flip(values):
    rows = lax.broadcasted_iota(jnp.int32, values.shape, 0)
    up = jnp.roll(values, -1, axis=0)
    down = jnp.roll(values, 1, axis=0)
    return jnp.where(rows % 2 == 0, up, down)


def add_conj_flip(spec):
    a, b = halves(spec)
    fa, fb = halves(pair_flip(spec))
    edge = first_col(a.shape)
    return jnp.concatenate([a + fa, jnp.where(edge, b + fb, b - fb)], axis=1)


def norm_gain_local(norm_gain, group_index, local_width):
    return lax.dynamic_slice_in_dim(norm_gain, group_index * local_width, local_width, 0)


def per_device(tokens, kmer_table, norm_gain, in_proj, long_filter, out_proj, cotangent):
    row_count = tokens.shape[0]
    kmer_len, letter_count, model_width = kmer_table.shape
    local_width = in_proj.shape[2]
    length = row_count * lax.axis_size("seq")
    group_index = lax.axis_index(("chan", "pair"))
    rim_width = kmer_len - 1
    before = from_behind(tokens[row_count - rim_width :] + 1, "seq", 1) - 1
    extended = jnp.concatenate([before, tokens])
    letters = jnp.arange(letter_count, dtype=jnp.int32)
    columns = []
    for shift_back in range(kmer_len):
        window = extended[rim_width - shift_back : rim_width - shift_back + row_count]
        columns.append(window[:, None] == letters[None, :])
    onehot_t = jnp.concatenate(columns, axis=1).T.astype(jnp.bfloat16)
    table_t = kmer_table.reshape(kmer_len * letter_count, model_width).T
    embedded = jnp.dot(table_t, onehot_t, preferred_element_type=jnp.float32)
    inv_rms = lax.rsqrt(jnp.mean(embedded * embedded, axis=0, keepdims=True) + NORM_EPSILON)
    normed = embedded * inv_rms
    scaled_normed = normed * norm_gain[:, None]
    hidden = scaled_normed.astype(jnp.bfloat16)
    projected = jnp.einsum("dr,dmc->mcr", hidden, in_proj, preferred_element_type=jnp.float32)
    residual = (scaled_normed - hidden.astype(jnp.float32)).astype(jnp.bfloat16)
    unrounded = projected + jnp.einsum(
        "dr,dmc->mcr", residual, in_proj, preferred_element_type=jnp.float32
    )
    query_part = projected[0]
    key_part = projected[1]
    value_part = projected[2]
    mixed_in = (key_part * value_part).astype(jnp.bfloat16)
    grad_scale = 1.0 / math.sqrt(length)
    groups = lax.axis_size("chan") * lax.axis_size("pair")
    gated_partial = jnp.einsum("rd,cd->rc", cotangent, out_proj, preferred_element_type=jnp.float32)
    gated_blocks = [gated_partial[:, g * local_width : (g + 1) * local_width] for g in range(groups)]
    d_gated = (
        reduce_scatter_lanes(jnp.concatenate(pair_major(gated_blocks), axis=1), local_width).T
        * grad_scale
    )
    dft = dft_matrix(length)
    filter_rows = long_filter.reshape(long_filter.shape[2], long_filter.shape[3])
    spec_g = add_conj_flip(forward_dft(filter_rows, dft))
    ga, gb = halves(spec_g)
    d_conv = (d_gated * query_part).astype(jnp.bfloat16)
    both_cols = all_to_all_seq(jnp.stack([mixed_in, d_conv]), 1, 2)
    mixed_cols, d_cols = both_cols[0], both_cols[1]
    spec_s = forward_dft(mixed_cols, dft)
    sa, sb = halves(spec_s)
    conv_cols = inverse_dft(cmul(ga, gb, sa, sb, False), dft).astype(jnp.bfloat16)
    spec_d = forward_dft(d_cols, dft)
    da, db = halves(spec_d)
    d_mixed_cols = inverse_dft(cmul(ga, gb, da, db, True), dft).astype(jnp.bfloat16)
    both_rows = all_to_all_seq(jnp.stack([conv_cols, d_mixed_cols]), 2, 1)
    conv_rows, d_mixed = both_rows[0], both_rows[1]
    gated_rows = (query_part * conv_rows.astype(jnp.float32)).astype(jnp.bfloat16)
    weight_rows = out_proj
    mixed_out = jnp.einsum(
        "cr,cd->rd",
        all_gather_cp(gated_rows),
        weight_rows,
        preferred_element_type=jnp.float32,
    )
    own_rows = lax.dynamic_slice_in_dim(embedded, group_index * local_width, local_width, 0)
    block_out = (mixed_out + own_rows.T).astype(jnp.bfloat16)
    d_query = d_gated * conv_rows.astype(jnp.float32)
    cross = cmul(sa, sb, da, db, True)
    filter_grad = inverse_dft(add_conj_flip(cross), dft)
    d_key = d_mixed.astype(jnp.float32) * value_part
    d_value = d_mixed.astype(jnp.float32) * key_part
    d_proj = jnp.stack([d_query, d_key, d_value]).astype(jnp.bfloat16)
    d_full = jnp.einsum("mcr,dmc->rd", d_proj, in_proj, preferred_element_type=jnp.float32)
    stat_part = jnp.sum(d_proj.astype(jnp.float32) * unrounded, axis=(0, 1))
    onehot_rows = onehot_t.T.astype(jnp.float32)
    weights = onehot_rows * inv_rms.T
    direct = jnp.einsum("rk,rd->kd", weights, d_full, precision=PRECISE)
    centred = jnp.einsum("rk,dr->kd", weights * stat_part[:, None], normed, precision=PRECISE)
    table_all = norm_gain[None, :] * direct - centred / model_width
    gain_all = jnp.einsum("rd,dr->d", d_full, normed, precision=PRECISE)
    partial = jnp.concatenate([table_all, gain_all[None, :]], axis=0)
    own_block = reduce_blocks_cp(partial, local_width)
    cot_table = jnp.einsum(
        "rk,rc->kc", onehot_rows, cotangent.astype(jnp.float32) * grad_scale, precision=PRECISE
    )
    own_block = own_block + jnp.concatenate(
        [cot_table, jnp.zeros((1, local_width), jnp.float32)], axis=0
    )
    summed = sum_over_seq(own_block)
    kmer_grad = summed[: kmer_len * letter_count]
    gain_grad = summed[kmer_len * letter_count]
    return (
        block_out,
        filter_grad.reshape(long_filter.shape),
        kmer_grad.reshape(kmer_len, letter_count, local_width),
        gain_grad,
    )


def solution(mesh):
    in_specs = (
        P(("groups", "seq")),
        P(),
        P(),
        P(None, None, ("chan", "pair")),
        P(("chan", "pair"), "seq", None, None),
        P(None, ("chan", "pair")),
        P(("groups", "seq"), ("chan", "pair")),
    )
    out_specs = (
        P(("groups", "seq"), ("chan", "pair")),
        P(("groups", "chan", "pair"), "seq", None, None),
        P("groups", None, ("chan", "pair")),
        P(("groups", "chan", "pair")),
    )
    return jax.shard_map(
        per_device, mesh=mesh, in_specs=in_specs, out_specs=out_specs, check_vma=False
    )
```

```python
import math

import jax
import jax.numpy as jnp
from jax import lax
from jax.sharding import PartitionSpec as P

NORM_EPSILON = 1e-05
PRECISE = lax.Precision.HIGHEST
TRANSFORM_PRECISION = lax.Precision.HIGH


def from_behind(value, axis, steps):
    count = lax.axis_size(axis)
    first, last = (max(0, -steps), min(count, count - steps))
    return lax.ppermute(value, axis, [(source, source + steps) for source in range(first, last)])


def dft_matrix(length):
    total = 2 * length
    inner_len = 32 if length % 32 == 0 else 1
    outer_len = length // inner_len
    j = lax.broadcasted_iota(jnp.int32, (1, total), 1)
    k = jnp.where(j < length, j, j - length)
    k = jnp.where(j == length, length, k)
    phase = jnp.where(j > length, 3 * total // 4, 0)
    scale = 2.0 * math.pi / total

    def angle(idx):
        idx = idx % total
        idx = jnp.where(idx >= length, idx - total, idx)
        return idx.astype(jnp.float32) * scale

    outer = lax.optimization_barrier(lax.broadcasted_iota(jnp.int32, (outer_len, 1), 0))
    inner = lax.optimization_barrier(lax.broadcasted_iota(jnp.int32, (inner_len, 1), 0))
    alpha = angle(outer * inner_len * k)
    beta = angle(inner * k + phase)
    ca, sa = jnp.cos(alpha), jnp.sin(alpha)
    cb, sb = jnp.cos(beta), jnp.sin(beta)
    table = ca[:, None, :] * cb[None, :, :] - sa[:, None, :] * sb[None, :, :]
    return lax.optimization_barrier(table.reshape(length, total))


def xor_exchange(x, axis, step):
    count = lax.axis_size(axis)
    return lax.ppermute(x, axis, [(i, i ^ step) for i in range(count)])


def reduce_scatter_lanes(x, width):
    for axis, inner in (("pair", lax.axis_size("chan")), ("chan", 1)):
        me, step = lax.axis_index(axis), lax.axis_size(axis) // 2
        while step >= 1:
            half = step * inner * width
            low = (me // step) % 2 == 0
            lo, hi = x[:, :half], x[:, half : 2 * half]
            keep = jnp.where(low, lo, hi)
            send = jnp.where(low, hi, lo)
            x = keep + xor_exchange(send, axis, step)
            step //= 2
    return x


def pair_major(blocks):
    chans, pairs = lax.axis_size("chan"), lax.axis_size("pair")
    return [blocks[c * pairs + p] for p in range(pairs) for c in range(chans)]


def ordered(mine, other, first, axis):
    return jnp.concatenate(
        [jnp.where(first, mine, other), jnp.where(first, other, mine)], axis=axis
    )


def all_gather_cp(x):
    chans, pairs = lax.axis_size("chan"), lax.axis_size("pair")
    y = x[None]
    me, step = lax.axis_index("chan"), 1
    while step < chans:
        y = ordered(y, xor_exchange(y, "chan", step), (me // step) % 2 == 0, 0)
        step *= 2
    y = y[:, None]
    me, step = lax.axis_index("pair"), 1
    while step < pairs:
        y = ordered(y, xor_exchange(y, "pair", step), (me // step) % 2 == 0, 1)
        step *= 2
    return y.reshape((chans * pairs * x.shape[0],) + x.shape[1:])


def group_exchange(x, axes, count, offset):
    return lax.ppermute(x, axes, [(i, i ^ offset) for i in range(count)])


def reduce_blocks_cp(x, width, shared):
    axes = ("chan", "pair")
    count = lax.axis_size("chan") * lax.axis_size("pair")
    me = lax.axis_index(axes)
    rows = x.shape[0]
    blocks = [x[:, g * width : (g + 1) * width] for g in range(count)]

    def pick(index):
        out = blocks[0]
        for g in range(1, count):
            out = jnp.where(index == g, blocks[g], out)
        return out

    extra = shared.astype(jnp.float32)
    total = pick(me)
    pieces = [(me, shared)]
    for offset in range(1, count):
        got = group_exchange(
            jnp.concatenate([pick(me ^ offset), extra], axis=0), axes, count, offset
        )
        total = total + got[:rows]
        pieces.append((me ^ offset, got[rows:].astype(shared.dtype)))
    return total, pieces


def sum_over_seq(x):
    count = lax.axis_size("seq")
    me = lax.axis_index("seq")
    if count > 4:
        step = 1
        while step < count:
            x = x + xor_exchange(x, "seq", step)
            step *= 2
        return x
    got = [x] + [group_exchange(x, "seq", count, offset) for offset in range(1, count)]
    total = None
    for source in range(count):
        piece = got[0]
        for offset in range(1, count):
            piece = jnp.where((me ^ source) == offset, got[offset], piece)
        total = piece if total is None else total + piece
    return total


def all_to_all_seq(x, split_axis, concat_axis):
    count = lax.axis_size("seq")
    if count > 4:
        return lax.all_to_all(x, "seq", split_axis=split_axis, concat_axis=concat_axis, tiled=True)
    me = lax.axis_index("seq")
    width = x.shape[split_axis] // count
    blocks = [lax.slice_in_dim(x, j * width, (j + 1) * width, axis=split_axis) for j in range(count)]

    def pick(index):
        out = blocks[0]
        for j in range(1, count):
            out = jnp.where(index == j, blocks[j], out)
        return out

    got = [pick(me)] + [
        group_exchange(pick(me ^ offset), "seq", count, offset) for offset in range(1, count)
    ]
    pieces = []
    for source in range(count):
        piece = got[0]
        for offset in range(1, count):
            piece = jnp.where((me ^ source) == offset, got[offset], piece)
        pieces.append(piece)
    return jnp.concatenate(pieces, axis=concat_axis)


def forward_dft(signal, dft):
    return jnp.dot(signal.astype(jnp.float32), dft, precision=TRANSFORM_PRECISION)


def inverse_dft(spec, dft):
    length = dft.shape[0]
    total = 2 * length
    col = lax.broadcasted_iota(jnp.int32, (1, total), 1)
    weight = jnp.where(col % length == 0, 1.0 / total, 2.0 / total).astype(jnp.float32)
    return lax.dot_general(
        spec * weight, dft, (((1,), (1,)), ((), ())), precision=TRANSFORM_PRECISION
    )


def halves(spec):
    length = spec.shape[1] // 2
    return spec[:, :length], spec[:, length:]


def first_col(shape):
    return lax.broadcasted_iota(jnp.int32, shape, 1) == 0


def cmul(ga, gb, xa, xb, conj_g):
    edge = first_col(ga.shape)
    sign = -1.0 if conj_g else 1.0
    ya = ga * xa - sign * (gb * xb)
    yb = ga * xb + sign * (gb * xa)
    ya = jnp.where(edge, ga * xa, ya)
    yb = jnp.where(edge, gb * xb, yb)
    return jnp.concatenate([ya, yb], axis=1)


def pair_flip(values):
    rows = lax.broadcasted_iota(jnp.int32, values.shape, 0)
    up = jnp.roll(values, -1, axis=0)
    down = jnp.roll(values, 1, axis=0)
    return jnp.where(rows % 2 == 0, up, down)


def add_conj_flip(spec):
    a, b = halves(spec)
    fa, fb = halves(pair_flip(spec))
    edge = first_col(a.shape)
    return jnp.concatenate([a + fa, jnp.where(edge, b + fb, b - fb)], axis=1)


def norm_gain_local(norm_gain, group_index, local_width):
    return lax.dynamic_slice_in_dim(norm_gain, group_index * local_width, local_width, 0)


def per_device(tokens, kmer_table, norm_gain, in_proj, long_filter, out_proj, cotangent):
    row_count = tokens.shape[0]
    kmer_len, letter_count, model_width = kmer_table.shape
    local_width = in_proj.shape[2]
    length = row_count * lax.axis_size("seq")
    group_index = lax.axis_index(("chan", "pair"))
    rim_width = kmer_len - 1
    before = from_behind(tokens[row_count - rim_width :] + 1, "seq", 1) - 1
    extended = jnp.concatenate([before, tokens])
    letters = jnp.arange(letter_count, dtype=jnp.int32)
    columns = []
    for shift_back in range(kmer_len):
        window = extended[rim_width - shift_back : rim_width - shift_back + row_count]
        columns.append(window[:, None] == letters[None, :])
    onehot_t = jnp.concatenate(columns, axis=1).T.astype(jnp.bfloat16)
    table_t = kmer_table.reshape(kmer_len * letter_count, model_width).T
    embedded = jnp.dot(table_t, onehot_t, preferred_element_type=jnp.float32)
    inv_rms = lax.rsqrt(jnp.mean(embedded * embedded, axis=0, keepdims=True) + NORM_EPSILON)
    normed = embedded * inv_rms
    scaled_normed = normed * norm_gain[:, None]
    hidden = scaled_normed.astype(jnp.bfloat16)
    projected = jnp.einsum("dr,dmc->mcr", hidden, in_proj, preferred_element_type=jnp.float32)
    residual = (scaled_normed - hidden.astype(jnp.float32)).astype(jnp.bfloat16)
    unrounded = projected + jnp.einsum(
        "dr,dmc->mcr", residual, in_proj, preferred_element_type=jnp.float32
    )
    query_part = projected[0]
    key_part = projected[1]
    value_part = projected[2]
    mixed_in = (key_part * value_part).astype(jnp.bfloat16)
    grad_scale = 1.0 / math.sqrt(length)
    groups = lax.axis_size("chan") * lax.axis_size("pair")
    gated_partial = jnp.einsum("rd,cd->rc", cotangent, out_proj, preferred_element_type=jnp.float32)
    gated_blocks = [gated_partial[:, g * local_width : (g + 1) * local_width] for g in range(groups)]
    d_gated = (
        reduce_scatter_lanes(jnp.concatenate(pair_major(gated_blocks), axis=1), local_width).T
        * grad_scale
    )
    dft = dft_matrix(length)
    filter_rows = long_filter.reshape(long_filter.shape[2], long_filter.shape[3])
    spec_g = add_conj_flip(forward_dft(filter_rows, dft))
    ga, gb = halves(spec_g)
    d_conv = (d_gated * query_part).astype(jnp.bfloat16)
    both_cols = all_to_all_seq(jnp.stack([mixed_in, d_conv]), 1, 2)
    mixed_cols, d_cols = both_cols[0], both_cols[1]
    spec_s = forward_dft(mixed_cols, dft)
    sa, sb = halves(spec_s)
    conv_cols = inverse_dft(cmul(ga, gb, sa, sb, False), dft).astype(jnp.bfloat16)
    spec_d = forward_dft(d_cols, dft)
    da, db = halves(spec_d)
    d_mixed_cols = inverse_dft(cmul(ga, gb, da, db, True), dft).astype(jnp.bfloat16)
    both_rows = all_to_all_seq(jnp.stack([conv_cols, d_mixed_cols]), 2, 1)
    conv_rows, d_mixed = both_rows[0], both_rows[1]
    gated_rows = (query_part * conv_rows.astype(jnp.float32)).astype(jnp.bfloat16)
    d_query = d_gated * conv_rows.astype(jnp.float32)
    cross = cmul(sa, sb, da, db, True)
    filter_grad = inverse_dft(add_conj_flip(cross), dft)
    d_key = d_mixed.astype(jnp.float32) * value_part
    d_value = d_mixed.astype(jnp.float32) * key_part
    d_proj = jnp.stack([d_query, d_key, d_value]).astype(jnp.bfloat16)
    d_full = jnp.einsum("mcr,dmc->rd", d_proj, in_proj, preferred_element_type=jnp.float32)
    stat_part = jnp.sum(d_proj.astype(jnp.float32) * unrounded, axis=(0, 1))
    onehot_rows = onehot_t.T.astype(jnp.float32)
    weights = onehot_rows * inv_rms.T
    direct = jnp.einsum("rk,rd->kd", weights, d_full, precision=PRECISE)
    centred = jnp.einsum("rk,dr->kd", weights * stat_part[:, None], normed, precision=PRECISE)
    table_all = norm_gain[None, :] * direct - centred / model_width
    gain_all = jnp.einsum("rd,dr->d", d_full, normed, precision=PRECISE)
    partial = jnp.concatenate([table_all, gain_all[None, :]], axis=0)
    own_block, gated_pieces = reduce_blocks_cp(partial, local_width, gated_rows.T)
    mixed_out = None
    for source, piece in gated_pieces:
        rows = lax.dynamic_slice_in_dim(out_proj, source * local_width, local_width, 0)
        term = jnp.dot(piece, rows, preferred_element_type=jnp.float32)
        mixed_out = term if mixed_out is None else mixed_out + term
    own_rows = lax.dynamic_slice_in_dim(embedded, group_index * local_width, local_width, 0)
    block_out = (mixed_out + own_rows.T).astype(jnp.bfloat16)
    cot_table = jnp.einsum(
        "rk,rc->kc", onehot_rows, cotangent.astype(jnp.float32) * grad_scale, precision=PRECISE
    )
    own_block = own_block + jnp.concatenate(
        [cot_table, jnp.zeros((1, local_width), jnp.float32)], axis=0
    )
    summed = sum_over_seq(own_block)
    kmer_grad = summed[: kmer_len * letter_count]
    gain_grad = summed[kmer_len * letter_count]
    return (
        block_out,
        filter_grad.reshape(long_filter.shape),
        kmer_grad.reshape(kmer_len, letter_count, local_width),
        gain_grad,
    )


def solution(mesh):
    in_specs = (
        P(("groups", "seq")),
        P(),
        P(),
        P(None, None, ("chan", "pair")),
        P(("chan", "pair"), "seq", None, None),
        P(None, ("chan", "pair")),
        P(("groups", "seq"), ("chan", "pair")),
    )
    out_specs = (
        P(("groups", "seq"), ("chan", "pair")),
        P(("groups", "chan", "pair"), "seq", None, None),
        P("groups", None, ("chan", "pair")),
        P(("groups", "chan", "pair")),
    )
    return jax.shard_map(
        per_device, mesh=mesh, in_specs=in_specs, out_specs=out_specs, check_vma=False
    )
```

```python
import math

import jax
import jax.numpy as jnp
from jax import lax
from jax.sharding import PartitionSpec as P

NORM_EPSILON = 1e-05
PRECISE = lax.Precision.HIGHEST
TRANSFORM_PRECISION = lax.Precision.HIGH


def from_behind(value, axis, steps):
    count = lax.axis_size(axis)
    first, last = (max(0, -steps), min(count, count - steps))
    return lax.ppermute(value, axis, [(source, source + steps) for source in range(first, last)])


def dft_matrix(length):
    total = 2 * length
    inner_len = 32 if length % 32 == 0 else 1
    outer_len = length // inner_len
    j = lax.broadcasted_iota(jnp.int32, (1, total), 1)
    k = jnp.where(j < length, j, j - length)
    k = jnp.where(j == length, length, k)
    phase = jnp.where(j > length, 3 * total // 4, 0)
    scale = 2.0 * math.pi / total

    def angle(idx):
        idx = idx % total
        idx = jnp.where(idx >= length, idx - total, idx)
        return idx.astype(jnp.float32) * scale

    outer = lax.optimization_barrier(lax.broadcasted_iota(jnp.int32, (outer_len, 1), 0))
    inner = lax.optimization_barrier(lax.broadcasted_iota(jnp.int32, (inner_len, 1), 0))
    alpha = angle(outer * inner_len * k)
    beta = angle(inner * k + phase)
    ca, sa = jnp.cos(alpha), jnp.sin(alpha)
    cb, sb = jnp.cos(beta), jnp.sin(beta)
    table = ca[:, None, :] * cb[None, :, :] - sa[:, None, :] * sb[None, :, :]
    return lax.optimization_barrier(table.reshape(length, total))


def xor_exchange(x, axis, step):
    count = lax.axis_size(axis)
    return lax.ppermute(x, axis, [(i, i ^ step) for i in range(count)])


def reduce_scatter_lanes(x, width):
    for axis, inner in (("pair", lax.axis_size("chan")), ("chan", 1)):
        me, step = lax.axis_index(axis), lax.axis_size(axis) // 2
        while step >= 1:
            half = step * inner * width
            low = (me // step) % 2 == 0
            lo, hi = x[:, :half], x[:, half : 2 * half]
            keep = jnp.where(low, lo, hi)
            send = jnp.where(low, hi, lo)
            x = keep + xor_exchange(send, axis, step)
            step //= 2
    return x


def pair_major(blocks):
    chans, pairs = lax.axis_size("chan"), lax.axis_size("pair")
    return [blocks[c * pairs + p] for p in range(pairs) for c in range(chans)]


def all_gather_cp(x):
    chans, pairs = lax.axis_size("chan"), lax.axis_size("pair")
    y = x[None]
    sources = [lax.axis_index(("chan", "pair"))]
    for axis, size, stride in (("chan", chans, pairs), ("pair", pairs, 1)):
        step = 1
        while step < size:
            y = jnp.concatenate([y, xor_exchange(y, axis, step)], axis=0)
            sources = sources + [source ^ (step * stride) for source in sources]
            step *= 2
    return y, sources


def group_exchange(x, axes, count, offset):
    return lax.ppermute(x, axes, [(i, i ^ offset) for i in range(count)])


def reduce_blocks_cp(x, width):
    axes = ("chan", "pair")
    count = lax.axis_size("chan") * lax.axis_size("pair")
    me = lax.axis_index(axes)
    blocks = [x[:, g * width : (g + 1) * width] for g in range(count)]

    def pick(index):
        out = blocks[0]
        for g in range(1, count):
            out = jnp.where(index == g, blocks[g], out)
        return out

    total = pick(me)
    for offset in range(1, count):
        total = total + group_exchange(pick(me ^ offset), axes, count, offset)
    return total


def sum_over_seq(x):
    count = lax.axis_size("seq")
    me = lax.axis_index("seq")
    if count > 4:
        step = 1
        while step < count:
            x = x + xor_exchange(x, "seq", step)
            step *= 2
        return x
    got = [x] + [group_exchange(x, "seq", count, offset) for offset in range(1, count)]
    total = None
    for source in range(count):
        piece = got[0]
        for offset in range(1, count):
            piece = jnp.where((me ^ source) == offset, got[offset], piece)
        total = piece if total is None else total + piece
    return total


def all_to_all_seq(x, split_axis, concat_axis):
    count = lax.axis_size("seq")
    if count > 4:
        return lax.all_to_all(x, "seq", split_axis=split_axis, concat_axis=concat_axis, tiled=True)
    me = lax.axis_index("seq")
    width = x.shape[split_axis] // count
    blocks = [lax.slice_in_dim(x, j * width, (j + 1) * width, axis=split_axis) for j in range(count)]

    def pick(index):
        out = blocks[0]
        for j in range(1, count):
            out = jnp.where(index == j, blocks[j], out)
        return out

    got = [pick(me)] + [
        group_exchange(pick(me ^ offset), "seq", count, offset) for offset in range(1, count)
    ]
    pieces = []
    for source in range(count):
        piece = got[0]
        for offset in range(1, count):
            piece = jnp.where((me ^ source) == offset, got[offset], piece)
        pieces.append(piece)
    return jnp.concatenate(pieces, axis=concat_axis)


def forward_dft(signal, dft):
    return jnp.dot(signal.astype(jnp.float32), dft, precision=TRANSFORM_PRECISION)


def inverse_dft(spec, dft):
    length = dft.shape[0]
    total = 2 * length
    col = lax.broadcasted_iota(jnp.int32, (1, total), 1)
    weight = jnp.where(col % length == 0, 1.0 / total, 2.0 / total).astype(jnp.float32)
    return lax.dot_general(
        spec * weight, dft, (((1,), (1,)), ((), ())), precision=TRANSFORM_PRECISION
    )


def halves(spec):
    length = spec.shape[1] // 2
    return spec[:, :length], spec[:, length:]


def first_col(shape):
    return lax.broadcasted_iota(jnp.int32, shape, 1) == 0


def cmul(ga, gb, xa, xb, conj_g):
    edge = first_col(ga.shape)
    sign = -1.0 if conj_g else 1.0
    ya = ga * xa - sign * (gb * xb)
    yb = ga * xb + sign * (gb * xa)
    ya = jnp.where(edge, ga * xa, ya)
    yb = jnp.where(edge, gb * xb, yb)
    return jnp.concatenate([ya, yb], axis=1)


def pair_flip(values):
    rows = lax.broadcasted_iota(jnp.int32, values.shape, 0)
    up = jnp.roll(values, -1, axis=0)
    down = jnp.roll(values, 1, axis=0)
    return jnp.where(rows % 2 == 0, up, down)


def add_conj_flip(spec):
    a, b = halves(spec)
    fa, fb = halves(pair_flip(spec))
    edge = first_col(a.shape)
    return jnp.concatenate([a + fa, jnp.where(edge, b + fb, b - fb)], axis=1)


def norm_gain_local(norm_gain, group_index, local_width):
    return lax.dynamic_slice_in_dim(norm_gain, group_index * local_width, local_width, 0)


def per_device(tokens, kmer_table, norm_gain, in_proj, long_filter, out_proj, cotangent):
    row_count = tokens.shape[0]
    kmer_len, letter_count, model_width = kmer_table.shape
    local_width = in_proj.shape[2]
    length = row_count * lax.axis_size("seq")
    group_index = lax.axis_index(("chan", "pair"))
    rim_width = kmer_len - 1
    before = from_behind(tokens[row_count - rim_width :] + 1, "seq", 1) - 1
    extended = jnp.concatenate([before, tokens])
    letters = jnp.arange(letter_count, dtype=jnp.int32)
    columns = []
    for shift_back in range(kmer_len):
        window = extended[rim_width - shift_back : rim_width - shift_back + row_count]
        columns.append(window[:, None] == letters[None, :])
    onehot_t = jnp.concatenate(columns, axis=1).T.astype(jnp.bfloat16)
    table_t = kmer_table.reshape(kmer_len * letter_count, model_width).T
    embedded = jnp.dot(table_t, onehot_t, preferred_element_type=jnp.float32)
    inv_rms = lax.rsqrt(jnp.mean(embedded * embedded, axis=0, keepdims=True) + NORM_EPSILON)
    normed = embedded * inv_rms
    scaled_normed = normed * norm_gain[:, None]
    hidden = scaled_normed.astype(jnp.bfloat16)
    projected = jnp.einsum("dr,dmc->mcr", hidden, in_proj, preferred_element_type=jnp.float32)
    residual = (scaled_normed - hidden.astype(jnp.float32)).astype(jnp.bfloat16)
    unrounded = projected + jnp.einsum(
        "dr,dmc->mcr", residual, in_proj, preferred_element_type=jnp.float32
    )
    query_part = projected[0]
    key_part = projected[1]
    value_part = projected[2]
    mixed_in = (key_part * value_part).astype(jnp.bfloat16)
    grad_scale = 1.0 / math.sqrt(length)
    groups = lax.axis_size("chan") * lax.axis_size("pair")
    gated_partial = jnp.einsum("rd,cd->rc", cotangent, out_proj, preferred_element_type=jnp.float32)
    gated_blocks = [gated_partial[:, g * local_width : (g + 1) * local_width] for g in range(groups)]
    d_gated = (
        reduce_scatter_lanes(jnp.concatenate(pair_major(gated_blocks), axis=1), local_width).T
        * grad_scale
    )
    dft = dft_matrix(length)
    filter_rows = long_filter.reshape(long_filter.shape[2], long_filter.shape[3])
    spec_g = add_conj_flip(forward_dft(filter_rows, dft))
    ga, gb = halves(spec_g)
    d_conv = (d_gated * query_part).astype(jnp.bfloat16)
    both_cols = all_to_all_seq(jnp.stack([mixed_in, d_conv]), 1, 2)
    mixed_cols, d_cols = both_cols[0], both_cols[1]
    spec_s = forward_dft(mixed_cols, dft)
    sa, sb = halves(spec_s)
    conv_cols = inverse_dft(cmul(ga, gb, sa, sb, False), dft).astype(jnp.bfloat16)
    spec_d = forward_dft(d_cols, dft)
    da, db = halves(spec_d)
    d_mixed_cols = inverse_dft(cmul(ga, gb, da, db, True), dft).astype(jnp.bfloat16)
    both_rows = all_to_all_seq(jnp.stack([conv_cols, d_mixed_cols]), 2, 1)
    conv_rows, d_mixed = both_rows[0], both_rows[1]
    gated_rows = (query_part * conv_rows.astype(jnp.float32)).astype(jnp.bfloat16)
    weight_rows = out_proj
    gathered, sources = all_gather_cp(gated_rows)
    weight_order = jnp.concatenate(
        [lax.dynamic_slice_in_dim(weight_rows, src * local_width, local_width, 0) for src in sources],
        axis=0,
    )
    mixed_out = jnp.einsum(
        "cr,cd->rd",
        gathered.reshape(-1, gathered.shape[-1]),
        weight_order,
        preferred_element_type=jnp.float32,
    )
    own_rows = lax.dynamic_slice_in_dim(embedded, group_index * local_width, local_width, 0)
    block_out = (mixed_out + own_rows.T).astype(jnp.bfloat16)
    d_query = d_gated * conv_rows.astype(jnp.float32)
    cross = cmul(sa, sb, da, db, True)
    filter_grad = inverse_dft(add_conj_flip(cross), dft)
    d_key = d_mixed.astype(jnp.float32) * value_part
    d_value = d_mixed.astype(jnp.float32) * key_part
    d_proj = jnp.stack([d_query, d_key, d_value]).astype(jnp.bfloat16)
    d_full = jnp.einsum("mcr,dmc->rd", d_proj, in_proj, preferred_element_type=jnp.float32)
    stat_part = jnp.sum(d_proj.astype(jnp.float32) * unrounded, axis=(0, 1))
    onehot_rows = onehot_t.T.astype(jnp.float32)
    weights = onehot_rows * inv_rms.T
    direct = jnp.einsum("rk,rd->kd", weights, d_full, precision=PRECISE)
    centred = jnp.einsum("rk,dr->kd", weights * stat_part[:, None], normed, precision=PRECISE)
    table_all = norm_gain[None, :] * direct - centred / model_width
    gain_all = jnp.einsum("rd,dr->d", d_full, normed, precision=PRECISE)
    partial = jnp.concatenate([table_all, gain_all[None, :]], axis=0)
    own_block = reduce_blocks_cp(partial, local_width)
    cot_table = jnp.einsum(
        "rk,rc->kc", onehot_rows, cotangent.astype(jnp.float32) * grad_scale, precision=PRECISE
    )
    own_block = own_block + jnp.concatenate(
        [cot_table, jnp.zeros((1, local_width), jnp.float32)], axis=0
    )
    summed = sum_over_seq(own_block)
    kmer_grad = summed[: kmer_len * letter_count]
    gain_grad = summed[kmer_len * letter_count]
    return (
        block_out,
        filter_grad.reshape(long_filter.shape),
        kmer_grad.reshape(kmer_len, letter_count, local_width),
        gain_grad,
    )


def solution(mesh):
    in_specs = (
        P(("groups", "seq")),
        P(),
        P(),
        P(None, None, ("chan", "pair")),
        P(("chan", "pair"), "seq", None, None),
        P(None, ("chan", "pair")),
        P(("groups", "seq"), ("chan", "pair")),
    )
    out_specs = (
        P(("groups", "seq"), ("chan", "pair")),
        P(("groups", "chan", "pair"), "seq", None, None),
        P("groups", None, ("chan", "pair")),
        P(("groups", "chan", "pair")),
    )
    return jax.shard_map(
        per_device, mesh=mesh, in_specs=in_specs, out_specs=out_specs, check_vma=False
    )
```

```python
import math

import jax
import jax.numpy as jnp
from jax import lax
from jax.sharding import PartitionSpec as P

NORM_EPSILON = 1e-05
PRECISE = lax.Precision.HIGHEST
TRANSFORM_PRECISION = lax.Precision.HIGH


def from_behind(value, axis, steps):
    count = lax.axis_size(axis)
    first, last = (max(0, -steps), min(count, count - steps))
    return lax.ppermute(value, axis, [(source, source + steps) for source in range(first, last)])


def dft_matrix(length):
    total = 2 * length
    inner_len = 32 if length % 32 == 0 else 1
    outer_len = length // inner_len
    j = lax.broadcasted_iota(jnp.int32, (1, total), 1)
    k = jnp.where(j < length, j, j - length)
    k = jnp.where(j == length, length, k)
    phase = jnp.where(j > length, 3 * total // 4, 0)
    scale = 2.0 * math.pi / total

    def angle(idx):
        idx = idx % total
        idx = jnp.where(idx >= length, idx - total, idx)
        return idx.astype(jnp.float32) * scale

    outer = lax.optimization_barrier(lax.broadcasted_iota(jnp.int32, (outer_len, 1), 0))
    inner = lax.optimization_barrier(lax.broadcasted_iota(jnp.int32, (inner_len, 1), 0))
    alpha = angle(outer * inner_len * k)
    beta = angle(inner * k + phase)
    ca, sa = jnp.cos(alpha), jnp.sin(alpha)
    cb, sb = jnp.cos(beta), jnp.sin(beta)
    table = ca[:, None, :] * cb[None, :, :] - sa[:, None, :] * sb[None, :, :]
    return lax.optimization_barrier(table.reshape(length, total))


def xor_exchange(x, axis, step):
    count = lax.axis_size(axis)
    return lax.ppermute(x, axis, [(i, i ^ step) for i in range(count)])


def all_gather_cp(x):
    chans, pairs = lax.axis_size("chan"), lax.axis_size("pair")
    y = x[None]
    sources = [lax.axis_index(("chan", "pair"))]
    for axis, size, stride in (("chan", chans, pairs), ("pair", pairs, 1)):
        step = 1
        while step < size:
            y = jnp.concatenate([y, xor_exchange(y, axis, step)], axis=0)
            sources = sources + [source ^ (step * stride) for source in sources]
            step *= 2
    return y, sources


def group_exchange(x, axes, count, offset):
    return lax.ppermute(x, axes, [(i, i ^ offset) for i in range(count)])


def reduce_blocks_cp(x, width):
    axes = ("chan", "pair")
    count = lax.axis_size("chan") * lax.axis_size("pair")
    me = lax.axis_index(axes)
    blocks = [x[:, g * width : (g + 1) * width] for g in range(count)]

    def pick(index):
        out = blocks[0]
        for g in range(1, count):
            out = jnp.where(index == g, blocks[g], out)
        return out

    total = pick(me)
    for offset in range(1, count):
        total = total + group_exchange(pick(me ^ offset), axes, count, offset)
    return total


def sum_over_seq(x):
    count = lax.axis_size("seq")
    me = lax.axis_index("seq")
    if count > 4:
        step = 1
        while step < count:
            x = x + xor_exchange(x, "seq", step)
            step *= 2
        return x
    got = [x] + [group_exchange(x, "seq", count, offset) for offset in range(1, count)]
    total = None
    for source in range(count):
        piece = got[0]
        for offset in range(1, count):
            piece = jnp.where((me ^ source) == offset, got[offset], piece)
        total = piece if total is None else total + piece
    return total


def all_to_all_seq(x, split_axis, concat_axis):
    count = lax.axis_size("seq")
    if count > 4:
        return lax.all_to_all(x, "seq", split_axis=split_axis, concat_axis=concat_axis, tiled=True)
    me = lax.axis_index("seq")
    width = x.shape[split_axis] // count
    blocks = [lax.slice_in_dim(x, j * width, (j + 1) * width, axis=split_axis) for j in range(count)]

    def pick(index):
        out = blocks[0]
        for j in range(1, count):
            out = jnp.where(index == j, blocks[j], out)
        return out

    got = [pick(me)] + [
        group_exchange(pick(me ^ offset), "seq", count, offset) for offset in range(1, count)
    ]
    pieces = []
    for source in range(count):
        piece = got[0]
        for offset in range(1, count):
            piece = jnp.where((me ^ source) == offset, got[offset], piece)
        pieces.append(piece)
    return jnp.concatenate(pieces, axis=concat_axis)


def forward_dft(signal, dft):
    return jnp.dot(signal.astype(jnp.float32), dft, precision=TRANSFORM_PRECISION)


def inverse_dft(spec, dft):
    length = dft.shape[0]
    total = 2 * length
    col = lax.broadcasted_iota(jnp.int32, (1, total), 1)
    weight = jnp.where(col % length == 0, 1.0 / total, 2.0 / total).astype(jnp.float32)
    return lax.dot_general(
        spec * weight, dft, (((1,), (1,)), ((), ())), precision=TRANSFORM_PRECISION
    )


def halves(spec):
    length = spec.shape[1] // 2
    return spec[:, :length], spec[:, length:]


def first_col(shape):
    return lax.broadcasted_iota(jnp.int32, shape, 1) == 0


def cmul(ga, gb, xa, xb, conj_g):
    edge = first_col(ga.shape)
    sign = -1.0 if conj_g else 1.0
    ya = ga * xa - sign * (gb * xb)
    yb = ga * xb + sign * (gb * xa)
    ya = jnp.where(edge, ga * xa, ya)
    yb = jnp.where(edge, gb * xb, yb)
    return jnp.concatenate([ya, yb], axis=1)


def pair_flip(values):
    rows = lax.broadcasted_iota(jnp.int32, values.shape, 0)
    up = jnp.roll(values, -1, axis=0)
    down = jnp.roll(values, 1, axis=0)
    return jnp.where(rows % 2 == 0, up, down)


def add_conj_flip(spec):
    a, b = halves(spec)
    fa, fb = halves(pair_flip(spec))
    edge = first_col(a.shape)
    return jnp.concatenate([a + fa, jnp.where(edge, b + fb, b - fb)], axis=1)


def norm_gain_local(norm_gain, group_index, local_width):
    return lax.dynamic_slice_in_dim(norm_gain, group_index * local_width, local_width, 0)


def per_device(tokens, kmer_table, norm_gain, in_proj, long_filter, out_proj, cotangent):
    row_count = tokens.shape[0]
    kmer_len, letter_count, model_width = kmer_table.shape
    local_width = in_proj.shape[2]
    length = row_count * lax.axis_size("seq")
    group_index = lax.axis_index(("chan", "pair"))
    rim_width = kmer_len - 1
    before = from_behind(tokens[row_count - rim_width :] + 1, "seq", 1) - 1
    extended = jnp.concatenate([before, tokens])
    letters = jnp.arange(letter_count, dtype=jnp.int32)
    columns = []
    for shift_back in range(kmer_len):
        window = extended[rim_width - shift_back : rim_width - shift_back + row_count]
        columns.append(window[:, None] == letters[None, :])
    onehot_t = jnp.concatenate(columns, axis=1).T.astype(jnp.bfloat16)
    table_t = kmer_table.reshape(kmer_len * letter_count, model_width).T
    embedded = jnp.dot(table_t, onehot_t, preferred_element_type=jnp.float32)
    inv_rms = lax.rsqrt(jnp.mean(embedded * embedded, axis=0, keepdims=True) + NORM_EPSILON)
    normed = embedded * inv_rms
    scaled_normed = normed * norm_gain[:, None]
    hidden = scaled_normed.astype(jnp.bfloat16)
    projected = jnp.einsum("dr,dmc->mcr", hidden, in_proj, preferred_element_type=jnp.float32)
    residual = (scaled_normed - hidden.astype(jnp.float32)).astype(jnp.bfloat16)
    unrounded = projected + jnp.einsum(
        "dr,dmc->mcr", residual, in_proj, preferred_element_type=jnp.float32
    )
    query_part = projected[0]
    key_part = projected[1]
    value_part = projected[2]
    mixed_in = (key_part * value_part).astype(jnp.bfloat16)
    grad_scale = 1.0 / math.sqrt(length)
    groups = lax.axis_size("chan") * lax.axis_size("pair")
    gated_partial = jnp.einsum("rd,cd->rc", cotangent, out_proj, preferred_element_type=jnp.float32)
    d_gated = reduce_blocks_cp(gated_partial, local_width).T * grad_scale
    dft = dft_matrix(length)
    filter_rows = long_filter.reshape(long_filter.shape[2], long_filter.shape[3])
    spec_g = add_conj_flip(forward_dft(filter_rows, dft))
    ga, gb = halves(spec_g)
    d_conv = (d_gated * query_part).astype(jnp.bfloat16)
    both_cols = all_to_all_seq(jnp.stack([mixed_in, d_conv]), 1, 2)
    mixed_cols, d_cols = both_cols[0], both_cols[1]
    spec_s = forward_dft(mixed_cols, dft)
    sa, sb = halves(spec_s)
    conv_cols = inverse_dft(cmul(ga, gb, sa, sb, False), dft).astype(jnp.bfloat16)
    spec_d = forward_dft(d_cols, dft)
    da, db = halves(spec_d)
    d_mixed_cols = inverse_dft(cmul(ga, gb, da, db, True), dft).astype(jnp.bfloat16)
    both_rows = all_to_all_seq(jnp.stack([conv_cols, d_mixed_cols]), 2, 1)
    conv_rows, d_mixed = both_rows[0], both_rows[1]
    gated_rows = (query_part * conv_rows.astype(jnp.float32)).astype(jnp.bfloat16)
    weight_rows = out_proj
    gathered, sources = all_gather_cp(gated_rows)
    mixed_out = None
    for slot in range(len(sources)):
        piece = gathered[0]
        for index in range(1, len(sources)):
            piece = jnp.where(sources[index] == slot, gathered[index], piece)
        term = jnp.einsum(
            "cr,cd->rd",
            piece,
            weight_rows[slot * local_width : (slot + 1) * local_width],
            preferred_element_type=jnp.float32,
        )
        mixed_out = term if mixed_out is None else mixed_out + term
    own_rows = lax.dynamic_slice_in_dim(embedded, group_index * local_width, local_width, 0)
    block_out = (mixed_out + own_rows.T).astype(jnp.bfloat16)
    d_query = d_gated * conv_rows.astype(jnp.float32)
    cross = cmul(sa, sb, da, db, True)
    filter_grad = inverse_dft(add_conj_flip(cross), dft)
    d_key = d_mixed.astype(jnp.float32) * value_part
    d_value = d_mixed.astype(jnp.float32) * key_part
    d_proj = jnp.stack([d_query, d_key, d_value]).astype(jnp.bfloat16)
    d_full = jnp.einsum("mcr,dmc->rd", d_proj, in_proj, preferred_element_type=jnp.float32)
    stat_part = jnp.sum(d_proj.astype(jnp.float32) * unrounded, axis=(0, 1))
    onehot_rows = onehot_t.T.astype(jnp.float32)
    weights = onehot_rows * inv_rms.T
    direct = jnp.einsum("rk,rd->kd", weights, d_full, precision=PRECISE)
    centred = jnp.einsum("rk,dr->kd", weights * stat_part[:, None], normed, precision=PRECISE)
    table_all = norm_gain[None, :] * direct - centred / model_width
    gain_all = jnp.einsum("rd,dr->d", d_full, normed, precision=PRECISE)
    partial = jnp.concatenate([table_all, gain_all[None, :]], axis=0)
    own_block = reduce_blocks_cp(partial, local_width)
    cot_table = jnp.einsum(
        "rk,rc->kc", onehot_rows, cotangent.astype(jnp.float32) * grad_scale, precision=PRECISE
    )
    own_block = own_block + jnp.concatenate(
        [cot_table, jnp.zeros((1, local_width), jnp.float32)], axis=0
    )
    summed = sum_over_seq(own_block)
    kmer_grad = summed[: kmer_len * letter_count]
    gain_grad = summed[kmer_len * letter_count]
    return (
        block_out,
        filter_grad.reshape(long_filter.shape),
        kmer_grad.reshape(kmer_len, letter_count, local_width),
        gain_grad,
    )


def solution(mesh):
    in_specs = (
        P(("groups", "seq")),
        P(),
        P(),
        P(None, None, ("chan", "pair")),
        P(("chan", "pair"), "seq", None, None),
        P(None, ("chan", "pair")),
        P(("groups", "seq"), ("chan", "pair")),
    )
    out_specs = (
        P(("groups", "seq"), ("chan", "pair")),
        P(("groups", "chan", "pair"), "seq", None, None),
        P("groups", None, ("chan", "pair")),
        P(("groups", "chan", "pair")),
    )
    return jax.shard_map(
        per_device, mesh=mesh, in_specs=in_specs, out_specs=out_specs, check_vma=False
    )
```

```python
import math

import jax
import jax.numpy as jnp
from jax import lax
from jax.sharding import PartitionSpec as P

NORM_EPSILON = 1e-05
PRECISE = lax.Precision.HIGHEST
TRANSFORM_PRECISION = lax.Precision.HIGH


def from_behind(value, axis, steps):
    count = lax.axis_size(axis)
    first, last = (max(0, -steps), min(count, count - steps))
    return lax.ppermute(value, axis, [(source, source + steps) for source in range(first, last)])


def dft_matrix(length):
    total = 2 * length
    inner_len = 32 if length % 32 == 0 else 1
    outer_len = length // inner_len
    j = lax.broadcasted_iota(jnp.int32, (1, total), 1)
    k = jnp.where(j < length, j, j - length)
    k = jnp.where(j == length, length, k)
    phase = jnp.where(j > length, 3 * total // 4, 0)
    scale = 2.0 * math.pi / total

    def angle(idx):
        idx = idx % total
        idx = jnp.where(idx >= length, idx - total, idx)
        return idx.astype(jnp.float32) * scale

    outer = lax.optimization_barrier(lax.broadcasted_iota(jnp.int32, (outer_len, 1), 0))
    inner = lax.optimization_barrier(lax.broadcasted_iota(jnp.int32, (inner_len, 1), 0))
    alpha = angle(outer * inner_len * k)
    beta = angle(inner * k + phase)
    ca, sa = jnp.cos(alpha), jnp.sin(alpha)
    cb, sb = jnp.cos(beta), jnp.sin(beta)
    table = ca[:, None, :] * cb[None, :, :] - sa[:, None, :] * sb[None, :, :]
    return lax.optimization_barrier(table.reshape(length, total))


def xor_exchange(x, axis, step):
    count = lax.axis_size(axis)
    return lax.ppermute(x, axis, [(i, i ^ step) for i in range(count)])


def all_gather_cp(x):
    chans, pairs = lax.axis_size("chan"), lax.axis_size("pair")
    y = x[None]
    sources = [lax.axis_index(("chan", "pair"))]
    for axis, size, stride in (("chan", chans, pairs), ("pair", pairs, 1)):
        step = 1
        while step < size:
            y = jnp.concatenate([y, xor_exchange(y, axis, step)], axis=0)
            sources = sources + [source ^ (step * stride) for source in sources]
            step *= 2
    return y, sources


def group_exchange(x, axes, count, offset):
    return lax.ppermute(x, axes, [(i, i ^ offset) for i in range(count)])


def reduce_blocks_cp(x, width):
    axes = ("chan", "pair")
    count = lax.axis_size("chan") * lax.axis_size("pair")
    me = lax.axis_index(axes)
    blocks = [x[:, g * width : (g + 1) * width] for g in range(count)]

    def pick(index):
        out = blocks[0]
        for g in range(1, count):
            out = jnp.where(index == g, blocks[g], out)
        return out

    total = pick(me)
    for offset in range(1, count):
        total = total + group_exchange(pick(me ^ offset), axes, count, offset)
    return total


def sum_over_seq(x, tied):
    count = lax.axis_size("seq")
    me = lax.axis_index("seq")
    if count > 4:
        step = 1
        while step < count:
            got, tied = lax.optimization_barrier((xor_exchange(x, "seq", step), tied))
            x = x + got
            step *= 2
        return x, tied
    got = [x] + [group_exchange(x, "seq", count, offset) for offset in range(1, count)]
    got, tied = lax.optimization_barrier((got, tied))
    total = None
    for source in range(count):
        piece = got[0]
        for offset in range(1, count):
            piece = jnp.where((me ^ source) == offset, got[offset], piece)
        total = piece if total is None else total + piece
    return total, tied


def all_to_all_seq(x, split_axis, concat_axis):
    count = lax.axis_size("seq")
    if count > 4:
        return lax.all_to_all(x, "seq", split_axis=split_axis, concat_axis=concat_axis, tiled=True)
    me = lax.axis_index("seq")
    width = x.shape[split_axis] // count
    blocks = [lax.slice_in_dim(x, j * width, (j + 1) * width, axis=split_axis) for j in range(count)]

    def pick(index):
        out = blocks[0]
        for j in range(1, count):
            out = jnp.where(index == j, blocks[j], out)
        return out

    got = [pick(me)] + [
        group_exchange(pick(me ^ offset), "seq", count, offset) for offset in range(1, count)
    ]
    pieces = []
    for source in range(count):
        piece = got[0]
        for offset in range(1, count):
            piece = jnp.where((me ^ source) == offset, got[offset], piece)
        pieces.append(piece)
    return jnp.concatenate(pieces, axis=concat_axis)


def forward_dft(signal, dft):
    return jnp.dot(signal.astype(jnp.float32), dft, precision=TRANSFORM_PRECISION)


def inverse_dft(spec, dft):
    length = dft.shape[0]
    total = 2 * length
    col = lax.broadcasted_iota(jnp.int32, (1, total), 1)
    weight = jnp.where(col % length == 0, 1.0 / total, 2.0 / total).astype(jnp.float32)
    return lax.dot_general(
        spec * weight, dft, (((1,), (1,)), ((), ())), precision=TRANSFORM_PRECISION
    )


def halves(spec):
    length = spec.shape[1] // 2
    return spec[:, :length], spec[:, length:]


def first_col(shape):
    return lax.broadcasted_iota(jnp.int32, shape, 1) == 0


def cmul(ga, gb, xa, xb, conj_g):
    edge = first_col(ga.shape)
    sign = -1.0 if conj_g else 1.0
    ya = ga * xa - sign * (gb * xb)
    yb = ga * xb + sign * (gb * xa)
    ya = jnp.where(edge, ga * xa, ya)
    yb = jnp.where(edge, gb * xb, yb)
    return jnp.concatenate([ya, yb], axis=1)


def pair_flip(values):
    rows = lax.broadcasted_iota(jnp.int32, values.shape, 0)
    up = jnp.roll(values, -1, axis=0)
    down = jnp.roll(values, 1, axis=0)
    return jnp.where(rows % 2 == 0, up, down)


def add_conj_flip(spec):
    a, b = halves(spec)
    fa, fb = halves(pair_flip(spec))
    edge = first_col(a.shape)
    return jnp.concatenate([a + fa, jnp.where(edge, b + fb, b - fb)], axis=1)


def norm_gain_local(norm_gain, group_index, local_width):
    return lax.dynamic_slice_in_dim(norm_gain, group_index * local_width, local_width, 0)


def per_device(tokens, kmer_table, norm_gain, in_proj, long_filter, out_proj, cotangent):
    row_count = tokens.shape[0]
    kmer_len, letter_count, model_width = kmer_table.shape
    local_width = in_proj.shape[2]
    length = row_count * lax.axis_size("seq")
    group_index = lax.axis_index(("chan", "pair"))
    rim_width = kmer_len - 1
    before = from_behind(tokens[row_count - rim_width :] + 1, "seq", 1) - 1
    extended = jnp.concatenate([before, tokens])
    letters = jnp.arange(letter_count, dtype=jnp.int32)
    columns = []
    for shift_back in range(kmer_len):
        window = extended[rim_width - shift_back : rim_width - shift_back + row_count]
        columns.append(window[:, None] == letters[None, :])
    onehot_t = jnp.concatenate(columns, axis=1).T.astype(jnp.bfloat16)
    table_t = kmer_table.reshape(kmer_len * letter_count, model_width).T
    embedded = jnp.dot(table_t, onehot_t, preferred_element_type=jnp.float32)
    inv_rms = lax.rsqrt(jnp.mean(embedded * embedded, axis=0, keepdims=True) + NORM_EPSILON)
    normed = embedded * inv_rms
    scaled_normed = normed * norm_gain[:, None]
    hidden = scaled_normed.astype(jnp.bfloat16)
    projected = jnp.einsum("dr,dmc->mcr", hidden, in_proj, preferred_element_type=jnp.float32)
    residual = (scaled_normed - hidden.astype(jnp.float32)).astype(jnp.bfloat16)
    unrounded = projected + jnp.einsum(
        "dr,dmc->mcr", residual, in_proj, preferred_element_type=jnp.float32
    )
    query_part = projected[0]
    key_part = projected[1]
    value_part = projected[2]
    mixed_in = (key_part * value_part).astype(jnp.bfloat16)
    grad_scale = 1.0 / math.sqrt(length)
    groups = lax.axis_size("chan") * lax.axis_size("pair")
    gated_partial = jnp.einsum("rd,cd->rc", cotangent, out_proj, preferred_element_type=jnp.float32)
    d_gated = reduce_blocks_cp(gated_partial, local_width).T * grad_scale
    dft = dft_matrix(length)
    filter_rows = long_filter.reshape(long_filter.shape[2], long_filter.shape[3])
    spec_g = add_conj_flip(forward_dft(filter_rows, dft))
    ga, gb = halves(spec_g)
    d_conv = (d_gated * query_part).astype(jnp.bfloat16)
    both_cols = all_to_all_seq(jnp.stack([mixed_in, d_conv]), 1, 2)
    mixed_cols, d_cols = both_cols[0], both_cols[1]
    spec_s = forward_dft(mixed_cols, dft)
    sa, sb = halves(spec_s)
    conv_cols = inverse_dft(cmul(ga, gb, sa, sb, False), dft).astype(jnp.bfloat16)
    spec_d = forward_dft(d_cols, dft)
    da, db = halves(spec_d)
    d_mixed_cols = inverse_dft(cmul(ga, gb, da, db, True), dft).astype(jnp.bfloat16)
    both_rows = all_to_all_seq(jnp.stack([conv_cols, d_mixed_cols]), 2, 1)
    conv_rows, d_mixed = both_rows[0], both_rows[1]
    gated_rows = (query_part * conv_rows.astype(jnp.float32)).astype(jnp.bfloat16)
    weight_rows = out_proj
    gathered, sources = all_gather_cp(gated_rows)
    mixed_out = None
    for slot in range(len(sources)):
        piece = gathered[0]
        for index in range(1, len(sources)):
            piece = jnp.where(sources[index] == slot, gathered[index], piece)
        term = jnp.einsum(
            "cr,cd->rd",
            piece,
            weight_rows[slot * local_width : (slot + 1) * local_width],
            preferred_element_type=jnp.float32,
        )
        mixed_out = term if mixed_out is None else mixed_out + term
    own_rows = lax.dynamic_slice_in_dim(embedded, group_index * local_width, local_width, 0)
    block_out = (mixed_out + own_rows.T).astype(jnp.bfloat16)
    d_query = d_gated * conv_rows.astype(jnp.float32)
    cross = cmul(sa, sb, da, db, True)
    filter_grad = inverse_dft(add_conj_flip(cross), dft)
    d_key = d_mixed.astype(jnp.float32) * value_part
    d_value = d_mixed.astype(jnp.float32) * key_part
    d_proj = jnp.stack([d_query, d_key, d_value]).astype(jnp.bfloat16)
    d_full = jnp.einsum("mcr,dmc->rd", d_proj, in_proj, preferred_element_type=jnp.float32)
    stat_part = jnp.sum(d_proj.astype(jnp.float32) * unrounded, axis=(0, 1))
    onehot_rows = onehot_t.T.astype(jnp.float32)
    weights = onehot_rows * inv_rms.T
    direct = jnp.einsum("rk,rd->kd", weights, d_full, precision=PRECISE)
    centred = jnp.einsum("rk,dr->kd", weights * stat_part[:, None], normed, precision=PRECISE)
    table_all = norm_gain[None, :] * direct - centred / model_width
    gain_all = jnp.einsum("rd,dr->d", d_full, normed, precision=PRECISE)
    partial = jnp.concatenate([table_all, gain_all[None, :]], axis=0)
    own_block = reduce_blocks_cp(partial, local_width)
    cot_table = jnp.einsum(
        "rk,rc->kc", onehot_rows, cotangent.astype(jnp.float32) * grad_scale, precision=PRECISE
    )
    own_block = own_block + jnp.concatenate(
        [cot_table, jnp.zeros((1, local_width), jnp.float32)], axis=0
    )
    summed, (block_out, filter_grad) = sum_over_seq(own_block, (block_out, filter_grad))
    kmer_grad = summed[: kmer_len * letter_count]
    gain_grad = summed[kmer_len * letter_count]
    return (
        block_out,
        filter_grad.reshape(long_filter.shape),
        kmer_grad.reshape(kmer_len, letter_count, local_width),
        gain_grad,
    )


def solution(mesh):
    in_specs = (
        P(("groups", "seq")),
        P(),
        P(),
        P(None, None, ("chan", "pair")),
        P(("chan", "pair"), "seq", None, None),
        P(None, ("chan", "pair")),
        P(("groups", "seq"), ("chan", "pair")),
    )
    out_specs = (
        P(("groups", "seq"), ("chan", "pair")),
        P(("groups", "chan", "pair"), "seq", None, None),
        P("groups", None, ("chan", "pair")),
        P(("groups", "chan", "pair")),
    )
    return jax.shard_map(
        per_device, mesh=mesh, in_specs=in_specs, out_specs=out_specs, check_vma=False
    )
```

```python
import math

import jax
import jax.numpy as jnp
from jax import lax
from jax.sharding import PartitionSpec as P

NORM_EPSILON = 1e-05
PRECISE = lax.Precision.HIGHEST
TRANSFORM_PRECISION = lax.Precision.HIGH


def from_behind(value, axis, steps):
    count = lax.axis_size(axis)
    first, last = (max(0, -steps), min(count, count - steps))
    return lax.ppermute(value, axis, [(source, source + steps) for source in range(first, last)])


def dft_matrix(length):
    total = 2 * length
    inner_len = 32 if length % 32 == 0 else 1
    outer_len = length // inner_len
    j = lax.broadcasted_iota(jnp.int32, (1, total), 1)
    k = jnp.where(j < length, j, j - length)
    k = jnp.where(j == length, length, k)
    phase = jnp.where(j > length, 3 * total // 4, 0)
    scale = 2.0 * math.pi / total

    def angle(idx):
        idx = idx % total
        idx = jnp.where(idx >= length, idx - total, idx)
        return idx.astype(jnp.float32) * scale

    outer = lax.optimization_barrier(lax.broadcasted_iota(jnp.int32, (outer_len, 1), 0))
    inner = lax.optimization_barrier(lax.broadcasted_iota(jnp.int32, (inner_len, 1), 0))
    alpha = angle(outer * inner_len * k)
    beta = angle(inner * k + phase)
    ca, sa = jnp.cos(alpha), jnp.sin(alpha)
    cb, sb = jnp.cos(beta), jnp.sin(beta)
    table = ca[:, None, :] * cb[None, :, :] - sa[:, None, :] * sb[None, :, :]
    return lax.optimization_barrier(table.reshape(length, total))


def xor_exchange(x, axis, step):
    count = lax.axis_size(axis)
    return lax.ppermute(x, axis, [(i, i ^ step) for i in range(count)])


def all_gather_cp(x):
    chans, pairs = lax.axis_size("chan"), lax.axis_size("pair")
    y = x[None]
    sources = [lax.axis_index(("chan", "pair"))]
    for axis, size, stride in (("chan", chans, pairs), ("pair", pairs, 1)):
        step = 1
        while step < size:
            y = jnp.concatenate([y, xor_exchange(y, axis, step)], axis=0)
            sources = sources + [source ^ (step * stride) for source in sources]
            step *= 2
    return y, sources


def group_exchange(x, axes, count, offset):
    return lax.ppermute(x, axes, [(i, i ^ offset) for i in range(count)])


def reduce_blocks_cp(x, width, axis=1):
    axes = ("chan", "pair")
    count = lax.axis_size("chan") * lax.axis_size("pair")
    me = lax.axis_index(axes)
    blocks = [lax.slice_in_dim(x, g * width, (g + 1) * width, axis=axis) for g in range(count)]

    def pick(index):
        out = blocks[0]
        for g in range(1, count):
            out = jnp.where(index == g, blocks[g], out)
        return out

    total = pick(me)
    for offset in range(1, count):
        total = total + group_exchange(pick(me ^ offset), axes, count, offset)
    return total


def sum_over_seq(x, tied):
    count = lax.axis_size("seq")
    me = lax.axis_index("seq")
    if count > 4:
        step = 1
        while step < count:
            got, tied = lax.optimization_barrier((xor_exchange(x, "seq", step), tied))
            x = x + got
            step *= 2
        return x, tied
    got = [x] + [group_exchange(x, "seq", count, offset) for offset in range(1, count)]
    got, tied = lax.optimization_barrier((got, tied))
    total = None
    for source in range(count):
        piece = got[0]
        for offset in range(1, count):
            piece = jnp.where((me ^ source) == offset, got[offset], piece)
        total = piece if total is None else total + piece
    return total, tied


def all_to_all_seq(x, split_axis, concat_axis):
    count = lax.axis_size("seq")
    if count > 4:
        return lax.all_to_all(x, "seq", split_axis=split_axis, concat_axis=concat_axis, tiled=True)
    me = lax.axis_index("seq")
    width = x.shape[split_axis] // count
    blocks = [lax.slice_in_dim(x, j * width, (j + 1) * width, axis=split_axis) for j in range(count)]

    def pick(index):
        out = blocks[0]
        for j in range(1, count):
            out = jnp.where(index == j, blocks[j], out)
        return out

    got = [pick(me)] + [
        group_exchange(pick(me ^ offset), "seq", count, offset) for offset in range(1, count)
    ]
    pieces = []
    for source in range(count):
        piece = got[0]
        for offset in range(1, count):
            piece = jnp.where((me ^ source) == offset, got[offset], piece)
        pieces.append(piece)
    return jnp.concatenate(pieces, axis=concat_axis)


def forward_dft(signal, dft):
    return jnp.dot(signal.astype(jnp.float32), dft, precision=TRANSFORM_PRECISION)


def inverse_dft(spec, dft):
    length = dft.shape[0]
    total = 2 * length
    col = lax.broadcasted_iota(jnp.int32, (1, total), 1)
    weight = jnp.where(col % length == 0, 1.0 / total, 2.0 / total).astype(jnp.float32)
    return lax.dot_general(
        spec * weight, dft, (((1,), (1,)), ((), ())), precision=TRANSFORM_PRECISION
    )


def halves(spec):
    length = spec.shape[1] // 2
    return spec[:, :length], spec[:, length:]


def first_col(shape):
    return lax.broadcasted_iota(jnp.int32, shape, 1) == 0


def cmul(ga, gb, xa, xb, conj_g):
    edge = first_col(ga.shape)
    sign = -1.0 if conj_g else 1.0
    ya = ga * xa - sign * (gb * xb)
    yb = ga * xb + sign * (gb * xa)
    ya = jnp.where(edge, ga * xa, ya)
    yb = jnp.where(edge, gb * xb, yb)
    return jnp.concatenate([ya, yb], axis=1)


def pair_flip(values):
    rows = lax.broadcasted_iota(jnp.int32, values.shape, 0)
    up = jnp.roll(values, -1, axis=0)
    down = jnp.roll(values, 1, axis=0)
    return jnp.where(rows % 2 == 0, up, down)


def add_conj_flip(spec):
    a, b = halves(spec)
    fa, fb = halves(pair_flip(spec))
    edge = first_col(a.shape)
    return jnp.concatenate([a + fa, jnp.where(edge, b + fb, b - fb)], axis=1)


def norm_gain_local(norm_gain, group_index, local_width):
    return lax.dynamic_slice_in_dim(norm_gain, group_index * local_width, local_width, 0)


def per_device(tokens, kmer_table, norm_gain, in_proj, long_filter, out_proj, cotangent):
    row_count = tokens.shape[0]
    kmer_len, letter_count, model_width = kmer_table.shape
    local_width = in_proj.shape[2]
    length = row_count * lax.axis_size("seq")
    group_index = lax.axis_index(("chan", "pair"))
    rim_width = kmer_len - 1
    before = from_behind(tokens[row_count - rim_width :] + 1, "seq", 1) - 1
    extended = jnp.concatenate([before, tokens])
    letters = jnp.arange(letter_count, dtype=jnp.int32)
    columns = []
    for shift_back in range(kmer_len):
        window = extended[rim_width - shift_back : rim_width - shift_back + row_count]
        columns.append(window[:, None] == letters[None, :])
    onehot_t = jnp.concatenate(columns, axis=1).T.astype(jnp.bfloat16)
    table_t = kmer_table.reshape(kmer_len * letter_count, model_width).T
    embedded = jnp.dot(table_t, onehot_t, preferred_element_type=jnp.float32)
    inv_rms = lax.rsqrt(jnp.mean(embedded * embedded, axis=0, keepdims=True) + NORM_EPSILON)
    normed = embedded * inv_rms
    scaled_normed = normed * norm_gain[:, None]
    hidden = scaled_normed.astype(jnp.bfloat16)
    projected = jnp.einsum("dr,dmc->mcr", hidden, in_proj, preferred_element_type=jnp.float32)
    residual = (scaled_normed - hidden.astype(jnp.float32)).astype(jnp.bfloat16)
    unrounded = projected + jnp.einsum(
        "dr,dmc->mcr", residual, in_proj, preferred_element_type=jnp.float32
    )
    query_part = projected[0]
    key_part = projected[1]
    value_part = projected[2]
    mixed_in = (key_part * value_part).astype(jnp.bfloat16)
    grad_scale = 1.0 / math.sqrt(length)
    groups = lax.axis_size("chan") * lax.axis_size("pair")
    gated_partial = jnp.einsum("cd,rd->cr", out_proj, cotangent, preferred_element_type=jnp.float32)
    d_gated = reduce_blocks_cp(gated_partial, local_width, axis=0) * grad_scale
    dft = dft_matrix(length)
    filter_rows = long_filter.reshape(long_filter.shape[2], long_filter.shape[3])
    spec_g = add_conj_flip(forward_dft(filter_rows, dft))
    ga, gb = halves(spec_g)
    d_conv = (d_gated * query_part).astype(jnp.bfloat16)
    both_cols = all_to_all_seq(jnp.stack([mixed_in, d_conv]), 1, 2)
    mixed_cols, d_cols = both_cols[0], both_cols[1]
    spec_s = forward_dft(mixed_cols, dft)
    sa, sb = halves(spec_s)
    conv_cols = inverse_dft(cmul(ga, gb, sa, sb, False), dft).astype(jnp.bfloat16)
    spec_d = forward_dft(d_cols, dft)
    da, db = halves(spec_d)
    d_mixed_cols = inverse_dft(cmul(ga, gb, da, db, True), dft).astype(jnp.bfloat16)
    both_rows = all_to_all_seq(jnp.stack([conv_cols, d_mixed_cols]), 2, 1)
    conv_rows, d_mixed = both_rows[0], both_rows[1]
    gated_rows = (query_part * conv_rows.astype(jnp.float32)).astype(jnp.bfloat16)
    weight_rows = out_proj
    gathered, sources = all_gather_cp(gated_rows)
    mixed_out = None
    for slot in range(len(sources)):
        piece = gathered[0]
        for index in range(1, len(sources)):
            piece = jnp.where(sources[index] == slot, gathered[index], piece)
        term = jnp.einsum(
            "cr,cd->rd",
            piece,
            weight_rows[slot * local_width : (slot + 1) * local_width],
            preferred_element_type=jnp.float32,
        )
        mixed_out = term if mixed_out is None else mixed_out + term
    own_rows = lax.dynamic_slice_in_dim(embedded, group_index * local_width, local_width, 0)
    block_out = (mixed_out + own_rows.T).astype(jnp.bfloat16)
    d_query = d_gated * conv_rows.astype(jnp.float32)
    cross = cmul(sa, sb, da, db, True)
    filter_grad = inverse_dft(add_conj_flip(cross), dft)
    d_key = d_mixed.astype(jnp.float32) * value_part
    d_value = d_mixed.astype(jnp.float32) * key_part
    d_proj = jnp.stack([d_query, d_key, d_value]).astype(jnp.bfloat16)
    d_full = jnp.einsum("mcr,dmc->rd", d_proj, in_proj, preferred_element_type=jnp.float32)
    stat_part = jnp.sum(d_proj.astype(jnp.float32) * unrounded, axis=(0, 1))
    onehot_rows = onehot_t.T.astype(jnp.float32)
    weights = onehot_rows * inv_rms.T
    direct = jnp.einsum("rk,rd->kd", weights, d_full, precision=PRECISE)
    centred = jnp.einsum("rk,dr->kd", weights * stat_part[:, None], normed, precision=PRECISE)
    table_all = norm_gain[None, :] * direct - centred / model_width
    gain_all = jnp.einsum("rd,dr->d", d_full, normed, precision=PRECISE)
    partial = jnp.concatenate([table_all, gain_all[None, :]], axis=0)
    own_block = reduce_blocks_cp(partial, local_width)
    cot_table = jnp.einsum(
        "rk,rc->kc", onehot_rows, cotangent.astype(jnp.float32) * grad_scale, precision=PRECISE
    )
    own_block = own_block + jnp.concatenate(
        [cot_table, jnp.zeros((1, local_width), jnp.float32)], axis=0
    )
    summed, (block_out, filter_grad) = sum_over_seq(own_block, (block_out, filter_grad))
    kmer_grad = summed[: kmer_len * letter_count]
    gain_grad = summed[kmer_len * letter_count]
    return (
        block_out,
        filter_grad.reshape(long_filter.shape),
        kmer_grad.reshape(kmer_len, letter_count, local_width),
        gain_grad,
    )


def solution(mesh):
    in_specs = (
        P(("groups", "seq")),
        P(),
        P(),
        P(None, None, ("chan", "pair")),
        P(("chan", "pair"), "seq", None, None),
        P(None, ("chan", "pair")),
        P(("groups", "seq"), ("chan", "pair")),
    )
    out_specs = (
        P(("groups", "seq"), ("chan", "pair")),
        P(("groups", "chan", "pair"), "seq", None, None),
        P("groups", None, ("chan", "pair")),
        P(("groups", "chan", "pair")),
    )
    return jax.shard_map(
        per_device, mesh=mesh, in_specs=in_specs, out_specs=out_specs, check_vma=False
    )
```

```python
import math

import jax
import jax.numpy as jnp
import numpy as np
from jax import lax
from jax.sharding import PartitionSpec as P

NORM_EPSILON = 1e-05
PRECISE = lax.Precision.HIGHEST
TRANSFORM_PRECISION = lax.Precision.HIGH


def from_behind(value, axis, steps):
    count = lax.axis_size(axis)
    first, last = (max(0, -steps), min(count, count - steps))
    return lax.ppermute(value, axis, [(source, source + steps) for source in range(first, last)])


def dft_matrix(length):
    total = 2 * length
    inner_len = 32 if length % 32 == 0 else 1
    outer_len = length // inner_len
    j = lax.broadcasted_iota(jnp.int32, (1, total), 1)
    k = jnp.where(j < length, j, j - length)
    k = jnp.where(j == length, length, k)
    phase = jnp.where(j > length, 3 * total // 4, 0)
    scale = 2.0 * math.pi / total

    def angle(idx):
        idx = idx % total
        idx = jnp.where(idx >= length, idx - total, idx)
        return idx.astype(jnp.float32) * scale

    outer = lax.optimization_barrier(lax.broadcasted_iota(jnp.int32, (outer_len, 1), 0))
    inner = lax.optimization_barrier(lax.broadcasted_iota(jnp.int32, (inner_len, 1), 0))
    alpha = angle(outer * inner_len * k)
    beta = angle(inner * k + phase)
    ca, sa = jnp.cos(alpha), jnp.sin(alpha)
    cb, sb = jnp.cos(beta), jnp.sin(beta)
    table = ca[:, None, :] * cb[None, :, :] - sa[:, None, :] * sb[None, :, :]
    return lax.optimization_barrier(table.reshape(length, total))


def xor_exchange(x, axis, step):
    count = lax.axis_size(axis)
    return lax.ppermute(x, axis, [(i, i ^ step) for i in range(count)])


def all_gather_cp(x):
    chans, pairs = lax.axis_size("chan"), lax.axis_size("pair")
    y = x[None]
    sources = [lax.axis_index(("chan", "pair"))]
    for axis, size, stride in (("chan", chans, pairs), ("pair", pairs, 1)):
        step = 1
        while step < size:
            y = jnp.concatenate([y, xor_exchange(y, axis, step)], axis=0)
            sources = sources + [source ^ (step * stride) for source in sources]
            step *= 2
    return y, sources


def group_exchange(x, axes, count, offset):
    return lax.ppermute(x, axes, [(i, i ^ offset) for i in range(count)])


def reduce_blocks_cp(x, width):
    axes = ("chan", "pair")
    count = lax.axis_size("chan") * lax.axis_size("pair")
    me = lax.axis_index(axes)
    blocks = [x[:, g * width : (g + 1) * width] for g in range(count)]

    def pick(index):
        out = blocks[0]
        for g in range(1, count):
            out = jnp.where(index == g, blocks[g], out)
        return out

    total = pick(me)
    for offset in range(1, count):
        total = total + group_exchange(pick(me ^ offset), axes, count, offset)
    return total


def sum_over_seq(x, tied):
    count = lax.axis_size("seq")
    me = lax.axis_index("seq")
    if count > 4:
        step = 1
        while step < count:
            got, tied = lax.optimization_barrier((xor_exchange(x, "seq", step), tied))
            x = x + got
            step *= 2
        return x, tied
    got = [x] + [group_exchange(x, "seq", count, offset) for offset in range(1, count)]
    got, tied = lax.optimization_barrier((got, tied))
    total = None
    for source in range(count):
        piece = got[0]
        for offset in range(1, count):
            piece = jnp.where((me ^ source) == offset, got[offset], piece)
        total = piece if total is None else total + piece
    return total, tied


def all_to_all_seq(x, split_axis, concat_axis):
    count = lax.axis_size("seq")
    if count > 4:
        return lax.all_to_all(x, "seq", split_axis=split_axis, concat_axis=concat_axis, tiled=True)
    me = lax.axis_index("seq")
    width = x.shape[split_axis] // count
    blocks = [lax.slice_in_dim(x, j * width, (j + 1) * width, axis=split_axis) for j in range(count)]

    def pick(index):
        out = blocks[0]
        for j in range(1, count):
            out = jnp.where(index == j, blocks[j], out)
        return out

    got = [pick(me)] + [
        group_exchange(pick(me ^ offset), "seq", count, offset) for offset in range(1, count)
    ]
    pieces = []
    for source in range(count):
        piece = got[0]
        for offset in range(1, count):
            piece = jnp.where((me ^ source) == offset, got[offset], piece)
        pieces.append(piece)
    return jnp.concatenate(pieces, axis=concat_axis)


def forward_dft(signal, dft):
    return jnp.dot(signal.astype(jnp.float32), dft, precision=TRANSFORM_PRECISION)


def inverse_dft(spec, dft):
    length = dft.shape[0]
    total = 2 * length
    col = np.arange(total)[None, :]
    weight = np.where(col % length == 0, 1.0 / total, 2.0 / total).astype(np.float32)
    return lax.dot_general(
        spec * weight, dft, (((1,), (1,)), ((), ())), precision=TRANSFORM_PRECISION
    )


def halves(spec):
    length = spec.shape[1] // 2
    return spec[:, :length], spec[:, length:]


def first_col(shape):
    return np.arange(shape[1])[None, :] == 0


def cmul(ga, gb, xa, xb, conj_g):
    edge = first_col(ga.shape)
    sign = -1.0 if conj_g else 1.0
    ya = ga * xa - sign * (gb * xb)
    yb = ga * xb + sign * (gb * xa)
    ya = jnp.where(edge, ga * xa, ya)
    yb = jnp.where(edge, gb * xb, yb)
    return jnp.concatenate([ya, yb], axis=1)


def pair_flip(values):
    even = (np.arange(values.shape[0]) % 2 == 0)[:, None]
    up = jnp.roll(values, -1, axis=0)
    down = jnp.roll(values, 1, axis=0)
    return jnp.where(even, up, down)


def add_conj_flip(spec):
    a, b = halves(spec)
    fa, fb = halves(pair_flip(spec))
    edge = first_col(a.shape)
    return jnp.concatenate([a + fa, jnp.where(edge, b + fb, b - fb)], axis=1)


def norm_gain_local(norm_gain, group_index, local_width):
    return lax.dynamic_slice_in_dim(norm_gain, group_index * local_width, local_width, 0)


def per_device(tokens, kmer_table, norm_gain, in_proj, long_filter, out_proj, cotangent):
    row_count = tokens.shape[0]
    kmer_len, letter_count, model_width = kmer_table.shape
    local_width = in_proj.shape[2]
    length = row_count * lax.axis_size("seq")
    group_index = lax.axis_index(("chan", "pair"))
    rim_width = kmer_len - 1
    before = from_behind(tokens[row_count - rim_width :] + 1, "seq", 1) - 1
    extended = jnp.concatenate([before, tokens])
    letters = jnp.arange(letter_count, dtype=jnp.int32)
    columns = []
    for shift_back in range(kmer_len):
        window = extended[rim_width - shift_back : rim_width - shift_back + row_count]
        columns.append(window[:, None] == letters[None, :])
    onehot_t = jnp.concatenate(columns, axis=1).T.astype(jnp.bfloat16)
    table_t = kmer_table.reshape(kmer_len * letter_count, model_width).T
    embedded = jnp.dot(table_t, onehot_t, preferred_element_type=jnp.float32)
    inv_rms = lax.rsqrt(jnp.mean(embedded * embedded, axis=0, keepdims=True) + NORM_EPSILON)
    normed = embedded * inv_rms
    scaled_normed = normed * norm_gain[:, None]
    hidden = scaled_normed.astype(jnp.bfloat16)
    projected = jnp.einsum("dr,dmc->mcr", hidden, in_proj, preferred_element_type=jnp.float32)
    residual = (scaled_normed - hidden.astype(jnp.float32)).astype(jnp.bfloat16)
    unrounded = projected + jnp.einsum(
        "dr,dmc->mcr", residual, in_proj, preferred_element_type=jnp.float32
    )
    query_part = projected[0]
    key_part = projected[1]
    value_part = projected[2]
    mixed_in = (key_part * value_part).astype(jnp.bfloat16)
    grad_scale = 1.0 / math.sqrt(length)
    groups = lax.axis_size("chan") * lax.axis_size("pair")
    gated_partial = jnp.einsum("rd,cd->rc", cotangent, out_proj, preferred_element_type=jnp.float32)
    d_gated = reduce_blocks_cp(gated_partial, local_width).T * grad_scale
    dft = dft_matrix(length)
    filter_rows = long_filter.reshape(long_filter.shape[2], long_filter.shape[3])
    spec_g = add_conj_flip(forward_dft(filter_rows, dft))
    ga, gb = halves(spec_g)
    d_conv = (d_gated * query_part).astype(jnp.bfloat16)
    both_cols = all_to_all_seq(jnp.stack([mixed_in, d_conv]), 1, 2)
    mixed_cols, d_cols = both_cols[0], both_cols[1]
    spec_s = forward_dft(mixed_cols, dft)
    sa, sb = halves(spec_s)
    conv_cols = inverse_dft(cmul(ga, gb, sa, sb, False), dft).astype(jnp.bfloat16)
    spec_d = forward_dft(d_cols, dft)
    da, db = halves(spec_d)
    d_mixed_cols = inverse_dft(cmul(ga, gb, da, db, True), dft).astype(jnp.bfloat16)
    both_rows = all_to_all_seq(jnp.stack([conv_cols, d_mixed_cols]), 2, 1)
    conv_rows, d_mixed = both_rows[0], both_rows[1]
    gated_rows = (query_part * conv_rows.astype(jnp.float32)).astype(jnp.bfloat16)
    weight_rows = out_proj
    gathered, sources = all_gather_cp(gated_rows)
    mixed_out = None
    for slot in range(len(sources)):
        piece = gathered[0]
        for index in range(1, len(sources)):
            piece = jnp.where(sources[index] == slot, gathered[index], piece)
        term = jnp.einsum(
            "cr,cd->rd",
            piece,
            weight_rows[slot * local_width : (slot + 1) * local_width],
            preferred_element_type=jnp.float32,
        )
        mixed_out = term if mixed_out is None else mixed_out + term
    own_rows = lax.dynamic_slice_in_dim(embedded, group_index * local_width, local_width, 0)
    block_out = (mixed_out + own_rows.T).astype(jnp.bfloat16)
    d_query = d_gated * conv_rows.astype(jnp.float32)
    cross = cmul(sa, sb, da, db, True)
    filter_grad = inverse_dft(add_conj_flip(cross), dft)
    d_key = d_mixed.astype(jnp.float32) * value_part
    d_value = d_mixed.astype(jnp.float32) * key_part
    d_proj = jnp.stack([d_query, d_key, d_value]).astype(jnp.bfloat16)
    d_full = jnp.einsum("mcr,dmc->rd", d_proj, in_proj, preferred_element_type=jnp.float32)
    stat_part = jnp.sum(d_proj.astype(jnp.float32) * unrounded, axis=(0, 1))
    onehot_rows = onehot_t.T.astype(jnp.float32)
    weights = onehot_rows * inv_rms.T
    direct = jnp.einsum("rk,rd->kd", weights, d_full, precision=PRECISE)
    centred = jnp.einsum("rk,dr->kd", weights * stat_part[:, None], normed, precision=PRECISE)
    table_all = norm_gain[None, :] * direct - centred / model_width
    gain_all = jnp.einsum("rd,dr->d", d_full, normed, precision=PRECISE)
    partial = jnp.concatenate([table_all, gain_all[None, :]], axis=0)
    own_block = reduce_blocks_cp(partial, local_width)
    cot_table = jnp.einsum(
        "rk,rc->kc", onehot_rows, cotangent.astype(jnp.float32) * grad_scale, precision=PRECISE
    )
    own_block = own_block + jnp.concatenate(
        [cot_table, jnp.zeros((1, local_width), jnp.float32)], axis=0
    )
    summed, (block_out, filter_grad) = sum_over_seq(own_block, (block_out, filter_grad))
    kmer_grad = summed[: kmer_len * letter_count]
    gain_grad = summed[kmer_len * letter_count]
    return (
        block_out,
        filter_grad.reshape(long_filter.shape),
        kmer_grad.reshape(kmer_len, letter_count, local_width),
        gain_grad,
    )


def solution(mesh):
    in_specs = (
        P(("groups", "seq")),
        P(),
        P(),
        P(None, None, ("chan", "pair")),
        P(("chan", "pair"), "seq", None, None),
        P(None, ("chan", "pair")),
        P(("groups", "seq"), ("chan", "pair")),
    )
    out_specs = (
        P(("groups", "seq"), ("chan", "pair")),
        P(("groups", "chan", "pair"), "seq", None, None),
        P("groups", None, ("chan", "pair")),
        P(("groups", "chan", "pair")),
    )
    return jax.shard_map(
        per_device, mesh=mesh, in_specs=in_specs, out_specs=out_specs, check_vma=False
    )
```

```python
import math

import jax
import jax.numpy as jnp
import numpy as np
from jax import lax
from jax.sharding import PartitionSpec as P

NORM_EPSILON = 1e-05
PRECISE = lax.Precision.HIGHEST
TRANSFORM_PRECISION = lax.Precision.HIGH


def from_behind(value, axis, steps):
    count = lax.axis_size(axis)
    first, last = (max(0, -steps), min(count, count - steps))
    return lax.ppermute(value, axis, [(source, source + steps) for source in range(first, last)])


def dft_matrix(length):
    total = 2 * length
    inner_len = 32 if length % 32 == 0 else 1
    outer_len = length // inner_len
    j = lax.broadcasted_iota(jnp.int32, (1, total), 1)
    k = jnp.where(j < length, j, j - length)
    k = jnp.where(j == length, length, k)
    phase = jnp.where(j > length, 3 * total // 4, 0)
    scale = 2.0 * math.pi / total

    def angle(idx):
        idx = idx % total
        idx = jnp.where(idx >= length, idx - total, idx)
        return idx.astype(jnp.float32) * scale

    outer = lax.optimization_barrier(lax.broadcasted_iota(jnp.int32, (outer_len, 1), 0))
    inner = lax.optimization_barrier(lax.broadcasted_iota(jnp.int32, (inner_len, 1), 0))
    alpha = angle(outer * inner_len * k)
    beta = angle(inner * k + phase)
    ca, sa = jnp.cos(alpha), jnp.sin(alpha)
    cb, sb = jnp.cos(beta), jnp.sin(beta)
    table = ca[:, None, :] * cb[None, :, :] - sa[:, None, :] * sb[None, :, :]
    return lax.optimization_barrier(table.reshape(length, total))


def xor_exchange(x, axis, step):
    count = lax.axis_size(axis)
    return lax.ppermute(x, axis, [(i, i ^ step) for i in range(count)])


def all_gather_cp(x):
    chans, pairs = lax.axis_size("chan"), lax.axis_size("pair")
    y = x[None]
    sources = [lax.axis_index(("chan", "pair"))]
    for axis, size, stride in (("chan", chans, pairs), ("pair", pairs, 1)):
        step = 1
        while step < size:
            y = jnp.concatenate([y, xor_exchange(y, axis, step)], axis=0)
            sources = sources + [source ^ (step * stride) for source in sources]
            step *= 2
    return y, sources


def group_exchange(x, axes, count, offset):
    return lax.ppermute(x, axes, [(i, i ^ offset) for i in range(count)])


def reduce_blocks_cp(x, width):
    axes = ("chan", "pair")
    count = lax.axis_size("chan") * lax.axis_size("pair")
    me = lax.axis_index(axes)
    blocks = [x[:, g * width : (g + 1) * width] for g in range(count)]

    def pick(index):
        out = blocks[0]
        for g in range(1, count):
            out = jnp.where(index == g, blocks[g], out)
        return out

    total = pick(me)
    for offset in range(1, count):
        total = total + group_exchange(pick(me ^ offset), axes, count, offset)
    return total


def sum_over_seq(x, tied):
    count = lax.axis_size("seq")
    me = lax.axis_index("seq")
    if count > 1:
        step = 1
        while step < count:
            got, tied = lax.optimization_barrier((xor_exchange(x, "seq", step), tied))
            x = x + got
            step *= 2
        return x, tied
    got = [x] + [group_exchange(x, "seq", count, offset) for offset in range(1, count)]
    got, tied = lax.optimization_barrier((got, tied))
    total = None
    for source in range(count):
        piece = got[0]
        for offset in range(1, count):
            piece = jnp.where((me ^ source) == offset, got[offset], piece)
        total = piece if total is None else total + piece
    return total, tied


def all_to_all_seq(x, split_axis, concat_axis):
    count = lax.axis_size("seq")
    if count > 4:
        return lax.all_to_all(x, "seq", split_axis=split_axis, concat_axis=concat_axis, tiled=True)
    me = lax.axis_index("seq")
    width = x.shape[split_axis] // count
    blocks = [lax.slice_in_dim(x, j * width, (j + 1) * width, axis=split_axis) for j in range(count)]

    def pick(index):
        out = blocks[0]
        for j in range(1, count):
            out = jnp.where(index == j, blocks[j], out)
        return out

    got = [pick(me)] + [
        group_exchange(pick(me ^ offset), "seq", count, offset) for offset in range(1, count)
    ]
    pieces = []
    for source in range(count):
        piece = got[0]
        for offset in range(1, count):
            piece = jnp.where((me ^ source) == offset, got[offset], piece)
        pieces.append(piece)
    return jnp.concatenate(pieces, axis=concat_axis)


def forward_dft(signal, dft):
    return jnp.dot(signal.astype(jnp.float32), dft, precision=TRANSFORM_PRECISION)


def inverse_dft(spec, dft):
    length = dft.shape[0]
    total = 2 * length
    col = np.arange(total)[None, :]
    weight = np.where(col % length == 0, 1.0 / total, 2.0 / total).astype(np.float32)
    return lax.dot_general(
        spec * weight, dft, (((1,), (1,)), ((), ())), precision=TRANSFORM_PRECISION
    )


def halves(spec):
    length = spec.shape[1] // 2
    return spec[:, :length], spec[:, length:]


def first_col(shape):
    return np.arange(shape[1])[None, :] == 0


def cmul(ga, gb, xa, xb, conj_g):
    edge = first_col(ga.shape)
    sign = -1.0 if conj_g else 1.0
    ya = ga * xa - sign * (gb * xb)
    yb = ga * xb + sign * (gb * xa)
    ya = jnp.where(edge, ga * xa, ya)
    yb = jnp.where(edge, gb * xb, yb)
    return jnp.concatenate([ya, yb], axis=1)


def pair_flip(values):
    even = (np.arange(values.shape[0]) % 2 == 0)[:, None]
    up = jnp.roll(values, -1, axis=0)
    down = jnp.roll(values, 1, axis=0)
    return jnp.where(even, up, down)


def add_conj_flip(spec):
    a, b = halves(spec)
    fa, fb = halves(pair_flip(spec))
    edge = first_col(a.shape)
    return jnp.concatenate([a + fa, jnp.where(edge, b + fb, b - fb)], axis=1)


def norm_gain_local(norm_gain, group_index, local_width):
    return lax.dynamic_slice_in_dim(norm_gain, group_index * local_width, local_width, 0)


def per_device(tokens, kmer_table, norm_gain, in_proj, long_filter, out_proj, cotangent):
    row_count = tokens.shape[0]
    kmer_len, letter_count, model_width = kmer_table.shape
    local_width = in_proj.shape[2]
    length = row_count * lax.axis_size("seq")
    group_index = lax.axis_index(("chan", "pair"))
    rim_width = kmer_len - 1
    before = from_behind(tokens[row_count - rim_width :] + 1, "seq", 1) - 1
    extended = jnp.concatenate([before, tokens])
    letters = jnp.arange(letter_count, dtype=jnp.int32)
    columns = []
    for shift_back in range(kmer_len):
        window = extended[rim_width - shift_back : rim_width - shift_back + row_count]
        columns.append(window[:, None] == letters[None, :])
    onehot_t = jnp.concatenate(columns, axis=1).T.astype(jnp.bfloat16)
    embedded = jnp.einsum(
        "kad,kar->dr",
        kmer_table,
        onehot_t.reshape(kmer_len, letter_count, row_count),
        preferred_element_type=jnp.float32,
    )
    inv_rms = lax.rsqrt(jnp.mean(embedded * embedded, axis=0, keepdims=True) + NORM_EPSILON)
    normed = embedded * inv_rms
    scaled_normed = normed * norm_gain[:, None]
    hidden = scaled_normed.astype(jnp.bfloat16)
    projected = jnp.einsum("dr,dmc->mcr", hidden, in_proj, preferred_element_type=jnp.float32)
    residual = (scaled_normed - hidden.astype(jnp.float32)).astype(jnp.bfloat16)
    unrounded = projected + jnp.einsum(
        "dr,dmc->mcr", residual, in_proj, preferred_element_type=jnp.float32
    )
    query_part = projected[0]
    key_part = projected[1]
    value_part = projected[2]
    mixed_in = (key_part * value_part).astype(jnp.bfloat16)
    grad_scale = 1.0 / math.sqrt(length)
    groups = lax.axis_size("chan") * lax.axis_size("pair")
    gated_partial = jnp.einsum("rd,cd->rc", cotangent, out_proj, preferred_element_type=jnp.float32)
    d_gated = reduce_blocks_cp(gated_partial, local_width).T * grad_scale
    dft = dft_matrix(length)
    filter_rows = long_filter.reshape(long_filter.shape[2], long_filter.shape[3])
    both_filters = forward_dft(jnp.concatenate([filter_rows, pair_flip(filter_rows)], axis=0), dft)
    conj_sign = np.where(np.arange(2 * length) > length, -1.0, 1.0).astype(np.float32)[None, :]
    channels = filter_rows.shape[0]
    spec_g = both_filters[:channels] + both_filters[channels:] * conj_sign
    ga, gb = halves(spec_g)
    d_conv = (d_gated * query_part).astype(jnp.bfloat16)
    both_cols = all_to_all_seq(jnp.stack([mixed_in, d_conv]), 1, 2)
    mixed_cols, d_cols = both_cols[0], both_cols[1]
    spec_s = forward_dft(mixed_cols, dft)
    sa, sb = halves(spec_s)
    conv_cols = inverse_dft(cmul(ga, gb, sa, sb, False), dft).astype(jnp.bfloat16)
    spec_d = forward_dft(d_cols, dft)
    da, db = halves(spec_d)
    d_mixed_cols = inverse_dft(cmul(ga, gb, da, db, True), dft).astype(jnp.bfloat16)
    both_rows = all_to_all_seq(jnp.stack([conv_cols, d_mixed_cols]), 2, 1)
    conv_rows, d_mixed = both_rows[0], both_rows[1]
    gated_rows = (query_part * conv_rows.astype(jnp.float32)).astype(jnp.bfloat16)
    weight_rows = out_proj
    gathered, sources = all_gather_cp(gated_rows)
    mixed_out = None
    for slot in range(len(sources)):
        piece = gathered[0]
        for index in range(1, len(sources)):
            piece = jnp.where(sources[index] == slot, gathered[index], piece)
        term = jnp.einsum(
            "cr,cd->rd",
            piece,
            weight_rows[slot * local_width : (slot + 1) * local_width],
            preferred_element_type=jnp.float32,
        )
        mixed_out = term if mixed_out is None else mixed_out + term
    own_rows = lax.dynamic_slice_in_dim(embedded, group_index * local_width, local_width, 0)
    block_out = (mixed_out + own_rows.T).astype(jnp.bfloat16)
    d_query = d_gated * conv_rows.astype(jnp.float32)
    cross = cmul(sa, sb, da, db, True)
    filter_grad = inverse_dft(add_conj_flip(cross), dft)
    d_key = d_mixed.astype(jnp.float32) * value_part
    d_value = d_mixed.astype(jnp.float32) * key_part
    d_proj = jnp.stack([d_query, d_key, d_value]).astype(jnp.bfloat16)
    d_full = jnp.einsum("mcr,dmc->rd", d_proj, in_proj, preferred_element_type=jnp.float32)
    stat_part = jnp.sum(d_proj.astype(jnp.float32) * unrounded, axis=(0, 1))
    onehot_rows = onehot_t.T.astype(jnp.float32)
    weights = onehot_rows * inv_rms.T
    direct = jnp.einsum("rk,rd->kd", weights, d_full, precision=PRECISE)
    centred = jnp.einsum("rk,dr->kd", weights * stat_part[:, None], normed, precision=PRECISE)
    table_all = norm_gain[None, :] * direct - centred / model_width
    gain_all = jnp.einsum("rd,dr->d", d_full, normed, precision=PRECISE)
    partial = jnp.concatenate([table_all, gain_all[None, :]], axis=0)
    own_block = reduce_blocks_cp(partial, local_width)
    cot_table = jnp.einsum(
        "rk,rc->kc", onehot_rows, cotangent.astype(jnp.float32) * grad_scale, precision=PRECISE
    )
    own_block = own_block + jnp.concatenate(
        [cot_table, jnp.zeros((1, local_width), jnp.float32)], axis=0
    )
    summed, (block_out, filter_grad) = sum_over_seq(own_block, (block_out, filter_grad))
    kmer_grad = summed[: kmer_len * letter_count]
    gain_grad = summed[kmer_len * letter_count]
    return (
        block_out,
        filter_grad.reshape(long_filter.shape),
        kmer_grad.reshape(kmer_len, letter_count, local_width),
        gain_grad,
    )


def solution(mesh):
    in_specs = (
        P(("groups", "seq")),
        P(),
        P(),
        P(None, None, ("chan", "pair")),
        P(("chan", "pair"), "seq", None, None),
        P(None, ("chan", "pair")),
        P(("groups", "seq"), ("chan", "pair")),
    )
    out_specs = (
        P(("groups", "seq"), ("chan", "pair")),
        P(("groups", "chan", "pair"), "seq", None, None),
        P("groups", None, ("chan", "pair")),
        P(("groups", "chan", "pair")),
    )
    return jax.shard_map(
        per_device, mesh=mesh, in_specs=in_specs, out_specs=out_specs, check_vma=False
    )
```

```python
import math

import jax
import jax.numpy as jnp
import numpy as np
from jax import lax
from jax.sharding import PartitionSpec as P

NORM_EPSILON = 1e-05
PRECISE = lax.Precision.HIGHEST
TRANSFORM_PRECISION = lax.Precision.HIGH


def from_behind(value, axis, steps):
    count = lax.axis_size(axis)
    first, last = (max(0, -steps), min(count, count - steps))
    return lax.ppermute(value, axis, [(source, source + steps) for source in range(first, last)])


def dft_matrix(length):
    total = 2 * length
    inner_len = 32 if length % 32 == 0 else 1
    outer_len = length // inner_len
    j = lax.broadcasted_iota(jnp.int32, (1, total), 1)
    k = jnp.where(j < length, j, j - length)
    k = jnp.where(j == length, length, k)
    phase = jnp.where(j > length, 3 * total // 4, 0)
    scale = 2.0 * math.pi / total

    def angle(idx):
        idx = idx % total
        idx = jnp.where(idx >= length, idx - total, idx)
        return idx.astype(jnp.float32) * scale

    outer = lax.optimization_barrier(lax.broadcasted_iota(jnp.int32, (outer_len, 1), 0))
    inner = lax.optimization_barrier(lax.broadcasted_iota(jnp.int32, (inner_len, 1), 0))
    alpha = angle(outer * inner_len * k)
    beta = angle(inner * k + phase)
    ca, sa = jnp.cos(alpha), jnp.sin(alpha)
    cb, sb = jnp.cos(beta), jnp.sin(beta)
    table = ca[:, None, :] * cb[None, :, :] - sa[:, None, :] * sb[None, :, :]
    return lax.optimization_barrier(table.reshape(length, total))


def xor_exchange(x, axis, step):
    count = lax.axis_size(axis)
    return lax.ppermute(x, axis, [(i, i ^ step) for i in range(count)])


def all_gather_cp(x):
    chans, pairs = lax.axis_size("chan"), lax.axis_size("pair")
    y = x[None]
    sources = [lax.axis_index(("chan", "pair"))]
    for axis, size, stride in (("chan", chans, pairs), ("pair", pairs, 1)):
        step = 1
        while step < size:
            y = jnp.concatenate([y, xor_exchange(y, axis, step)], axis=0)
            sources = sources + [source ^ (step * stride) for source in sources]
            step *= 2
    return y, sources


def group_exchange(x, axes, count, offset):
    return lax.ppermute(x, axes, [(i, i ^ offset) for i in range(count)])


def reduce_blocks_cp(x, width):
    axes = ("chan", "pair")
    count = lax.axis_size("chan") * lax.axis_size("pair")
    me = lax.axis_index(axes)
    blocks = [x[:, g * width : (g + 1) * width] for g in range(count)]

    def pick(index):
        out = blocks[0]
        for g in range(1, count):
            out = jnp.where(index == g, blocks[g], out)
        return out

    total = pick(me)
    for offset in range(1, count):
        total = total + group_exchange(pick(me ^ offset), axes, count, offset)
    return total


def sum_over_seq(x, tied):
    count = lax.axis_size("seq")
    me = lax.axis_index("seq")
    if count > 4:
        step = 1
        while step < count:
            got, tied = lax.optimization_barrier((xor_exchange(x, "seq", step), tied))
            x = x + got
            step *= 2
        return x, tied
    got = [x] + [group_exchange(x, "seq", count, offset) for offset in range(1, count)]
    got, tied = lax.optimization_barrier((got, tied))
    total = None
    for source in range(count):
        piece = got[0]
        for offset in range(1, count):
            piece = jnp.where((me ^ source) == offset, got[offset], piece)
        total = piece if total is None else total + piece
    return total, tied


def all_to_all_seq(x, split_axis, concat_axis):
    count = lax.axis_size("seq")
    if count > 4:
        return lax.all_to_all(x, "seq", split_axis=split_axis, concat_axis=concat_axis, tiled=True)
    me = lax.axis_index("seq")
    width = x.shape[split_axis] // count
    blocks = [lax.slice_in_dim(x, j * width, (j + 1) * width, axis=split_axis) for j in range(count)]

    def pick(index):
        out = blocks[0]
        for j in range(1, count):
            out = jnp.where(index == j, blocks[j], out)
        return out

    got = [pick(me)] + [
        group_exchange(pick(me ^ offset), "seq", count, offset) for offset in range(1, count)
    ]
    pieces = []
    for source in range(count):
        piece = got[0]
        for offset in range(1, count):
            piece = jnp.where((me ^ source) == offset, got[offset], piece)
        pieces.append(piece)
    return jnp.concatenate(pieces, axis=concat_axis)


def forward_dft(signal, dft):
    return jnp.dot(signal.astype(jnp.float32), dft, precision=TRANSFORM_PRECISION)


def inverse_dft(spec, dft):
    length = dft.shape[0]
    total = 2 * length
    col = np.arange(total)[None, :]
    weight = np.where(col % length == 0, 1.0 / total, 2.0 / total).astype(np.float32)
    return lax.dot_general(
        spec * weight, dft, (((1,), (1,)), ((), ())), precision=TRANSFORM_PRECISION
    )


def halves(spec):
    length = spec.shape[1] // 2
    return spec[:, :length], spec[:, length:]


def first_col(shape):
    return np.arange(shape[1])[None, :] == 0


def cmul(ga, gb, xa, xb, conj_g):
    edge = first_col(ga.shape)
    sign = -1.0 if conj_g else 1.0
    ya = ga * xa - sign * (gb * xb)
    yb = ga * xb + sign * (gb * xa)
    ya = jnp.where(edge, ga * xa, ya)
    yb = jnp.where(edge, gb * xb, yb)
    return jnp.concatenate([ya, yb], axis=1)


def pair_flip(values):
    even = (np.arange(values.shape[0]) % 2 == 0)[:, None]
    up = jnp.roll(values, -1, axis=0)
    down = jnp.roll(values, 1, axis=0)
    return jnp.where(even, up, down)


def add_conj_flip(spec):
    a, b = halves(spec)
    fa, fb = halves(pair_flip(spec))
    edge = first_col(a.shape)
    return jnp.concatenate([a + fa, jnp.where(edge, b + fb, b - fb)], axis=1)


def norm_gain_local(norm_gain, group_index, local_width):
    return lax.dynamic_slice_in_dim(norm_gain, group_index * local_width, local_width, 0)


def per_device(tokens, kmer_table, norm_gain, in_proj, long_filter, out_proj, cotangent):
    row_count = tokens.shape[0]
    kmer_len, letter_count, model_width = kmer_table.shape
    local_width = in_proj.shape[2]
    length = row_count * lax.axis_size("seq")
    group_index = lax.axis_index(("chan", "pair"))
    rim_width = kmer_len - 1
    before = from_behind(tokens[row_count - rim_width :] + 1, "seq", 1) - 1
    extended = jnp.concatenate([before, tokens])
    letters = jnp.arange(letter_count, dtype=jnp.int32)
    columns = []
    for shift_back in range(kmer_len):
        window = extended[rim_width - shift_back : rim_width - shift_back + row_count]
        columns.append(window[:, None] == letters[None, :])
    onehot_t = jnp.concatenate(columns, axis=1).T.astype(jnp.bfloat16)
    embedded = jnp.einsum(
        "kad,kar->dr",
        kmer_table,
        onehot_t.reshape(kmer_len, letter_count, row_count),
        preferred_element_type=jnp.float32,
    )
    inv_rms = lax.rsqrt(jnp.mean(embedded * embedded, axis=0, keepdims=True) + NORM_EPSILON)
    normed = embedded * inv_rms
    scaled_normed = normed * norm_gain[:, None]
    hidden = scaled_normed.astype(jnp.bfloat16)
    projected = jnp.einsum("dr,dmc->mcr", hidden, in_proj, preferred_element_type=jnp.float32)
    residual = (scaled_normed - hidden.astype(jnp.float32)).astype(jnp.bfloat16)
    unrounded = projected + jnp.einsum(
        "dr,dmc->mcr", residual, in_proj, preferred_element_type=jnp.float32
    )
    query_part = projected[0]
    key_part = projected[1]
    value_part = projected[2]
    mixed_in = (key_part * value_part).astype(jnp.bfloat16)
    grad_scale = 1.0 / math.sqrt(length)
    groups = lax.axis_size("chan") * lax.axis_size("pair")
    gated_partial = jnp.einsum("rd,cd->rc", cotangent, out_proj, preferred_element_type=jnp.float32)
    d_gated = reduce_blocks_cp(gated_partial, local_width).T * grad_scale
    dft = dft_matrix(length)
    filter_rows = long_filter.reshape(long_filter.shape[2], long_filter.shape[3])
    both_filters = forward_dft(jnp.concatenate([filter_rows, pair_flip(filter_rows)], axis=0), dft)
    conj_sign = np.where(np.arange(2 * length) > length, -1.0, 1.0).astype(np.float32)[None, :]
    channels = filter_rows.shape[0]
    spec_g = both_filters[:channels] + both_filters[channels:] * conj_sign
    ga, gb = halves(spec_g)
    d_conv = (d_gated * query_part).astype(jnp.bfloat16)
    both_cols = all_to_all_seq(jnp.stack([mixed_in, d_conv]), 1, 2)
    mixed_cols, d_cols = both_cols[0], both_cols[1]
    spec_s = forward_dft(mixed_cols, dft)
    sa, sb = halves(spec_s)
    conv_cols = inverse_dft(cmul(ga, gb, sa, sb, False), dft).astype(jnp.bfloat16)
    spec_d = forward_dft(d_cols, dft)
    da, db = halves(spec_d)
    d_mixed_cols = inverse_dft(cmul(ga, gb, da, db, True), dft).astype(jnp.bfloat16)
    both_rows = all_to_all_seq(jnp.stack([conv_cols, d_mixed_cols]), 2, 1)
    conv_rows, d_mixed = both_rows[0], both_rows[1]
    gated_rows = (query_part * conv_rows.astype(jnp.float32)).astype(jnp.bfloat16)
    weight_rows = out_proj
    gathered, sources = all_gather_cp(gated_rows)
    mixed_out = None
    for slot in range(len(sources)):
        piece = gathered[0]
        for index in range(1, len(sources)):
            piece = jnp.where(sources[index] == slot, gathered[index], piece)
        term = jnp.einsum(
            "cr,cd->rd",
            piece,
            weight_rows[slot * local_width : (slot + 1) * local_width],
            preferred_element_type=jnp.float32,
        )
        mixed_out = term if mixed_out is None else mixed_out + term
    own_rows = lax.dynamic_slice_in_dim(embedded, group_index * local_width, local_width, 0)
    block_out = (mixed_out + own_rows.T).astype(jnp.bfloat16)
    d_query = d_gated * conv_rows.astype(jnp.float32)
    cross = cmul(sa, sb, da, db, True)
    filter_grad = inverse_dft(add_conj_flip(cross), dft)
    d_key = d_mixed.astype(jnp.float32) * value_part
    d_value = d_mixed.astype(jnp.float32) * key_part
    d_proj = jnp.stack([d_query, d_key, d_value]).astype(jnp.bfloat16)
    d_full = jnp.einsum("mcr,dmc->rd", d_proj, in_proj, preferred_element_type=jnp.float32)
    stat_part = jnp.sum(d_proj.astype(jnp.float32) * unrounded, axis=(0, 1))
    onehot_rows = onehot_t.T.astype(jnp.float32)
    weights = onehot_rows * inv_rms.T
    direct = jnp.einsum("rk,rd->kd", weights, d_full, precision=PRECISE)
    centred = jnp.einsum("rk,dr->kd", weights * stat_part[:, None], normed, precision=PRECISE)
    table_all = norm_gain[None, :] * direct - centred / model_width
    gain_all = jnp.einsum("rd,dr->d", d_full, normed, precision=PRECISE)
    partial = jnp.concatenate([table_all, gain_all[None, :]], axis=0)
    own_block = reduce_blocks_cp(partial, local_width)
    cot_table = jnp.einsum(
        "rk,rc->kc", onehot_rows, cotangent.astype(jnp.float32) * grad_scale, precision=PRECISE
    )
    own_block = own_block + jnp.concatenate(
        [cot_table, jnp.zeros((1, local_width), jnp.float32)], axis=0
    )
    summed, (block_out, filter_grad) = sum_over_seq(own_block, (block_out, filter_grad))
    kmer_grad = summed[: kmer_len * letter_count]
    gain_grad = summed[kmer_len * letter_count]
    return (
        block_out,
        filter_grad.reshape(long_filter.shape),
        kmer_grad.reshape(kmer_len, letter_count, local_width),
        gain_grad,
    )


def solution(mesh):
    in_specs = (
        P(("groups", "seq")),
        P(),
        P(),
        P(None, None, ("chan", "pair")),
        P(("chan", "pair"), "seq", None, None),
        P(None, ("chan", "pair")),
        P(("groups", "seq"), ("chan", "pair")),
    )
    out_specs = (
        P(("groups", "seq"), ("chan", "pair")),
        P(("groups", "chan", "pair"), "seq", None, None),
        P("groups", None, ("chan", "pair")),
        P(("groups", "chan", "pair")),
    )
    return jax.shard_map(
        per_device, mesh=mesh, in_specs=in_specs, out_specs=out_specs, check_vma=False
    )
```

```python
import math

import jax
import jax.numpy as jnp
import numpy as np
from jax import lax
from jax.sharding import PartitionSpec as P

NORM_EPSILON = 1e-05
PRECISE = lax.Precision.HIGHEST
TRANSFORM_PRECISION = lax.Precision.HIGH


def from_behind(value, axis, steps):
    count = lax.axis_size(axis)
    first, last = (max(0, -steps), min(count, count - steps))
    return lax.ppermute(value, axis, [(source, source + steps) for source in range(first, last)])


def dft_matrix(length):
    total = 2 * length
    inner_len = 32 if length % 32 == 0 else 1
    outer_len = length // inner_len
    j = lax.broadcasted_iota(jnp.int32, (1, total), 1)
    k = jnp.where(j < length, j, j - length)
    k = jnp.where(j == length, length, k)
    phase = jnp.where(j > length, 3 * total // 4, 0)
    scale = 2.0 * math.pi / total

    def angle(idx):
        idx = idx % total
        idx = jnp.where(idx >= length, idx - total, idx)
        return idx.astype(jnp.float32) * scale

    outer = lax.optimization_barrier(lax.broadcasted_iota(jnp.int32, (outer_len, 1), 0))
    inner = lax.optimization_barrier(lax.broadcasted_iota(jnp.int32, (inner_len, 1), 0))
    alpha = angle(outer * inner_len * k)
    beta = angle(inner * k + phase)
    ca, sa = jnp.cos(alpha), jnp.sin(alpha)
    cb, sb = jnp.cos(beta), jnp.sin(beta)
    table = ca[:, None, :] * cb[None, :, :] - sa[:, None, :] * sb[None, :, :]
    return lax.optimization_barrier(table.reshape(length, total))


def xor_exchange(x, axis, step):
    count = lax.axis_size(axis)
    return lax.ppermute(x, axis, [(i, i ^ step) for i in range(count)])


def all_gather_cp(x):
    chans, pairs = lax.axis_size("chan"), lax.axis_size("pair")
    y = x[None]
    sources = [lax.axis_index(("chan", "pair"))]
    for axis, size, stride in (("chan", chans, pairs), ("pair", pairs, 1)):
        step = 1
        while step < size:
            y = jnp.concatenate([y, xor_exchange(y, axis, step)], axis=0)
            sources = sources + [source ^ (step * stride) for source in sources]
            step *= 2
    return y, sources


def group_exchange(x, axes, count, offset):
    return lax.ppermute(x, axes, [(i, i ^ offset) for i in range(count)])


def reduce_blocks_cp(x, width):
    axes = ("chan", "pair")
    count = lax.axis_size("chan") * lax.axis_size("pair")
    me = lax.axis_index(axes)
    blocks = [x[:, g * width : (g + 1) * width] for g in range(count)]

    def pick(index):
        out = blocks[0]
        for g in range(1, count):
            out = jnp.where(index == g, blocks[g], out)
        return out

    total = pick(me)
    for offset in range(1, count):
        total = total + group_exchange(pick(me ^ offset), axes, count, offset)
    return total


def sum_over_seq(x, tied):
    count = lax.axis_size("seq")
    me = lax.axis_index("seq")
    if count > 4:
        step = 1
        while step < count:
            got, tied = lax.optimization_barrier((xor_exchange(x, "seq", step), tied))
            x = x + got
            step *= 2
        return x, tied
    got = [x] + [group_exchange(x, "seq", count, offset) for offset in range(1, count)]
    got, tied = lax.optimization_barrier((got, tied))
    total = None
    for source in range(count):
        piece = got[0]
        for offset in range(1, count):
            piece = jnp.where((me ^ source) == offset, got[offset], piece)
        total = piece if total is None else total + piece
    return total, tied


def all_to_all_seq(x, split_axis, concat_axis):
    count = lax.axis_size("seq")
    if count > 4:
        return lax.all_to_all(x, "seq", split_axis=split_axis, concat_axis=concat_axis, tiled=True)
    me = lax.axis_index("seq")
    width = x.shape[split_axis] // count
    blocks = [lax.slice_in_dim(x, j * width, (j + 1) * width, axis=split_axis) for j in range(count)]

    def pick(index):
        out = blocks[0]
        for j in range(1, count):
            out = jnp.where(index == j, blocks[j], out)
        return out

    got = [pick(me)] + [
        group_exchange(pick(me ^ offset), "seq", count, offset) for offset in range(1, count)
    ]
    pieces = []
    for source in range(count):
        piece = got[0]
        for offset in range(1, count):
            piece = jnp.where((me ^ source) == offset, got[offset], piece)
        pieces.append(piece)
    return jnp.concatenate(pieces, axis=concat_axis)


def forward_dft(signal, dft):
    return jnp.dot(signal.astype(jnp.float32), dft, precision=TRANSFORM_PRECISION)


def inverse_dft(spec, dft):
    length = dft.shape[0]
    total = 2 * length
    col = np.arange(total)[None, :]
    weight = np.where(col % length == 0, 1.0 / total, 2.0 / total).astype(np.float32)
    return lax.dot_general(
        spec * weight, dft, (((1,), (1,)), ((), ())), precision=TRANSFORM_PRECISION
    )


def halves(spec):
    length = spec.shape[1] // 2
    return spec[:, :length], spec[:, length:]


def first_col(shape):
    return np.arange(shape[1])[None, :] == 0


def cmul(ga, gb, xa, xb, conj_g):
    edge = first_col(ga.shape)
    sign = -1.0 if conj_g else 1.0
    ya = ga * xa - sign * (gb * xb)
    yb = ga * xb + sign * (gb * xa)
    ya = jnp.where(edge, ga * xa, ya)
    yb = jnp.where(edge, gb * xb, yb)
    return jnp.concatenate([ya, yb], axis=1)


def pair_flip(values):
    even = (np.arange(values.shape[0]) % 2 == 0)[:, None]
    up = jnp.roll(values, -1, axis=0)
    down = jnp.roll(values, 1, axis=0)
    return jnp.where(even, up, down)


def add_conj_flip(spec):
    a, b = halves(spec)
    fa, fb = halves(pair_flip(spec))
    edge = first_col(a.shape)
    return jnp.concatenate([a + fa, jnp.where(edge, b + fb, b - fb)], axis=1)


def norm_gain_local(norm_gain, group_index, local_width):
    return lax.dynamic_slice_in_dim(norm_gain, group_index * local_width, local_width, 0)


def per_device(tokens, kmer_table, norm_gain, in_proj, long_filter, out_proj, cotangent):
    row_count = tokens.shape[0]
    kmer_len, letter_count, model_width = kmer_table.shape
    local_width = in_proj.shape[2]
    length = row_count * lax.axis_size("seq")
    group_index = lax.axis_index(("chan", "pair"))
    rim_width = kmer_len - 1
    before = from_behind(tokens[row_count - rim_width :] + 1, "seq", 1) - 1
    extended = jnp.concatenate([before, tokens])
    letters = jnp.arange(letter_count, dtype=jnp.int32)
    columns = []
    for shift_back in range(kmer_len):
        window = extended[rim_width - shift_back : rim_width - shift_back + row_count]
        columns.append(window[:, None] == letters[None, :])
    onehot_t = jnp.concatenate(columns, axis=1).T.astype(jnp.bfloat16)
    table_t = kmer_table.reshape(kmer_len * letter_count, model_width).T
    embedded = jnp.dot(table_t, onehot_t, preferred_element_type=jnp.float32)
    inv_rms = lax.rsqrt(jnp.mean(embedded * embedded, axis=0, keepdims=True) + NORM_EPSILON)
    normed = embedded * inv_rms
    scaled_normed = normed * norm_gain[:, None]
    hidden = scaled_normed.astype(jnp.bfloat16)
    projected = jnp.einsum("dr,dmc->mcr", hidden, in_proj, preferred_element_type=jnp.float32)
    residual = (scaled_normed - hidden.astype(jnp.float32)).astype(jnp.bfloat16)
    unrounded = projected + jnp.einsum(
        "dr,dmc->mcr", residual, in_proj, preferred_element_type=jnp.float32
    )
    query_part = projected[0]
    key_part = projected[1]
    value_part = projected[2]
    mixed_in = (key_part * value_part).astype(jnp.bfloat16)
    grad_scale = 1.0 / math.sqrt(length)
    groups = lax.axis_size("chan") * lax.axis_size("pair")
    gated_partial = jnp.einsum("rd,cd->rc", cotangent, out_proj, preferred_element_type=jnp.float32)
    d_gated = reduce_blocks_cp(gated_partial, local_width).T * grad_scale
    dft = dft_matrix(length)
    filter_rows = long_filter.reshape(long_filter.shape[2], long_filter.shape[3])
    spec_g = add_conj_flip(forward_dft(filter_rows, dft))
    d_conv = (d_gated * query_part).astype(jnp.bfloat16)
    both_cols = all_to_all_seq(jnp.stack([mixed_in, d_conv]), 1, 2)
    both_cols, (spec_g, dft, unrounded) = lax.optimization_barrier(
        (both_cols, (spec_g, dft, unrounded))
    )
    mixed_cols, d_cols = both_cols[0], both_cols[1]
    ga, gb = halves(spec_g)
    spec_s = forward_dft(mixed_cols, dft)
    sa, sb = halves(spec_s)
    conv_cols = inverse_dft(cmul(ga, gb, sa, sb, False), dft).astype(jnp.bfloat16)
    spec_d = forward_dft(d_cols, dft)
    da, db = halves(spec_d)
    d_mixed_cols = inverse_dft(cmul(ga, gb, da, db, True), dft).astype(jnp.bfloat16)
    both_rows = all_to_all_seq(jnp.stack([conv_cols, d_mixed_cols]), 2, 1)
    conv_rows, d_mixed = both_rows[0], both_rows[1]
    gated_rows = (query_part * conv_rows.astype(jnp.float32)).astype(jnp.bfloat16)
    weight_rows = out_proj
    gathered, sources = all_gather_cp(gated_rows)
    mixed_out = None
    for slot in range(len(sources)):
        piece = gathered[0]
        for index in range(1, len(sources)):
            piece = jnp.where(sources[index] == slot, gathered[index], piece)
        term = jnp.einsum(
            "cr,cd->rd",
            piece,
            weight_rows[slot * local_width : (slot + 1) * local_width],
            preferred_element_type=jnp.float32,
        )
        mixed_out = term if mixed_out is None else mixed_out + term
    own_rows = lax.dynamic_slice_in_dim(embedded, group_index * local_width, local_width, 0)
    block_out = (mixed_out + own_rows.T).astype(jnp.bfloat16)
    d_query = d_gated * conv_rows.astype(jnp.float32)
    cross = cmul(sa, sb, da, db, True)
    filter_grad = inverse_dft(add_conj_flip(cross), dft)
    d_key = d_mixed.astype(jnp.float32) * value_part
    d_value = d_mixed.astype(jnp.float32) * key_part
    d_proj = jnp.stack([d_query, d_key, d_value]).astype(jnp.bfloat16)
    d_full = jnp.einsum("mcr,dmc->rd", d_proj, in_proj, preferred_element_type=jnp.float32)
    stat_part = jnp.sum(d_proj.astype(jnp.float32) * unrounded, axis=(0, 1))
    onehot_rows = onehot_t.T.astype(jnp.float32)
    weights = onehot_rows * inv_rms.T
    direct = jnp.einsum("rk,rd->kd", weights, d_full, precision=PRECISE)
    centred = jnp.einsum("rk,dr->kd", weights * stat_part[:, None], normed, precision=PRECISE)
    table_all = norm_gain[None, :] * direct - centred / model_width
    gain_all = jnp.einsum("rd,dr->d", d_full, normed, precision=PRECISE)
    partial = jnp.concatenate([table_all, gain_all[None, :]], axis=0)
    own_block = reduce_blocks_cp(partial, local_width)
    cot_table = jnp.einsum(
        "rk,rc->kc", onehot_rows, cotangent.astype(jnp.float32) * grad_scale, precision=PRECISE
    )
    own_block = own_block + jnp.concatenate(
        [cot_table, jnp.zeros((1, local_width), jnp.float32)], axis=0
    )
    summed, (block_out, filter_grad) = sum_over_seq(own_block, (block_out, filter_grad))
    kmer_grad = summed[: kmer_len * letter_count]
    gain_grad = summed[kmer_len * letter_count]
    return (
        block_out,
        filter_grad.reshape(long_filter.shape),
        kmer_grad.reshape(kmer_len, letter_count, local_width),
        gain_grad,
    )


def solution(mesh):
    in_specs = (
        P(("groups", "seq")),
        P(),
        P(),
        P(None, None, ("chan", "pair")),
        P(("chan", "pair"), "seq", None, None),
        P(None, ("chan", "pair")),
        P(("groups", "seq"), ("chan", "pair")),
    )
    out_specs = (
        P(("groups", "seq"), ("chan", "pair")),
        P(("groups", "chan", "pair"), "seq", None, None),
        P("groups", None, ("chan", "pair")),
        P(("groups", "chan", "pair")),
    )
    return jax.shard_map(
        per_device, mesh=mesh, in_specs=in_specs, out_specs=out_specs, check_vma=False
    )
```

```python
import math

import jax
import jax.numpy as jnp
import numpy as np
from jax import lax
from jax.sharding import PartitionSpec as P

NORM_EPSILON = 1e-05
PRECISE = lax.Precision.HIGHEST
TRANSFORM_PRECISION = lax.Precision.HIGH


def from_behind(value, axis, steps):
    count = lax.axis_size(axis)
    first, last = (max(0, -steps), min(count, count - steps))
    return lax.ppermute(value, axis, [(source, source + steps) for source in range(first, last)])


def dft_matrix(length):
    total = 2 * length
    inner_len = 32 if length % 32 == 0 else 1
    outer_len = length // inner_len
    j = lax.broadcasted_iota(jnp.int32, (1, total), 1)
    k = jnp.where(j < length, j, j - length)
    k = jnp.where(j == length, length, k)
    phase = jnp.where(j > length, 3 * total // 4, 0)
    scale = 2.0 * math.pi / total

    def angle(idx):
        idx = idx % total
        idx = jnp.where(idx >= length, idx - total, idx)
        return idx.astype(jnp.float32) * scale

    outer = lax.optimization_barrier(lax.broadcasted_iota(jnp.int32, (outer_len, 1), 0))
    inner = lax.optimization_barrier(lax.broadcasted_iota(jnp.int32, (inner_len, 1), 0))
    alpha = angle(outer * inner_len * k)
    beta = angle(inner * k + phase)
    ca, sa = jnp.cos(alpha), jnp.sin(alpha)
    cb, sb = jnp.cos(beta), jnp.sin(beta)
    table = ca[:, None, :] * cb[None, :, :] - sa[:, None, :] * sb[None, :, :]
    return lax.optimization_barrier(table.reshape(length, total))


def xor_exchange(x, axis, step):
    count = lax.axis_size(axis)
    return lax.ppermute(x, axis, [(i, i ^ step) for i in range(count)])


def all_gather_cp(x):
    chans, pairs = lax.axis_size("chan"), lax.axis_size("pair")
    y = x[None]
    sources = [lax.axis_index(("chan", "pair"))]
    for axis, size, stride in (("chan", chans, pairs), ("pair", pairs, 1)):
        step = 1
        while step < size:
            y = jnp.concatenate([y, xor_exchange(y, axis, step)], axis=0)
            sources = sources + [source ^ (step * stride) for source in sources]
            step *= 2
    return y, sources


def group_exchange(x, axes, count, offset):
    return lax.ppermute(x, axes, [(i, i ^ offset) for i in range(count)])


def reduce_blocks_cp(x, width):
    axes = ("chan", "pair")
    count = lax.axis_size("chan") * lax.axis_size("pair")
    me = lax.axis_index(axes)
    blocks = [x[:, g * width : (g + 1) * width] for g in range(count)]

    def pick(index):
        out = blocks[0]
        for g in range(1, count):
            out = jnp.where(index == g, blocks[g], out)
        return out

    total = pick(me)
    for offset in range(1, count):
        total = total + group_exchange(pick(me ^ offset), axes, count, offset)
    return total


def sum_over_seq(x, tied):
    count = lax.axis_size("seq")
    me = lax.axis_index("seq")
    if count > 4:
        step = 1
        while step < count:
            got, tied = lax.optimization_barrier((xor_exchange(x, "seq", step), tied))
            x = x + got
            step *= 2
        return x, tied
    got = [x] + [group_exchange(x, "seq", count, offset) for offset in range(1, count)]
    got, tied = lax.optimization_barrier((got, tied))
    total = None
    for source in range(count):
        piece = got[0]
        for offset in range(1, count):
            piece = jnp.where((me ^ source) == offset, got[offset], piece)
        total = piece if total is None else total + piece
    return total, tied


def all_to_all_seq(x, split_axis, concat_axis):
    count = lax.axis_size("seq")
    if count > 4:
        return lax.all_to_all(x, "seq", split_axis=split_axis, concat_axis=concat_axis, tiled=True)
    me = lax.axis_index("seq")
    width = x.shape[split_axis] // count
    blocks = [lax.slice_in_dim(x, j * width, (j + 1) * width, axis=split_axis) for j in range(count)]

    def pick(index):
        out = blocks[0]
        for j in range(1, count):
            out = jnp.where(index == j, blocks[j], out)
        return out

    got = [pick(me)] + [
        group_exchange(pick(me ^ offset), "seq", count, offset) for offset in range(1, count)
    ]
    pieces = []
    for source in range(count):
        piece = got[0]
        for offset in range(1, count):
            piece = jnp.where((me ^ source) == offset, got[offset], piece)
        pieces.append(piece)
    return jnp.concatenate(pieces, axis=concat_axis)


def forward_dft(signal, dft):
    return jnp.dot(signal.astype(jnp.float32), dft, precision=TRANSFORM_PRECISION)


def inverse_dft(spec, dft):
    length = dft.shape[0]
    total = 2 * length
    col = np.arange(total)[None, :]
    weight = np.where(col % length == 0, 1.0 / total, 2.0 / total).astype(np.float32)
    return lax.dot_general(
        spec * weight, dft, (((1,), (1,)), ((), ())), precision=TRANSFORM_PRECISION
    )


def halves(spec):
    length = spec.shape[1] // 2
    return spec[:, :length], spec[:, length:]


def first_col(shape):
    return np.arange(shape[1])[None, :] == 0


def cmul(ga, gb, xa, xb, conj_g):
    edge = first_col(ga.shape)
    sign = -1.0 if conj_g else 1.0
    ya = ga * xa - sign * (gb * xb)
    yb = ga * xb + sign * (gb * xa)
    ya = jnp.where(edge, ga * xa, ya)
    yb = jnp.where(edge, gb * xb, yb)
    return jnp.concatenate([ya, yb], axis=1)


def pair_flip(values):
    even = (np.arange(values.shape[0]) % 2 == 0)[:, None]
    up = jnp.roll(values, -1, axis=0)
    down = jnp.roll(values, 1, axis=0)
    return jnp.where(even, up, down)


def add_conj_flip(spec):
    a, b = halves(spec)
    fa, fb = halves(pair_flip(spec))
    edge = first_col(a.shape)
    return jnp.concatenate([a + fa, jnp.where(edge, b + fb, b - fb)], axis=1)


def norm_gain_local(norm_gain, group_index, local_width):
    return lax.dynamic_slice_in_dim(norm_gain, group_index * local_width, local_width, 0)


def per_device(tokens, kmer_table, norm_gain, in_proj, long_filter, out_proj, cotangent):
    row_count = tokens.shape[0]
    kmer_len, letter_count, model_width = kmer_table.shape
    local_width = in_proj.shape[2]
    length = row_count * lax.axis_size("seq")
    group_index = lax.axis_index(("chan", "pair"))
    rim_width = kmer_len - 1
    seq_count = lax.axis_size("seq")
    before = lax.ppermute(
        tokens[row_count - rim_width :], "seq", [(i, (i + 1) % seq_count) for i in range(seq_count)]
    )
    before = jnp.where(lax.axis_index("seq") == 0, -1, before)
    extended = jnp.concatenate([before, tokens])
    letters = jnp.arange(letter_count, dtype=jnp.int32)
    columns = []
    for shift_back in range(kmer_len):
        window = extended[rim_width - shift_back : rim_width - shift_back + row_count]
        columns.append(window[:, None] == letters[None, :])
    onehot_t = jnp.concatenate(columns, axis=1).T.astype(jnp.bfloat16)
    table_t = kmer_table.reshape(kmer_len * letter_count, model_width).T
    embedded = jnp.dot(table_t, onehot_t, preferred_element_type=jnp.float32)
    inv_rms = lax.rsqrt(jnp.mean(embedded * embedded, axis=0, keepdims=True) + NORM_EPSILON)
    normed = embedded * inv_rms
    scaled_normed = normed * norm_gain[:, None]
    hidden = scaled_normed.astype(jnp.bfloat16)
    projected = jnp.einsum("dr,dmc->mcr", hidden, in_proj, preferred_element_type=jnp.float32)
    residual = (scaled_normed - hidden.astype(jnp.float32)).astype(jnp.bfloat16)
    unrounded = projected + jnp.einsum(
        "dr,dmc->mcr", residual, in_proj, preferred_element_type=jnp.float32
    )
    query_part = projected[0]
    key_part = projected[1]
    value_part = projected[2]
    mixed_in = (key_part * value_part).astype(jnp.bfloat16)
    grad_scale = 1.0 / math.sqrt(length)
    groups = lax.axis_size("chan") * lax.axis_size("pair")
    gated_partial = jnp.einsum("rd,cd->rc", cotangent, out_proj, preferred_element_type=jnp.float32)
    d_gated = reduce_blocks_cp(gated_partial, local_width).T * grad_scale
    dft = dft_matrix(length)
    filter_rows = long_filter.reshape(long_filter.shape[2], long_filter.shape[3])
    spec_g = add_conj_flip(forward_dft(filter_rows, dft))
    d_conv = (d_gated * query_part).astype(jnp.bfloat16)
    both_cols = all_to_all_seq(jnp.stack([mixed_in, d_conv]), 1, 2)
    both_cols, (spec_g, dft, unrounded) = lax.optimization_barrier(
        (both_cols, (spec_g, dft, unrounded))
    )
    mixed_cols, d_cols = both_cols[0], both_cols[1]
    ga, gb = halves(spec_g)
    spec_s = forward_dft(mixed_cols, dft)
    sa, sb = halves(spec_s)
    conv_cols = inverse_dft(cmul(ga, gb, sa, sb, False), dft).astype(jnp.bfloat16)
    spec_d = forward_dft(d_cols, dft)
    da, db = halves(spec_d)
    d_mixed_cols = inverse_dft(cmul(ga, gb, da, db, True), dft).astype(jnp.bfloat16)
    both_rows = all_to_all_seq(jnp.stack([conv_cols, d_mixed_cols]), 2, 1)
    conv_rows, d_mixed = both_rows[0], both_rows[1]
    gated_rows = (query_part * conv_rows.astype(jnp.float32)).astype(jnp.bfloat16)
    weight_rows = out_proj
    gathered, sources = all_gather_cp(gated_rows)
    mixed_out = None
    for slot in range(len(sources)):
        piece = gathered[0]
        for index in range(1, len(sources)):
            piece = jnp.where(sources[index] == slot, gathered[index], piece)
        term = jnp.einsum(
            "cr,cd->rd",
            piece,
            weight_rows[slot * local_width : (slot + 1) * local_width],
            preferred_element_type=jnp.float32,
        )
        mixed_out = term if mixed_out is None else mixed_out + term
    own_rows = lax.dynamic_slice_in_dim(embedded, group_index * local_width, local_width, 0)
    block_out = (mixed_out + own_rows.T).astype(jnp.bfloat16)
    d_query = d_gated * conv_rows.astype(jnp.float32)
    cross = cmul(sa, sb, da, db, True)
    filter_grad = inverse_dft(add_conj_flip(cross), dft)
    d_key = d_mixed.astype(jnp.float32) * value_part
    d_value = d_mixed.astype(jnp.float32) * key_part
    d_proj = jnp.stack([d_query, d_key, d_value]).astype(jnp.bfloat16)
    d_full = jnp.einsum("mcr,dmc->rd", d_proj, in_proj, preferred_element_type=jnp.float32)
    stat_part = jnp.sum(d_proj.astype(jnp.float32) * unrounded, axis=(0, 1))
    onehot_rows = onehot_t.T.astype(jnp.float32)
    weights = onehot_rows * inv_rms.T
    direct = jnp.einsum("rk,rd->kd", weights, d_full, precision=PRECISE)
    centred = jnp.einsum("rk,dr->kd", weights * stat_part[:, None], normed, precision=PRECISE)
    table_all = norm_gain[None, :] * direct - centred / model_width
    gain_all = jnp.einsum("rd,dr->d", d_full, normed, precision=PRECISE)
    partial = jnp.concatenate([table_all, gain_all[None, :]], axis=0)
    own_block = reduce_blocks_cp(partial, local_width)
    cot_table = jnp.einsum(
        "rk,rc->kc", onehot_rows, cotangent.astype(jnp.float32) * grad_scale, precision=PRECISE
    )
    own_block = own_block + jnp.concatenate(
        [cot_table, jnp.zeros((1, local_width), jnp.float32)], axis=0
    )
    summed, (block_out, filter_grad) = sum_over_seq(own_block, (block_out, filter_grad))
    kmer_grad = summed[: kmer_len * letter_count]
    gain_grad = summed[kmer_len * letter_count]
    return (
        block_out,
        filter_grad.reshape(long_filter.shape),
        kmer_grad.reshape(kmer_len, letter_count, local_width),
        gain_grad,
    )


def solution(mesh):
    in_specs = (
        P(("groups", "seq")),
        P(),
        P(),
        P(None, None, ("chan", "pair")),
        P(("chan", "pair"), "seq", None, None),
        P(None, ("chan", "pair")),
        P(("groups", "seq"), ("chan", "pair")),
    )
    out_specs = (
        P(("groups", "seq"), ("chan", "pair")),
        P(("groups", "chan", "pair"), "seq", None, None),
        P("groups", None, ("chan", "pair")),
        P(("groups", "chan", "pair")),
    )
    return jax.shard_map(
        per_device, mesh=mesh, in_specs=in_specs, out_specs=out_specs, check_vma=False
    )
```

```python
import math

import jax
import jax.numpy as jnp
import numpy as np
from jax import lax
from jax.sharding import PartitionSpec as P

NORM_EPSILON = 1e-05
PRECISE = lax.Precision.HIGHEST
TRANSFORM_PRECISION = lax.Precision.HIGH


def from_behind(value, axis, steps):
    count = lax.axis_size(axis)
    first, last = (max(0, -steps), min(count, count - steps))
    return lax.ppermute(value, axis, [(source, source + steps) for source in range(first, last)])


def dft_matrix(length):
    total = 2 * length
    inner_len = 32 if length % 32 == 0 else 1
    outer_len = length // inner_len
    j = lax.broadcasted_iota(jnp.int32, (1, total), 1)
    k = jnp.where(j < length, j, j - length)
    k = jnp.where(j == length, length, k)
    phase = jnp.where(j > length, 3 * total // 4, 0)
    scale = 2.0 * math.pi / total

    def angle(idx):
        idx = idx % total
        idx = jnp.where(idx >= length, idx - total, idx)
        return idx.astype(jnp.float32) * scale

    outer = lax.optimization_barrier(lax.broadcasted_iota(jnp.int32, (outer_len, 1), 0))
    inner = lax.optimization_barrier(lax.broadcasted_iota(jnp.int32, (inner_len, 1), 0))
    alpha = angle(outer * inner_len * k)
    beta = angle(inner * k + phase)
    ca, sa = jnp.cos(alpha), jnp.sin(alpha)
    cb, sb = jnp.cos(beta), jnp.sin(beta)
    table = ca[:, None, :] * cb[None, :, :] - sa[:, None, :] * sb[None, :, :]
    return lax.optimization_barrier(table.reshape(length, total))


def xor_exchange(x, axis, step):
    count = lax.axis_size(axis)
    return lax.ppermute(x, axis, [(i, i ^ step) for i in range(count)])


def all_gather_cp(x):
    chans, pairs = lax.axis_size("chan"), lax.axis_size("pair")
    y = x[None]
    sources = [lax.axis_index(("chan", "pair"))]
    for axis, size, stride in (("chan", chans, pairs), ("pair", pairs, 1)):
        step = 1
        while step < size:
            y = jnp.concatenate([y, xor_exchange(y, axis, step)], axis=0)
            sources = sources + [source ^ (step * stride) for source in sources]
            step *= 2
    return y, sources


def group_exchange(x, axes, count, offset):
    return lax.ppermute(x, axes, [(i, i ^ offset) for i in range(count)])


def reduce_blocks_cp(x, width):
    axes = ("chan", "pair")
    count = lax.axis_size("chan") * lax.axis_size("pair")
    me = lax.axis_index(axes)
    blocks = [x[:, g * width : (g + 1) * width] for g in range(count)]

    def pick(index):
        out = blocks[0]
        for g in range(1, count):
            out = jnp.where(index == g, blocks[g], out)
        return out

    total = pick(me)
    for offset in range(1, count):
        total = total + group_exchange(pick(me ^ offset), axes, count, offset)
    return total


def sum_over_seq(x, tied):
    count = lax.axis_size("seq")
    me = lax.axis_index("seq")
    if count > 4:
        step = 1
        while step < count:
            got, tied = lax.optimization_barrier((xor_exchange(x, "seq", step), tied))
            x = x + got
            step *= 2
        return x, tied
    sent = {offset: group_exchange(x, "seq", count, offset) for offset in range(count - 1, 0, -1)}
    got = [x] + [sent[offset] for offset in range(1, count)]
    got, tied = lax.optimization_barrier((got, tied))
    total = None
    for source in range(count):
        piece = got[0]
        for offset in range(1, count):
            piece = jnp.where((me ^ source) == offset, got[offset], piece)
        total = piece if total is None else total + piece
    return total, tied


def all_to_all_seq(x, split_axis, concat_axis):
    count = lax.axis_size("seq")
    if count > 4:
        return lax.all_to_all(x, "seq", split_axis=split_axis, concat_axis=concat_axis, tiled=True)
    me = lax.axis_index("seq")
    width = x.shape[split_axis] // count
    blocks = [lax.slice_in_dim(x, j * width, (j + 1) * width, axis=split_axis) for j in range(count)]

    def pick(index):
        out = blocks[0]
        for j in range(1, count):
            out = jnp.where(index == j, blocks[j], out)
        return out

    sent = {
        offset: group_exchange(pick(me ^ offset), "seq", count, offset)
        for offset in range(count - 1, 0, -1)
    }
    got = [pick(me)] + [sent[offset] for offset in range(1, count)]
    pieces = []
    for source in range(count):
        piece = got[0]
        for offset in range(1, count):
            piece = jnp.where((me ^ source) == offset, got[offset], piece)
        pieces.append(piece)
    return jnp.concatenate(pieces, axis=concat_axis)


def forward_dft(signal, dft):
    return jnp.dot(signal.astype(jnp.float32), dft, precision=TRANSFORM_PRECISION)


def inverse_dft(spec, dft):
    length = dft.shape[0]
    total = 2 * length
    col = np.arange(total)[None, :]
    weight = np.where(col % length == 0, 1.0 / total, 2.0 / total).astype(np.float32)
    return lax.dot_general(
        spec * weight, dft, (((1,), (1,)), ((), ())), precision=TRANSFORM_PRECISION
    )


def halves(spec):
    length = spec.shape[1] // 2
    return spec[:, :length], spec[:, length:]


def first_col(shape):
    return np.arange(shape[1])[None, :] == 0


def cmul(ga, gb, xa, xb, conj_g):
    edge = first_col(ga.shape)
    sign = -1.0 if conj_g else 1.0
    ya = ga * xa - sign * (gb * xb)
    yb = ga * xb + sign * (gb * xa)
    ya = jnp.where(edge, ga * xa, ya)
    yb = jnp.where(edge, gb * xb, yb)
    return jnp.concatenate([ya, yb], axis=1)


def pair_flip(values):
    even = (np.arange(values.shape[0]) % 2 == 0)[:, None]
    up = jnp.roll(values, -1, axis=0)
    down = jnp.roll(values, 1, axis=0)
    return jnp.where(even, up, down)


def add_conj_flip(spec):
    a, b = halves(spec)
    fa, fb = halves(pair_flip(spec))
    edge = first_col(a.shape)
    return jnp.concatenate([a + fa, jnp.where(edge, b + fb, b - fb)], axis=1)


def norm_gain_local(norm_gain, group_index, local_width):
    return lax.dynamic_slice_in_dim(norm_gain, group_index * local_width, local_width, 0)


def per_device(tokens, kmer_table, norm_gain, in_proj, long_filter, out_proj, cotangent):
    row_count = tokens.shape[0]
    kmer_len, letter_count, model_width = kmer_table.shape
    local_width = in_proj.shape[2]
    length = row_count * lax.axis_size("seq")
    group_index = lax.axis_index(("chan", "pair"))
    rim_width = kmer_len - 1
    seq_count = lax.axis_size("seq")
    before = lax.ppermute(
        tokens[row_count - rim_width :], "seq", [(i, (i + 1) % seq_count) for i in range(seq_count)]
    )
    before = jnp.where(lax.axis_index("seq") == 0, -1, before)
    extended = jnp.concatenate([before, tokens])
    letters = jnp.arange(letter_count, dtype=jnp.int32)
    columns = []
    for shift_back in range(kmer_len):
        window = extended[rim_width - shift_back : rim_width - shift_back + row_count]
        columns.append(window[:, None] == letters[None, :])
    onehot_t = jnp.concatenate(columns, axis=1).T.astype(jnp.bfloat16)
    table_t = kmer_table.reshape(kmer_len * letter_count, model_width).T
    embedded = jnp.dot(table_t, onehot_t, preferred_element_type=jnp.float32)
    inv_rms = lax.rsqrt(jnp.mean(embedded * embedded, axis=0, keepdims=True) + NORM_EPSILON)
    normed = embedded * inv_rms
    scaled_normed = normed * norm_gain[:, None]
    hidden = scaled_normed.astype(jnp.bfloat16)
    projected = jnp.einsum("dr,dmc->mcr", hidden, in_proj, preferred_element_type=jnp.float32)
    residual = (scaled_normed - hidden.astype(jnp.float32)).astype(jnp.bfloat16)
    unrounded = projected + jnp.einsum(
        "dr,dmc->mcr", residual, in_proj, preferred_element_type=jnp.float32
    )
    query_part = projected[0]
    key_part = projected[1]
    value_part = projected[2]
    mixed_in = (key_part * value_part).astype(jnp.bfloat16)
    grad_scale = 1.0 / math.sqrt(length)
    groups = lax.axis_size("chan") * lax.axis_size("pair")
    gated_partial = jnp.einsum("rd,cd->rc", cotangent, out_proj, preferred_element_type=jnp.float32)
    d_gated = reduce_blocks_cp(gated_partial, local_width).T * grad_scale
    dft = dft_matrix(length)
    filter_rows = long_filter.reshape(long_filter.shape[2], long_filter.shape[3])
    spec_g = add_conj_flip(forward_dft(filter_rows, dft))
    d_conv = (d_gated * query_part).astype(jnp.bfloat16)
    both_cols = all_to_all_seq(jnp.stack([mixed_in, d_conv]), 1, 2)
    both_cols, (spec_g, dft, unrounded) = lax.optimization_barrier(
        (both_cols, (spec_g, dft, unrounded))
    )
    mixed_cols, d_cols = both_cols[0], both_cols[1]
    ga, gb = halves(spec_g)
    spec_s = forward_dft(mixed_cols, dft)
    sa, sb = halves(spec_s)
    conv_cols = inverse_dft(cmul(ga, gb, sa, sb, False), dft).astype(jnp.bfloat16)
    spec_d = forward_dft(d_cols, dft)
    da, db = halves(spec_d)
    d_mixed_cols = inverse_dft(cmul(ga, gb, da, db, True), dft).astype(jnp.bfloat16)
    both_rows = all_to_all_seq(jnp.stack([conv_cols, d_mixed_cols]), 2, 1)
    conv_rows, d_mixed = both_rows[0], both_rows[1]
    gated_rows = (query_part * conv_rows.astype(jnp.float32)).astype(jnp.bfloat16)
    weight_rows = out_proj
    gathered, sources = all_gather_cp(gated_rows)
    mixed_out = None
    for slot in range(len(sources)):
        piece = gathered[0]
        for index in range(1, len(sources)):
            piece = jnp.where(sources[index] == slot, gathered[index], piece)
        term = jnp.einsum(
            "cr,cd->rd",
            piece,
            weight_rows[slot * local_width : (slot + 1) * local_width],
            preferred_element_type=jnp.float32,
        )
        mixed_out = term if mixed_out is None else mixed_out + term
    own_rows = lax.dynamic_slice_in_dim(embedded, group_index * local_width, local_width, 0)
    block_out = (mixed_out + own_rows.T).astype(jnp.bfloat16)
    d_query = d_gated * conv_rows.astype(jnp.float32)
    cross = cmul(sa, sb, da, db, True)
    filter_grad = inverse_dft(add_conj_flip(cross), dft)
    d_key = d_mixed.astype(jnp.float32) * value_part
    d_value = d_mixed.astype(jnp.float32) * key_part
    d_proj = jnp.stack([d_query, d_key, d_value]).astype(jnp.bfloat16)
    d_full = jnp.einsum("mcr,dmc->rd", d_proj, in_proj, preferred_element_type=jnp.float32)
    stat_part = jnp.sum(d_proj.astype(jnp.float32) * unrounded, axis=(0, 1))
    onehot_rows = onehot_t.T.astype(jnp.float32)
    weights = onehot_rows * inv_rms.T
    direct = jnp.einsum("rk,rd->kd", weights, d_full, precision=PRECISE)
    centred = jnp.einsum("rk,dr->kd", weights * stat_part[:, None], normed, precision=PRECISE)
    table_all = norm_gain[None, :] * direct - centred / model_width
    gain_all = jnp.einsum("rd,dr->d", d_full, normed, precision=PRECISE)
    partial = jnp.concatenate([table_all, gain_all[None, :]], axis=0)
    own_block = reduce_blocks_cp(partial, local_width)
    cot_table = jnp.einsum(
        "rk,rc->kc", onehot_rows, cotangent.astype(jnp.float32) * grad_scale, precision=PRECISE
    )
    own_block = own_block + jnp.concatenate(
        [cot_table, jnp.zeros((1, local_width), jnp.float32)], axis=0
    )
    summed, (block_out, filter_grad) = sum_over_seq(own_block, (block_out, filter_grad))
    kmer_grad = summed[: kmer_len * letter_count]
    gain_grad = summed[kmer_len * letter_count]
    return (
        block_out,
        filter_grad.reshape(long_filter.shape),
        kmer_grad.reshape(kmer_len, letter_count, local_width),
        gain_grad,
    )


def solution(mesh):
    in_specs = (
        P(("groups", "seq")),
        P(),
        P(),
        P(None, None, ("chan", "pair")),
        P(("chan", "pair"), "seq", None, None),
        P(None, ("chan", "pair")),
        P(("groups", "seq"), ("chan", "pair")),
    )
    out_specs = (
        P(("groups", "seq"), ("chan", "pair")),
        P(("groups", "chan", "pair"), "seq", None, None),
        P("groups", None, ("chan", "pair")),
        P(("groups", "chan", "pair")),
    )
    return jax.shard_map(
        per_device, mesh=mesh, in_specs=in_specs, out_specs=out_specs, check_vma=False
    )
```

```python
import math

import jax
import jax.numpy as jnp
import numpy as np
from jax import lax
from jax.sharding import PartitionSpec as P

NORM_EPSILON = 1e-05
PRECISE = lax.Precision.HIGHEST
TRANSFORM_PRECISION = lax.Precision.HIGH


def from_behind(value, axis, steps):
    count = lax.axis_size(axis)
    first, last = (max(0, -steps), min(count, count - steps))
    return lax.ppermute(value, axis, [(source, source + steps) for source in range(first, last)])


def dft_matrix(length):
    total = 2 * length
    inner_len = 32 if length % 32 == 0 else 1
    outer_len = length // inner_len
    j = lax.broadcasted_iota(jnp.int32, (1, total), 1)
    k = jnp.where(j < length, j, j - length)
    k = jnp.where(j == length, length, k)
    phase = jnp.where(j > length, 3 * total // 4, 0)
    scale = 2.0 * math.pi / total

    def angle(idx):
        idx = idx % total
        idx = jnp.where(idx >= length, idx - total, idx)
        return idx.astype(jnp.float32) * scale

    outer = lax.optimization_barrier(lax.broadcasted_iota(jnp.int32, (outer_len, 1), 0))
    inner = lax.optimization_barrier(lax.broadcasted_iota(jnp.int32, (inner_len, 1), 0))
    alpha = angle(outer * inner_len * k)
    beta = angle(inner * k + phase)
    ca, sa = jnp.cos(alpha), jnp.sin(alpha)
    cb, sb = jnp.cos(beta), jnp.sin(beta)
    table = ca[:, None, :] * cb[None, :, :] - sa[:, None, :] * sb[None, :, :]
    return lax.optimization_barrier(table.reshape(length, total))


def xor_exchange(x, axis, step):
    count = lax.axis_size(axis)
    return lax.ppermute(x, axis, [(i, i ^ step) for i in range(count)])


def all_gather_cp(x):
    chans, pairs = lax.axis_size("chan"), lax.axis_size("pair")
    y = x[None]
    sources = [lax.axis_index(("chan", "pair"))]
    for axis, size, stride in (("chan", chans, pairs), ("pair", pairs, 1)):
        step = 1
        while step < size:
            y = jnp.concatenate([y, xor_exchange(y, axis, step)], axis=0)
            sources = sources + [source ^ (step * stride) for source in sources]
            step *= 2
    return y, sources


def group_exchange(x, axes, count, offset):
    return lax.ppermute(x, axes, [(i, i ^ offset) for i in range(count)])


def reduce_blocks_cp(x, width):
    axes = ("chan", "pair")
    count = lax.axis_size("chan") * lax.axis_size("pair")
    me = lax.axis_index(axes)
    blocks = [x[:, g * width : (g + 1) * width] for g in range(count)]

    def pick(index):
        out = blocks[0]
        for g in range(1, count):
            out = jnp.where(index == g, blocks[g], out)
        return out

    sent = {
        offset: group_exchange(pick(me ^ offset), axes, count, offset)
        for offset in range(count - 1, 0, -1)
    }
    total = pick(me)
    for offset in range(1, count):
        total = total + sent[offset]
    return total


def sum_over_seq(x, tied):
    count = lax.axis_size("seq")
    me = lax.axis_index("seq")
    if count > 4:
        step = 1
        while step < count:
            got, tied = lax.optimization_barrier((xor_exchange(x, "seq", step), tied))
            x = x + got
            step *= 2
        return x, tied
    sent = {offset: group_exchange(x, "seq", count, offset) for offset in range(count - 1, 0, -1)}
    got = [x] + [sent[offset] for offset in range(1, count)]
    got, tied = lax.optimization_barrier((got, tied))
    total = None
    for source in range(count):
        piece = got[0]
        for offset in range(1, count):
            piece = jnp.where((me ^ source) == offset, got[offset], piece)
        total = piece if total is None else total + piece
    return total, tied


def all_to_all_seq(x, split_axis, concat_axis):
    count = lax.axis_size("seq")
    if count > 4:
        return lax.all_to_all(x, "seq", split_axis=split_axis, concat_axis=concat_axis, tiled=True)
    me = lax.axis_index("seq")
    width = x.shape[split_axis] // count
    blocks = [lax.slice_in_dim(x, j * width, (j + 1) * width, axis=split_axis) for j in range(count)]

    def pick(index):
        out = blocks[0]
        for j in range(1, count):
            out = jnp.where(index == j, blocks[j], out)
        return out

    sent = {
        offset: group_exchange(pick(me ^ offset), "seq", count, offset)
        for offset in range(count - 1, 0, -1)
    }
    got = [pick(me)] + [sent[offset] for offset in range(1, count)]
    pieces = []
    for source in range(count):
        piece = got[0]
        for offset in range(1, count):
            piece = jnp.where((me ^ source) == offset, got[offset], piece)
        pieces.append(piece)
    return jnp.concatenate(pieces, axis=concat_axis)


def forward_dft(signal, dft):
    return jnp.dot(signal.astype(jnp.float32), dft, precision=TRANSFORM_PRECISION)


def inverse_dft(spec, dft):
    length = dft.shape[0]
    total = 2 * length
    col = np.arange(total)[None, :]
    weight = np.where(col % length == 0, 1.0 / total, 2.0 / total).astype(np.float32)
    return lax.dot_general(
        spec * weight, dft, (((1,), (1,)), ((), ())), precision=TRANSFORM_PRECISION
    )


def halves(spec):
    length = spec.shape[1] // 2
    return spec[:, :length], spec[:, length:]


def first_col(shape):
    return np.arange(shape[1])[None, :] == 0


def cmul(ga, gb, xa, xb, conj_g):
    edge = first_col(ga.shape)
    sign = -1.0 if conj_g else 1.0
    ya = ga * xa - sign * (gb * xb)
    yb = ga * xb + sign * (gb * xa)
    ya = jnp.where(edge, ga * xa, ya)
    yb = jnp.where(edge, gb * xb, yb)
    return jnp.concatenate([ya, yb], axis=1)


def pair_flip(values):
    even = (np.arange(values.shape[0]) % 2 == 0)[:, None]
    up = jnp.roll(values, -1, axis=0)
    down = jnp.roll(values, 1, axis=0)
    return jnp.where(even, up, down)


def add_conj_flip(spec):
    a, b = halves(spec)
    fa, fb = halves(pair_flip(spec))
    edge = first_col(a.shape)
    return jnp.concatenate([a + fa, jnp.where(edge, b + fb, b - fb)], axis=1)


def norm_gain_local(norm_gain, group_index, local_width):
    return lax.dynamic_slice_in_dim(norm_gain, group_index * local_width, local_width, 0)


def per_device(tokens, kmer_table, norm_gain, in_proj, long_filter, out_proj, cotangent):
    row_count = tokens.shape[0]
    kmer_len, letter_count, model_width = kmer_table.shape
    local_width = in_proj.shape[2]
    length = row_count * lax.axis_size("seq")
    group_index = lax.axis_index(("chan", "pair"))
    rim_width = kmer_len - 1
    seq_count = lax.axis_size("seq")
    before = lax.ppermute(
        tokens[row_count - rim_width :], "seq", [(i, (i + 1) % seq_count) for i in range(seq_count)]
    )
    before = jnp.where(lax.axis_index("seq") == 0, -1, before)
    extended = jnp.concatenate([before, tokens])
    letters = jnp.arange(letter_count, dtype=jnp.int32)
    columns = []
    for shift_back in range(kmer_len):
        window = extended[rim_width - shift_back : rim_width - shift_back + row_count]
        columns.append(window[:, None] == letters[None, :])
    onehot_t = jnp.concatenate(columns, axis=1).T.astype(jnp.bfloat16)
    table_t = kmer_table.reshape(kmer_len * letter_count, model_width).T
    embedded = jnp.dot(table_t, onehot_t, preferred_element_type=jnp.float32)
    inv_rms = lax.rsqrt(jnp.mean(embedded * embedded, axis=0, keepdims=True) + NORM_EPSILON)
    normed = embedded * inv_rms
    scaled_normed = normed * norm_gain[:, None]
    hidden = scaled_normed.astype(jnp.bfloat16)
    projected = jnp.einsum("dr,dmc->mcr", hidden, in_proj, preferred_element_type=jnp.float32)
    residual = (scaled_normed - hidden.astype(jnp.float32)).astype(jnp.bfloat16)
    unrounded = projected + jnp.einsum(
        "dr,dmc->mcr", residual, in_proj, preferred_element_type=jnp.float32
    )
    query_part = projected[0]
    key_part = projected[1]
    value_part = projected[2]
    mixed_in = (key_part * value_part).astype(jnp.bfloat16)
    grad_scale = 1.0 / math.sqrt(length)
    groups = lax.axis_size("chan") * lax.axis_size("pair")
    gated_partial = jnp.einsum("rd,cd->rc", cotangent, out_proj, preferred_element_type=jnp.float32)
    d_gated = reduce_blocks_cp(gated_partial, local_width).T * grad_scale
    dft = dft_matrix(length)
    filter_rows = long_filter.reshape(long_filter.shape[2], long_filter.shape[3])
    spec_g = add_conj_flip(forward_dft(filter_rows, dft))
    d_conv = (d_gated * query_part).astype(jnp.bfloat16)
    both_cols = all_to_all_seq(jnp.stack([mixed_in, d_conv]), 1, 2)
    both_cols, (spec_g, dft, unrounded) = lax.optimization_barrier(
        (both_cols, (spec_g, dft, unrounded))
    )
    mixed_cols, d_cols = both_cols[0], both_cols[1]
    ga, gb = halves(spec_g)
    spec_s = forward_dft(mixed_cols, dft)
    sa, sb = halves(spec_s)
    conv_cols = inverse_dft(cmul(ga, gb, sa, sb, False), dft).astype(jnp.bfloat16)
    spec_d = forward_dft(d_cols, dft)
    da, db = halves(spec_d)
    d_mixed_cols = inverse_dft(cmul(ga, gb, da, db, True), dft).astype(jnp.bfloat16)
    both_rows = all_to_all_seq(jnp.stack([conv_cols, d_mixed_cols]), 2, 1)
    conv_rows, d_mixed = both_rows[0], both_rows[1]
    gated_rows = (query_part * conv_rows.astype(jnp.float32)).astype(jnp.bfloat16)
    weight_rows = out_proj
    gathered, sources = all_gather_cp(gated_rows)
    mixed_out = None
    for slot in range(len(sources)):
        piece = gathered[0]
        for index in range(1, len(sources)):
            piece = jnp.where(sources[index] == slot, gathered[index], piece)
        term = jnp.einsum(
            "cr,cd->rd",
            piece,
            weight_rows[slot * local_width : (slot + 1) * local_width],
            preferred_element_type=jnp.float32,
        )
        mixed_out = term if mixed_out is None else mixed_out + term
    own_rows = lax.dynamic_slice_in_dim(embedded, group_index * local_width, local_width, 0)
    block_out = (mixed_out + own_rows.T).astype(jnp.bfloat16)
    d_query = d_gated * conv_rows.astype(jnp.float32)
    cross = cmul(sa, sb, da, db, True)
    filter_grad = inverse_dft(add_conj_flip(cross), dft)
    d_key = d_mixed.astype(jnp.float32) * value_part
    d_value = d_mixed.astype(jnp.float32) * key_part
    d_proj = jnp.stack([d_query, d_key, d_value]).astype(jnp.bfloat16)
    d_full = jnp.einsum("mcr,dmc->rd", d_proj, in_proj, preferred_element_type=jnp.float32)
    stat_part = jnp.sum(d_proj.astype(jnp.float32) * unrounded, axis=(0, 1))
    onehot_rows = onehot_t.T.astype(jnp.float32)
    weights = onehot_rows * inv_rms.T
    direct = jnp.einsum("rk,rd->kd", weights, d_full, precision=PRECISE)
    centred = jnp.einsum("rk,dr->kd", weights * stat_part[:, None], normed, precision=PRECISE)
    table_all = norm_gain[None, :] * direct - centred / model_width
    gain_all = jnp.einsum("rd,dr->d", d_full, normed, precision=PRECISE)
    partial = jnp.concatenate([table_all, gain_all[None, :]], axis=0)
    own_block = reduce_blocks_cp(partial, local_width)
    cot_table = jnp.einsum(
        "rk,rc->kc", onehot_rows, cotangent.astype(jnp.float32) * grad_scale, precision=PRECISE
    )
    own_block = own_block + jnp.concatenate(
        [cot_table, jnp.zeros((1, local_width), jnp.float32)], axis=0
    )
    summed, (block_out, filter_grad) = sum_over_seq(own_block, (block_out, filter_grad))
    kmer_grad = summed[: kmer_len * letter_count]
    gain_grad = summed[kmer_len * letter_count]
    return (
        block_out,
        filter_grad.reshape(long_filter.shape),
        kmer_grad.reshape(kmer_len, letter_count, local_width),
        gain_grad,
    )


def solution(mesh):
    in_specs = (
        P(("groups", "seq")),
        P(),
        P(),
        P(None, None, ("chan", "pair")),
        P(("chan", "pair"), "seq", None, None),
        P(None, ("chan", "pair")),
        P(("groups", "seq"), ("chan", "pair")),
    )
    out_specs = (
        P(("groups", "seq"), ("chan", "pair")),
        P(("groups", "chan", "pair"), "seq", None, None),
        P("groups", None, ("chan", "pair")),
        P(("groups", "chan", "pair")),
    )
    return jax.shard_map(
        per_device, mesh=mesh, in_specs=in_specs, out_specs=out_specs, check_vma=False
    )
```

```python
import math

import jax
import jax.numpy as jnp
import numpy as np
from jax import lax
from jax.sharding import PartitionSpec as P

NORM_EPSILON = 1e-05
PRECISE = lax.Precision.HIGHEST
TRANSFORM_PRECISION = lax.Precision.HIGH


def from_behind(value, axis, steps):
    count = lax.axis_size(axis)
    first, last = (max(0, -steps), min(count, count - steps))
    return lax.ppermute(value, axis, [(source, source + steps) for source in range(first, last)])


def dft_matrix(length):
    total = 2 * length
    inner_len = 32 if length % 32 == 0 else 1
    outer_len = length // inner_len
    j = lax.broadcasted_iota(jnp.int32, (1, total), 1)
    k = jnp.where(j < length, j, j - length)
    k = jnp.where(j == length, length, k)
    phase = jnp.where(j > length, 3 * total // 4, 0)
    scale = 2.0 * math.pi / total

    def angle(idx):
        idx = idx % total
        idx = jnp.where(idx >= length, idx - total, idx)
        return idx.astype(jnp.float32) * scale

    outer = lax.optimization_barrier(lax.broadcasted_iota(jnp.int32, (outer_len, 1), 0))
    inner = lax.optimization_barrier(lax.broadcasted_iota(jnp.int32, (inner_len, 1), 0))
    alpha = angle(outer * inner_len * k)
    beta = angle(inner * k + phase)
    ca, sa = jnp.cos(alpha), jnp.sin(alpha)
    cb, sb = jnp.cos(beta), jnp.sin(beta)
    table = ca[:, None, :] * cb[None, :, :] - sa[:, None, :] * sb[None, :, :]
    return lax.optimization_barrier(table.reshape(length, total))


def xor_exchange(x, axis, step):
    count = lax.axis_size(axis)
    return lax.ppermute(x, axis, [(i, i ^ step) for i in range(count)])


def all_gather_cp(x):
    chans, pairs = lax.axis_size("chan"), lax.axis_size("pair")
    y = x[None]
    sources = [lax.axis_index(("chan", "pair"))]
    for axis, size, stride in (("chan", chans, pairs), ("pair", pairs, 1)):
        step = 1
        while step < size:
            y = jnp.concatenate([y, xor_exchange(y, axis, step)], axis=0)
            sources = sources + [source ^ (step * stride) for source in sources]
            step *= 2
    return y, sources


def group_exchange(x, axes, count, offset):
    return lax.ppermute(x, axes, [(i, i ^ offset) for i in range(count)])


def reduce_blocks_cp(x, width):
    axes = ("chan", "pair")
    count = lax.axis_size("chan") * lax.axis_size("pair")
    me = lax.axis_index(axes)

    def pick(index):
        return lax.dynamic_slice_in_dim(x, index * width, width, 1)

    total = pick(me)
    for offset in range(1, count):
        total = total + group_exchange(pick(me ^ offset), axes, count, offset)
    return total


def sum_over_seq(x, tied):
    count = lax.axis_size("seq")
    me = lax.axis_index("seq")
    if count > 4:
        step = 1
        while step < count:
            got, tied = lax.optimization_barrier((xor_exchange(x, "seq", step), tied))
            x = x + got
            step *= 2
        return x, tied
    sent = {offset: group_exchange(x, "seq", count, offset) for offset in range(count - 1, 0, -1)}
    got = [x] + [sent[offset] for offset in range(1, count)]
    got, tied = lax.optimization_barrier((got, tied))
    total = None
    for source in range(count):
        piece = got[0]
        for offset in range(1, count):
            piece = jnp.where((me ^ source) == offset, got[offset], piece)
        total = piece if total is None else total + piece
    return total, tied


def all_to_all_seq(x, split_axis, concat_axis):
    count = lax.axis_size("seq")
    if count > 4:
        return lax.all_to_all(x, "seq", split_axis=split_axis, concat_axis=concat_axis, tiled=True)
    me = lax.axis_index("seq")
    width = x.shape[split_axis] // count
    blocks = [lax.slice_in_dim(x, j * width, (j + 1) * width, axis=split_axis) for j in range(count)]

    def pick(index):
        out = blocks[0]
        for j in range(1, count):
            out = jnp.where(index == j, blocks[j], out)
        return out

    sent = {
        offset: group_exchange(pick(me ^ offset), "seq", count, offset)
        for offset in range(count - 1, 0, -1)
    }
    got = [pick(me)] + [sent[offset] for offset in range(1, count)]
    pieces = []
    for source in range(count):
        piece = got[0]
        for offset in range(1, count):
            piece = jnp.where((me ^ source) == offset, got[offset], piece)
        pieces.append(piece)
    return jnp.concatenate(pieces, axis=concat_axis)


def forward_dft(signal, dft):
    return jnp.dot(signal.astype(jnp.float32), dft, precision=TRANSFORM_PRECISION)


def inverse_dft(spec, dft):
    length = dft.shape[0]
    total = 2 * length
    col = np.arange(total)[None, :]
    weight = np.where(col % length == 0, 1.0 / total, 2.0 / total).astype(np.float32)
    return lax.dot_general(
        spec * weight, dft, (((1,), (1,)), ((), ())), precision=TRANSFORM_PRECISION
    )


def halves(spec):
    length = spec.shape[1] // 2
    return spec[:, :length], spec[:, length:]


def first_col(shape):
    return np.arange(shape[1])[None, :] == 0


def cmul(ga, gb, xa, xb, conj_g):
    edge = first_col(ga.shape)
    sign = -1.0 if conj_g else 1.0
    ya = ga * xa - sign * (gb * xb)
    yb = ga * xb + sign * (gb * xa)
    ya = jnp.where(edge, ga * xa, ya)
    yb = jnp.where(edge, gb * xb, yb)
    return jnp.concatenate([ya, yb], axis=1)


def pair_flip(values):
    even = (np.arange(values.shape[0]) % 2 == 0)[:, None]
    up = jnp.roll(values, -1, axis=0)
    down = jnp.roll(values, 1, axis=0)
    return jnp.where(even, up, down)


def add_conj_flip(spec):
    a, b = halves(spec)
    fa, fb = halves(pair_flip(spec))
    edge = first_col(a.shape)
    return jnp.concatenate([a + fa, jnp.where(edge, b + fb, b - fb)], axis=1)


def norm_gain_local(norm_gain, group_index, local_width):
    return lax.dynamic_slice_in_dim(norm_gain, group_index * local_width, local_width, 0)


def per_device(tokens, kmer_table, norm_gain, in_proj, long_filter, out_proj, cotangent):
    row_count = tokens.shape[0]
    kmer_len, letter_count, model_width = kmer_table.shape
    local_width = in_proj.shape[2]
    length = row_count * lax.axis_size("seq")
    group_index = lax.axis_index(("chan", "pair"))
    rim_width = kmer_len - 1
    seq_count = lax.axis_size("seq")
    before = lax.ppermute(
        tokens[row_count - rim_width :], "seq", [(i, (i + 1) % seq_count) for i in range(seq_count)]
    )
    before = jnp.where(lax.axis_index("seq") == 0, -1, before)
    extended = jnp.concatenate([before, tokens])
    letters = jnp.arange(letter_count, dtype=jnp.int32)
    columns = []
    for shift_back in range(kmer_len):
        window = extended[rim_width - shift_back : rim_width - shift_back + row_count]
        columns.append(window[:, None] == letters[None, :])
    onehot_t = jnp.concatenate(columns, axis=1).T.astype(jnp.bfloat16)
    table_t = kmer_table.reshape(kmer_len * letter_count, model_width).T
    embedded = jnp.dot(table_t, onehot_t, preferred_element_type=jnp.float32)
    inv_rms = lax.rsqrt(jnp.mean(embedded * embedded, axis=0, keepdims=True) + NORM_EPSILON)
    normed = embedded * inv_rms
    scaled_normed = normed * norm_gain[:, None]
    hidden = scaled_normed.astype(jnp.bfloat16)
    projected = jnp.einsum("dr,dmc->mcr", hidden, in_proj, preferred_element_type=jnp.float32)
    residual = (scaled_normed - hidden.astype(jnp.float32)).astype(jnp.bfloat16)
    unrounded = projected + jnp.einsum(
        "dr,dmc->mcr", residual, in_proj, preferred_element_type=jnp.float32
    )
    query_part = projected[0]
    key_part = projected[1]
    value_part = projected[2]
    mixed_in = (key_part * value_part).astype(jnp.bfloat16)
    grad_scale = 1.0 / math.sqrt(length)
    groups = lax.axis_size("chan") * lax.axis_size("pair")
    gated_partial = jnp.einsum("rd,cd->rc", cotangent, out_proj, preferred_element_type=jnp.float32)
    d_gated = reduce_blocks_cp(gated_partial, local_width).T * grad_scale
    dft = dft_matrix(length)
    filter_rows = long_filter.reshape(long_filter.shape[2], long_filter.shape[3])
    spec_g = add_conj_flip(forward_dft(filter_rows, dft))
    d_conv = (d_gated * query_part).astype(jnp.bfloat16)
    both_cols = all_to_all_seq(jnp.stack([mixed_in, d_conv]), 1, 2)
    both_cols, (spec_g, dft, unrounded) = lax.optimization_barrier(
        (both_cols, (spec_g, dft, unrounded))
    )
    mixed_cols, d_cols = both_cols[0], both_cols[1]
    ga, gb = halves(spec_g)
    spec_s = forward_dft(mixed_cols, dft)
    sa, sb = halves(spec_s)
    conv_cols = inverse_dft(cmul(ga, gb, sa, sb, False), dft).astype(jnp.bfloat16)
    spec_d = forward_dft(d_cols, dft)
    da, db = halves(spec_d)
    d_mixed_cols = inverse_dft(cmul(ga, gb, da, db, True), dft).astype(jnp.bfloat16)
    both_rows = all_to_all_seq(jnp.stack([conv_cols, d_mixed_cols]), 2, 1)
    conv_rows, d_mixed = both_rows[0], both_rows[1]
    gated_rows = (query_part * conv_rows.astype(jnp.float32)).astype(jnp.bfloat16)
    weight_rows = out_proj
    gathered, sources = all_gather_cp(gated_rows)
    mixed_out = None
    for slot in range(len(sources)):
        piece = gathered[0]
        for index in range(1, len(sources)):
            piece = jnp.where(sources[index] == slot, gathered[index], piece)
        term = jnp.einsum(
            "cr,cd->rd",
            piece,
            weight_rows[slot * local_width : (slot + 1) * local_width],
            preferred_element_type=jnp.float32,
        )
        mixed_out = term if mixed_out is None else mixed_out + term
    own_rows = lax.dynamic_slice_in_dim(embedded, group_index * local_width, local_width, 0)
    block_out = (mixed_out + own_rows.T).astype(jnp.bfloat16)
    d_query = d_gated * conv_rows.astype(jnp.float32)
    cross = cmul(sa, sb, da, db, True)
    filter_grad = inverse_dft(add_conj_flip(cross), dft)
    d_key = d_mixed.astype(jnp.float32) * value_part
    d_value = d_mixed.astype(jnp.float32) * key_part
    d_proj = jnp.stack([d_query, d_key, d_value]).astype(jnp.bfloat16)
    d_full = jnp.einsum("mcr,dmc->rd", d_proj, in_proj, preferred_element_type=jnp.float32)
    stat_part = jnp.sum(d_proj.astype(jnp.float32) * unrounded, axis=(0, 1))
    onehot_rows = onehot_t.T.astype(jnp.float32)
    weights = onehot_rows * inv_rms.T
    direct = jnp.einsum("rk,rd->kd", weights, d_full, precision=PRECISE)
    centred = jnp.einsum("rk,dr->kd", weights * stat_part[:, None], normed, precision=PRECISE)
    table_all = norm_gain[None, :] * direct - centred / model_width
    gain_all = jnp.einsum("rd,dr->d", d_full, normed, precision=PRECISE)
    partial = jnp.concatenate([table_all, gain_all[None, :]], axis=0)
    own_block = reduce_blocks_cp(partial, local_width)
    cot_table = jnp.einsum(
        "rk,rc->kc", onehot_rows, cotangent.astype(jnp.float32) * grad_scale, precision=PRECISE
    )
    own_block = own_block + jnp.concatenate(
        [cot_table, jnp.zeros((1, local_width), jnp.float32)], axis=0
    )
    summed, (block_out, filter_grad) = sum_over_seq(own_block, (block_out, filter_grad))
    kmer_grad = summed[: kmer_len * letter_count]
    gain_grad = summed[kmer_len * letter_count]
    return (
        block_out,
        filter_grad.reshape(long_filter.shape),
        kmer_grad.reshape(kmer_len, letter_count, local_width),
        gain_grad,
    )


def solution(mesh):
    in_specs = (
        P(("groups", "seq")),
        P(),
        P(),
        P(None, None, ("chan", "pair")),
        P(("chan", "pair"), "seq", None, None),
        P(None, ("chan", "pair")),
        P(("groups", "seq"), ("chan", "pair")),
    )
    out_specs = (
        P(("groups", "seq"), ("chan", "pair")),
        P(("groups", "chan", "pair"), "seq", None, None),
        P("groups", None, ("chan", "pair")),
        P(("groups", "chan", "pair")),
    )
    return jax.shard_map(
        per_device, mesh=mesh, in_specs=in_specs, out_specs=out_specs, check_vma=False
    )
```

```python
import math

import jax
import jax.numpy as jnp
import numpy as np
from jax import lax
from jax.sharding import PartitionSpec as P

NORM_EPSILON = 1e-05
PRECISE = lax.Precision.HIGHEST
TRANSFORM_PRECISION = lax.Precision.HIGH


def from_behind(value, axis, steps):
    count = lax.axis_size(axis)
    first, last = (max(0, -steps), min(count, count - steps))
    return lax.ppermute(value, axis, [(source, source + steps) for source in range(first, last)])


def dft_matrix(length):
    total = 2 * length
    inner_len = 32 if length % 32 == 0 else 1
    outer_len = length // inner_len
    j = lax.broadcasted_iota(jnp.int32, (1, total), 1)
    k = jnp.where(j < length, j, j - length)
    k = jnp.where(j == length, length, k)
    phase = jnp.where(j > length, 3 * total // 4, 0)
    scale = 2.0 * math.pi / total

    def angle(idx):
        idx = idx % total
        idx = jnp.where(idx >= length, idx - total, idx)
        return idx.astype(jnp.float32) * scale

    outer = lax.optimization_barrier(lax.broadcasted_iota(jnp.int32, (outer_len, 1), 0))
    inner = lax.optimization_barrier(lax.broadcasted_iota(jnp.int32, (inner_len, 1), 0))
    alpha = angle(outer * inner_len * k)
    beta = angle(inner * k + phase)
    ca, sa = jnp.cos(alpha), jnp.sin(alpha)
    cb, sb = jnp.cos(beta), jnp.sin(beta)
    table = ca[:, None, :] * cb[None, :, :] - sa[:, None, :] * sb[None, :, :]
    return lax.optimization_barrier(table.reshape(length, total))


def xor_exchange(x, axis, step):
    count = lax.axis_size(axis)
    return lax.ppermute(x, axis, [(i, i ^ step) for i in range(count)])


def all_gather_cp(x):
    chans, pairs = lax.axis_size("chan"), lax.axis_size("pair")
    y = x[None]
    sources = [lax.axis_index(("chan", "pair"))]
    for axis, size, stride in (("chan", chans, pairs), ("pair", pairs, 1)):
        step = 1
        while step < size:
            y = jnp.concatenate([y, xor_exchange(y, axis, step)], axis=0)
            sources = sources + [source ^ (step * stride) for source in sources]
            step *= 2
    return y, sources


def group_exchange(x, axes, count, offset):
    return lax.ppermute(x, axes, [(i, i ^ offset) for i in range(count)])


def reduce_blocks_cp(x, width):
    axes = ("chan", "pair")
    count = lax.axis_size("chan") * lax.axis_size("pair")
    me = lax.axis_index(axes)

    def pick(index):
        return lax.dynamic_slice_in_dim(x, index * width, width, 1)

    total = pick(me)
    for offset in range(1, count):
        total = total + group_exchange(pick(me ^ offset), axes, count, offset)
    return total


def sum_over_seq(x, tied):
    count = lax.axis_size("seq")
    me = lax.axis_index("seq")
    if count > 4:
        step = 1
        while step < count:
            got, tied = lax.optimization_barrier((xor_exchange(x, "seq", step), tied))
            x = x + got
            step *= 2
        return x, tied
    sent = {offset: group_exchange(x, "seq", count, offset) for offset in range(count - 1, 0, -1)}
    got = [x] + [sent[offset] for offset in range(1, count)]
    got, tied = lax.optimization_barrier((got, tied))
    total = None
    for source in range(count):
        piece = got[0]
        for offset in range(1, count):
            piece = jnp.where((me ^ source) == offset, got[offset], piece)
        total = piece if total is None else total + piece
    return total, tied


def all_to_all_seq(x, split_axis, concat_axis):
    count = lax.axis_size("seq")
    if count > 4:
        return lax.all_to_all(x, "seq", split_axis=split_axis, concat_axis=concat_axis, tiled=True)
    me = lax.axis_index("seq")
    width = x.shape[split_axis] // count

    def pick(index):
        return lax.dynamic_slice_in_dim(x, index * width, width, split_axis)

    sent = {
        offset: group_exchange(pick(me ^ offset), "seq", count, offset)
        for offset in range(count - 1, 0, -1)
    }
    got = [pick(me)] + [sent[offset] for offset in range(1, count)]
    pieces = []
    for source in range(count):
        piece = got[0]
        for offset in range(1, count):
            piece = jnp.where((me ^ source) == offset, got[offset], piece)
        pieces.append(piece)
    return jnp.concatenate(pieces, axis=concat_axis)


def forward_dft(signal, dft):
    return jnp.dot(signal.astype(jnp.float32), dft, precision=TRANSFORM_PRECISION)


def inverse_dft(spec, dft):
    length = dft.shape[0]
    total = 2 * length
    col = np.arange(total)[None, :]
    weight = np.where(col % length == 0, 1.0 / total, 2.0 / total).astype(np.float32)
    return lax.dot_general(
        spec * weight, dft, (((1,), (1,)), ((), ())), precision=TRANSFORM_PRECISION
    )


def halves(spec):
    length = spec.shape[1] // 2
    return spec[:, :length], spec[:, length:]


def first_col(shape):
    return np.arange(shape[1])[None, :] == 0


def cmul(ga, gb, xa, xb, conj_g):
    edge = first_col(ga.shape)
    sign = -1.0 if conj_g else 1.0
    ya = ga * xa - sign * (gb * xb)
    yb = ga * xb + sign * (gb * xa)
    ya = jnp.where(edge, ga * xa, ya)
    yb = jnp.where(edge, gb * xb, yb)
    return jnp.concatenate([ya, yb], axis=1)


def pair_flip(values):
    even = (np.arange(values.shape[0]) % 2 == 0)[:, None]
    up = jnp.roll(values, -1, axis=0)
    down = jnp.roll(values, 1, axis=0)
    return jnp.where(even, up, down)


def add_conj_flip(spec):
    a, b = halves(spec)
    fa, fb = halves(pair_flip(spec))
    edge = first_col(a.shape)
    return jnp.concatenate([a + fa, jnp.where(edge, b + fb, b - fb)], axis=1)


def norm_gain_local(norm_gain, group_index, local_width):
    return lax.dynamic_slice_in_dim(norm_gain, group_index * local_width, local_width, 0)


def per_device(tokens, kmer_table, norm_gain, in_proj, long_filter, out_proj, cotangent):
    row_count = tokens.shape[0]
    kmer_len, letter_count, model_width = kmer_table.shape
    local_width = in_proj.shape[2]
    length = row_count * lax.axis_size("seq")
    group_index = lax.axis_index(("chan", "pair"))
    rim_width = kmer_len - 1
    seq_count = lax.axis_size("seq")
    before = lax.ppermute(
        tokens[row_count - rim_width :], "seq", [(i, (i + 1) % seq_count) for i in range(seq_count)]
    )
    before = jnp.where(lax.axis_index("seq") == 0, -1, before)
    extended = jnp.concatenate([before, tokens])
    letters = jnp.arange(letter_count, dtype=jnp.int32)
    columns = []
    for shift_back in range(kmer_len):
        window = extended[rim_width - shift_back : rim_width - shift_back + row_count]
        columns.append(window[:, None] == letters[None, :])
    onehot_t = jnp.concatenate(columns, axis=1).T.astype(jnp.bfloat16)
    table_t = kmer_table.reshape(kmer_len * letter_count, model_width).T
    embedded = jnp.dot(table_t, onehot_t, preferred_element_type=jnp.float32)
    inv_rms = lax.rsqrt(jnp.mean(embedded * embedded, axis=0, keepdims=True) + NORM_EPSILON)
    normed = embedded * inv_rms
    scaled_normed = normed * norm_gain[:, None]
    hidden = scaled_normed.astype(jnp.bfloat16)
    projected = jnp.einsum("dr,dmc->mcr", hidden, in_proj, preferred_element_type=jnp.float32)
    residual = (scaled_normed - hidden.astype(jnp.float32)).astype(jnp.bfloat16)
    unrounded = projected + jnp.einsum(
        "dr,dmc->mcr", residual, in_proj, preferred_element_type=jnp.float32
    )
    query_part = projected[0]
    key_part = projected[1]
    value_part = projected[2]
    mixed_in = (key_part * value_part).astype(jnp.bfloat16)
    grad_scale = 1.0 / math.sqrt(length)
    groups = lax.axis_size("chan") * lax.axis_size("pair")
    gated_partial = jnp.einsum("rd,cd->rc", cotangent, out_proj, preferred_element_type=jnp.float32)
    d_gated = reduce_blocks_cp(gated_partial, local_width).T * grad_scale
    dft = dft_matrix(length)
    filter_rows = long_filter.reshape(long_filter.shape[2], long_filter.shape[3])
    spec_g = add_conj_flip(forward_dft(filter_rows, dft))
    d_conv = (d_gated * query_part).astype(jnp.bfloat16)
    both_cols = all_to_all_seq(jnp.stack([mixed_in, d_conv]), 1, 2)
    both_cols, (spec_g, dft, unrounded) = lax.optimization_barrier(
        (both_cols, (spec_g, dft, unrounded))
    )
    mixed_cols, d_cols = both_cols[0], both_cols[1]
    ga, gb = halves(spec_g)
    spec_s = forward_dft(mixed_cols, dft)
    sa, sb = halves(spec_s)
    conv_cols = inverse_dft(cmul(ga, gb, sa, sb, False), dft).astype(jnp.bfloat16)
    spec_d = forward_dft(d_cols, dft)
    da, db = halves(spec_d)
    d_mixed_cols = inverse_dft(cmul(ga, gb, da, db, True), dft).astype(jnp.bfloat16)
    both_rows = all_to_all_seq(jnp.stack([conv_cols, d_mixed_cols]), 2, 1)
    conv_rows, d_mixed = both_rows[0], both_rows[1]
    gated_rows = (query_part * conv_rows.astype(jnp.float32)).astype(jnp.bfloat16)
    weight_rows = out_proj
    gathered, sources = all_gather_cp(gated_rows)
    mixed_out = None
    for slot in range(len(sources)):
        piece = gathered[0]
        for index in range(1, len(sources)):
            piece = jnp.where(sources[index] == slot, gathered[index], piece)
        term = jnp.einsum(
            "cr,cd->rd",
            piece,
            weight_rows[slot * local_width : (slot + 1) * local_width],
            preferred_element_type=jnp.float32,
        )
        mixed_out = term if mixed_out is None else mixed_out + term
    own_rows = lax.dynamic_slice_in_dim(embedded, group_index * local_width, local_width, 0)
    block_out = (mixed_out + own_rows.T).astype(jnp.bfloat16)
    d_query = d_gated * conv_rows.astype(jnp.float32)
    cross = cmul(sa, sb, da, db, True)
    filter_grad = inverse_dft(add_conj_flip(cross), dft)
    d_key = d_mixed.astype(jnp.float32) * value_part
    d_value = d_mixed.astype(jnp.float32) * key_part
    d_proj = jnp.stack([d_query, d_key, d_value]).astype(jnp.bfloat16)
    d_full = jnp.einsum("mcr,dmc->rd", d_proj, in_proj, preferred_element_type=jnp.float32)
    stat_part = jnp.sum(d_proj.astype(jnp.float32) * unrounded, axis=(0, 1))
    onehot_rows = onehot_t.T.astype(jnp.float32)
    weights = onehot_rows * inv_rms.T
    direct = jnp.einsum("rk,rd->kd", weights, d_full, precision=PRECISE)
    centred = jnp.einsum("rk,dr->kd", weights * stat_part[:, None], normed, precision=PRECISE)
    table_all = norm_gain[None, :] * direct - centred / model_width
    gain_all = jnp.einsum("rd,dr->d", d_full, normed, precision=PRECISE)
    partial = jnp.concatenate([table_all, gain_all[None, :]], axis=0)
    own_block = reduce_blocks_cp(partial, local_width)
    cot_table = jnp.einsum(
        "rk,rc->kc", onehot_rows, cotangent.astype(jnp.float32) * grad_scale, precision=PRECISE
    )
    own_block = own_block + jnp.concatenate(
        [cot_table, jnp.zeros((1, local_width), jnp.float32)], axis=0
    )
    summed, (block_out, filter_grad) = sum_over_seq(own_block, (block_out, filter_grad))
    kmer_grad = summed[: kmer_len * letter_count]
    gain_grad = summed[kmer_len * letter_count]
    return (
        block_out,
        filter_grad.reshape(long_filter.shape),
        kmer_grad.reshape(kmer_len, letter_count, local_width),
        gain_grad,
    )


def solution(mesh):
    in_specs = (
        P(("groups", "seq")),
        P(),
        P(),
        P(None, None, ("chan", "pair")),
        P(("chan", "pair"), "seq", None, None),
        P(None, ("chan", "pair")),
        P(("groups", "seq"), ("chan", "pair")),
    )
    out_specs = (
        P(("groups", "seq"), ("chan", "pair")),
        P(("groups", "chan", "pair"), "seq", None, None),
        P("groups", None, ("chan", "pair")),
        P(("groups", "chan", "pair")),
    )
    return jax.shard_map(
        per_device, mesh=mesh, in_specs=in_specs, out_specs=out_specs, check_vma=False
    )
```

```python
import math

import jax
import jax.numpy as jnp
import numpy as np
from jax import lax
from jax.sharding import PartitionSpec as P

NORM_EPSILON = 1e-05
PRECISE = lax.Precision.HIGHEST
TRANSFORM_PRECISION = lax.Precision.HIGH


def from_behind(value, axis, steps):
    count = lax.axis_size(axis)
    first, last = (max(0, -steps), min(count, count - steps))
    return lax.ppermute(value, axis, [(source, source + steps) for source in range(first, last)])


def dft_matrix(length):
    total = 2 * length
    inner_len = 32 if length % 32 == 0 else 1
    outer_len = length // inner_len
    j = lax.broadcasted_iota(jnp.int32, (1, total), 1)
    k = jnp.where(j < length, j, j - length)
    k = jnp.where(j == length, length, k)
    phase = jnp.where(j > length, 3 * total // 4, 0)
    scale = 2.0 * math.pi / total

    def angle(idx):
        idx = idx % total
        idx = jnp.where(idx >= length, idx - total, idx)
        return idx.astype(jnp.float32) * scale

    outer = lax.optimization_barrier(lax.broadcasted_iota(jnp.int32, (outer_len, 1), 0))
    inner = lax.optimization_barrier(lax.broadcasted_iota(jnp.int32, (inner_len, 1), 0))
    alpha = angle(outer * inner_len * k)
    beta = angle(inner * k + phase)
    ca, sa = jnp.cos(alpha), jnp.sin(alpha)
    cb, sb = jnp.cos(beta), jnp.sin(beta)
    table = ca[:, None, :] * cb[None, :, :] - sa[:, None, :] * sb[None, :, :]
    return lax.optimization_barrier(table.reshape(length, total))


def xor_exchange(x, axis, step):
    count = lax.axis_size(axis)
    return lax.ppermute(x, axis, [(i, i ^ step) for i in range(count)])


def all_gather_cp(x):
    chans, pairs = lax.axis_size("chan"), lax.axis_size("pair")
    y = x[None]
    sources = [lax.axis_index(("chan", "pair"))]
    for axis, size, stride in (("chan", chans, pairs), ("pair", pairs, 1)):
        step = 1
        while step < size:
            y = jnp.concatenate([y, xor_exchange(y, axis, step)], axis=0)
            sources = sources + [source ^ (step * stride) for source in sources]
            step *= 2
    return y, sources


def group_exchange(x, axes, count, offset):
    return lax.ppermute(x, axes, [(i, i ^ offset) for i in range(count)])


def reduce_blocks_cp(x, width):
    axes = ("chan", "pair")
    count = lax.axis_size("chan") * lax.axis_size("pair")
    me = lax.axis_index(axes)

    def pick(index):
        return lax.dynamic_slice_in_dim(x, index * width, width, 1)

    total = pick(me)
    for offset in range(1, count):
        total = total + group_exchange(pick(me ^ offset), axes, count, offset)
    return total


def sum_over_seq(x, tied):
    count = lax.axis_size("seq")
    me = lax.axis_index("seq")
    if count > 4:
        step = 1
        while step < count:
            got, tied = lax.optimization_barrier((xor_exchange(x, "seq", step), tied))
            x = x + got
            step *= 2
        return x, tied
    sent = {offset: group_exchange(x, "seq", count, offset) for offset in range(count - 1, 0, -1)}
    got = [x] + [sent[offset] for offset in range(1, count)]
    got, tied = lax.optimization_barrier((got, tied))
    stacked = jnp.stack(got)
    total = None
    for source in range(count):
        piece = lax.dynamic_index_in_dim(stacked, me ^ source, 0, keepdims=False)
        total = piece if total is None else total + piece
    return total, tied


def all_to_all_seq(x, split_axis, concat_axis):
    count = lax.axis_size("seq")
    if count > 4:
        return lax.all_to_all(x, "seq", split_axis=split_axis, concat_axis=concat_axis, tiled=True)
    me = lax.axis_index("seq")
    width = x.shape[split_axis] // count
    blocks = [lax.slice_in_dim(x, j * width, (j + 1) * width, axis=split_axis) for j in range(count)]

    def pick(index):
        out = blocks[0]
        for j in range(1, count):
            out = jnp.where(index == j, blocks[j], out)
        return out

    sent = {
        offset: group_exchange(pick(me ^ offset), "seq", count, offset)
        for offset in range(count - 1, 0, -1)
    }
    got = [pick(me)] + [sent[offset] for offset in range(1, count)]
    pieces = []
    for source in range(count):
        piece = got[0]
        for offset in range(1, count):
            piece = jnp.where((me ^ source) == offset, got[offset], piece)
        pieces.append(piece)
    return jnp.concatenate(pieces, axis=concat_axis)


def forward_dft(signal, dft):
    return jnp.dot(signal.astype(jnp.float32), dft, precision=TRANSFORM_PRECISION)


def inverse_dft(spec, dft):
    length = dft.shape[0]
    total = 2 * length
    col = np.arange(total)[None, :]
    weight = np.where(col % length == 0, 1.0 / total, 2.0 / total).astype(np.float32)
    return lax.dot_general(
        spec * weight, dft, (((1,), (1,)), ((), ())), precision=TRANSFORM_PRECISION
    )


def halves(spec):
    length = spec.shape[1] // 2
    return spec[:, :length], spec[:, length:]


def first_col(shape):
    return np.arange(shape[1])[None, :] == 0


def cmul(ga, gb, xa, xb, conj_g):
    edge = first_col(ga.shape)
    sign = -1.0 if conj_g else 1.0
    ya = ga * xa - sign * (gb * xb)
    yb = ga * xb + sign * (gb * xa)
    ya = jnp.where(edge, ga * xa, ya)
    yb = jnp.where(edge, gb * xb, yb)
    return jnp.concatenate([ya, yb], axis=1)


def pair_flip(values):
    even = (np.arange(values.shape[0]) % 2 == 0)[:, None]
    up = jnp.roll(values, -1, axis=0)
    down = jnp.roll(values, 1, axis=0)
    return jnp.where(even, up, down)


def add_conj_flip(spec):
    a, b = halves(spec)
    fa, fb = halves(pair_flip(spec))
    edge = first_col(a.shape)
    return jnp.concatenate([a + fa, jnp.where(edge, b + fb, b - fb)], axis=1)


def norm_gain_local(norm_gain, group_index, local_width):
    return lax.dynamic_slice_in_dim(norm_gain, group_index * local_width, local_width, 0)


def per_device(tokens, kmer_table, norm_gain, in_proj, long_filter, out_proj, cotangent):
    row_count = tokens.shape[0]
    kmer_len, letter_count, model_width = kmer_table.shape
    local_width = in_proj.shape[2]
    length = row_count * lax.axis_size("seq")
    group_index = lax.axis_index(("chan", "pair"))
    rim_width = kmer_len - 1
    seq_count = lax.axis_size("seq")
    before = lax.ppermute(
        tokens[row_count - rim_width :], "seq", [(i, (i + 1) % seq_count) for i in range(seq_count)]
    )
    before = jnp.where(lax.axis_index("seq") == 0, -1, before)
    extended = jnp.concatenate([before, tokens])
    letters = jnp.arange(letter_count, dtype=jnp.int32)
    columns = []
    for shift_back in range(kmer_len):
        window = extended[rim_width - shift_back : rim_width - shift_back + row_count]
        columns.append(window[:, None] == letters[None, :])
    onehot_t = jnp.concatenate(columns, axis=1).T.astype(jnp.bfloat16)
    table_t = kmer_table.reshape(kmer_len * letter_count, model_width).T
    embedded = jnp.dot(table_t, onehot_t, preferred_element_type=jnp.float32)
    inv_rms = lax.rsqrt(jnp.mean(embedded * embedded, axis=0, keepdims=True) + NORM_EPSILON)
    normed = embedded * inv_rms
    scaled_normed = normed * norm_gain[:, None]
    hidden = scaled_normed.astype(jnp.bfloat16)
    projected = jnp.einsum("dr,dmc->mcr", hidden, in_proj, preferred_element_type=jnp.float32)
    residual = (scaled_normed - hidden.astype(jnp.float32)).astype(jnp.bfloat16)
    unrounded = projected + jnp.einsum(
        "dr,dmc->mcr", residual, in_proj, preferred_element_type=jnp.float32
    )
    query_part = projected[0]
    key_part = projected[1]
    value_part = projected[2]
    mixed_in = (key_part * value_part).astype(jnp.bfloat16)
    grad_scale = 1.0 / math.sqrt(length)
    groups = lax.axis_size("chan") * lax.axis_size("pair")
    gated_partial = jnp.einsum("rd,cd->rc", cotangent, out_proj, preferred_element_type=jnp.float32)
    d_gated = reduce_blocks_cp(gated_partial, local_width).T * grad_scale
    dft = dft_matrix(length)
    filter_rows = long_filter.reshape(long_filter.shape[2], long_filter.shape[3])
    spec_g = add_conj_flip(forward_dft(filter_rows, dft))
    d_conv = (d_gated * query_part).astype(jnp.bfloat16)
    both_cols = all_to_all_seq(jnp.stack([mixed_in, d_conv]), 1, 2)
    both_cols, (spec_g, dft, unrounded) = lax.optimization_barrier(
        (both_cols, (spec_g, dft, unrounded))
    )
    mixed_cols, d_cols = both_cols[0], both_cols[1]
    ga, gb = halves(spec_g)
    spec_s = forward_dft(mixed_cols, dft)
    sa, sb = halves(spec_s)
    conv_cols = inverse_dft(cmul(ga, gb, sa, sb, False), dft).astype(jnp.bfloat16)
    spec_d = forward_dft(d_cols, dft)
    da, db = halves(spec_d)
    d_mixed_cols = inverse_dft(cmul(ga, gb, da, db, True), dft).astype(jnp.bfloat16)
    both_rows = all_to_all_seq(jnp.stack([conv_cols, d_mixed_cols]), 2, 1)
    conv_rows, d_mixed = both_rows[0], both_rows[1]
    gated_rows = (query_part * conv_rows.astype(jnp.float32)).astype(jnp.bfloat16)
    weight_rows = out_proj
    gathered, sources = all_gather_cp(gated_rows)
    mixed_out = None
    for slot in range(len(sources)):
        piece = gathered[0]
        for index in range(1, len(sources)):
            piece = jnp.where(sources[index] == slot, gathered[index], piece)
        term = jnp.einsum(
            "cr,cd->rd",
            piece,
            weight_rows[slot * local_width : (slot + 1) * local_width],
            preferred_element_type=jnp.float32,
        )
        mixed_out = term if mixed_out is None else mixed_out + term
    own_rows = lax.dynamic_slice_in_dim(embedded, group_index * local_width, local_width, 0)
    block_out = (mixed_out + own_rows.T).astype(jnp.bfloat16)
    d_query = d_gated * conv_rows.astype(jnp.float32)
    cross = cmul(sa, sb, da, db, True)
    filter_grad = inverse_dft(add_conj_flip(cross), dft)
    d_key = d_mixed.astype(jnp.float32) * value_part
    d_value = d_mixed.astype(jnp.float32) * key_part
    d_proj = jnp.stack([d_query, d_key, d_value]).astype(jnp.bfloat16)
    d_full = jnp.einsum("mcr,dmc->rd", d_proj, in_proj, preferred_element_type=jnp.float32)
    stat_part = jnp.sum(d_proj.astype(jnp.float32) * unrounded, axis=(0, 1))
    onehot_rows = onehot_t.T.astype(jnp.float32)
    weights = onehot_rows * inv_rms.T
    direct = jnp.einsum("rk,rd->kd", weights, d_full, precision=PRECISE)
    centred = jnp.einsum("rk,dr->kd", weights * stat_part[:, None], normed, precision=PRECISE)
    table_all = norm_gain[None, :] * direct - centred / model_width
    gain_all = jnp.einsum("rd,dr->d", d_full, normed, precision=PRECISE)
    partial = jnp.concatenate([table_all, gain_all[None, :]], axis=0)
    own_block = reduce_blocks_cp(partial, local_width)
    cot_table = jnp.einsum(
        "rk,rc->kc", onehot_rows, cotangent.astype(jnp.float32) * grad_scale, precision=PRECISE
    )
    own_block = own_block + jnp.concatenate(
        [cot_table, jnp.zeros((1, local_width), jnp.float32)], axis=0
    )
    summed, (block_out, filter_grad) = sum_over_seq(own_block, (block_out, filter_grad))
    kmer_grad = summed[: kmer_len * letter_count]
    gain_grad = summed[kmer_len * letter_count]
    return (
        block_out,
        filter_grad.reshape(long_filter.shape),
        kmer_grad.reshape(kmer_len, letter_count, local_width),
        gain_grad,
    )


def solution(mesh):
    in_specs = (
        P(("groups", "seq")),
        P(),
        P(),
        P(None, None, ("chan", "pair")),
        P(("chan", "pair"), "seq", None, None),
        P(None, ("chan", "pair")),
        P(("groups", "seq"), ("chan", "pair")),
    )
    out_specs = (
        P(("groups", "seq"), ("chan", "pair")),
        P(("groups", "chan", "pair"), "seq", None, None),
        P("groups", None, ("chan", "pair")),
        P(("groups", "chan", "pair")),
    )
    return jax.shard_map(
        per_device, mesh=mesh, in_specs=in_specs, out_specs=out_specs, check_vma=False
    )
```

```python
import math

import jax
import jax.numpy as jnp
import numpy as np
from jax import lax
from jax.sharding import PartitionSpec as P

NORM_EPSILON = 1e-05
PRECISE = lax.Precision.HIGHEST
TRANSFORM_PRECISION = lax.Precision.HIGH


def from_behind(value, axis, steps):
    count = lax.axis_size(axis)
    first, last = (max(0, -steps), min(count, count - steps))
    return lax.ppermute(value, axis, [(source, source + steps) for source in range(first, last)])


def dft_matrix(length):
    total = 2 * length
    inner_len = 32 if length % 32 == 0 else 1
    outer_len = length // inner_len
    j = lax.broadcasted_iota(jnp.int32, (1, total), 1)
    k = jnp.where(j < length, j, j - length)
    k = jnp.where(j == length, length, k)
    phase = jnp.where(j > length, 3 * total // 4, 0)
    scale = 2.0 * math.pi / total

    def angle(idx):
        idx = idx % total
        idx = jnp.where(idx >= length, idx - total, idx)
        return idx.astype(jnp.float32) * scale

    outer = lax.optimization_barrier(lax.broadcasted_iota(jnp.int32, (outer_len, 1), 0))
    inner = lax.optimization_barrier(lax.broadcasted_iota(jnp.int32, (inner_len, 1), 0))
    alpha = angle(outer * inner_len * k)
    beta = angle(inner * k + phase)
    ca, sa = jnp.cos(alpha), jnp.sin(alpha)
    cb, sb = jnp.cos(beta), jnp.sin(beta)
    table = ca[:, None, :] * cb[None, :, :] - sa[:, None, :] * sb[None, :, :]
    return lax.optimization_barrier(table.reshape(length, total))


def xor_exchange(x, axis, step):
    count = lax.axis_size(axis)
    return lax.ppermute(x, axis, [(i, i ^ step) for i in range(count)])


def all_gather_cp(x):
    chans, pairs = lax.axis_size("chan"), lax.axis_size("pair")
    y = x[None]
    sources = [lax.axis_index(("chan", "pair"))]
    for axis, size, stride in (("chan", chans, pairs), ("pair", pairs, 1)):
        step = 1
        while step < size:
            y = jnp.concatenate([y, xor_exchange(y, axis, step)], axis=0)
            sources = sources + [source ^ (step * stride) for source in sources]
            step *= 2
    return y, sources


def group_exchange(x, axes, count, offset):
    return lax.ppermute(x, axes, [(i, i ^ offset) for i in range(count)])


def reduce_blocks_cp(x, width):
    axes = ("chan", "pair")
    count = lax.axis_size("chan") * lax.axis_size("pair")
    me = lax.axis_index(axes)

    def pick(index):
        return lax.dynamic_slice_in_dim(x, index * width, width, 1)

    total = pick(me)
    for offset in range(1, count):
        total = total + group_exchange(pick(me ^ offset), axes, count, offset)
    return total


def sum_over_seq(x, tied):
    count = lax.axis_size("seq")
    me = lax.axis_index("seq")
    if count > 4:
        step = 1
        while step < count:
            got, tied = lax.optimization_barrier((xor_exchange(x, "seq", step), tied))
            x = x + got
            step *= 2
        return x, tied
    sent = {offset: group_exchange(x, "seq", count, offset) for offset in range(count - 1, 0, -1)}
    got = [x] + [sent[offset] for offset in range(1, count)]
    got, tied = lax.optimization_barrier((got, tied))
    total = None
    for source in range(count):
        piece = got[0]
        for offset in range(1, count):
            piece = jnp.where((me ^ source) == offset, got[offset], piece)
        total = piece if total is None else total + piece
    return total, tied


def all_to_all_seq(x, split_axis, concat_axis):
    count = lax.axis_size("seq")
    if count > 4:
        return lax.all_to_all(x, "seq", split_axis=split_axis, concat_axis=concat_axis, tiled=True)
    me = lax.axis_index("seq")
    width = x.shape[split_axis] // count
    blocks = [lax.slice_in_dim(x, j * width, (j + 1) * width, axis=split_axis) for j in range(count)]

    def pick(index):
        out = blocks[0]
        for j in range(1, count):
            out = jnp.where(index == j, blocks[j], out)
        return out

    sent = {
        offset: group_exchange(pick(me ^ offset), "seq", count, offset)
        for offset in range(count - 1, 0, -1)
    }
    got = [pick(me)] + [sent[offset] for offset in range(1, count)]
    pieces = []
    for source in range(count):
        piece = got[0]
        for offset in range(1, count):
            piece = jnp.where((me ^ source) == offset, got[offset], piece)
        pieces.append(piece)
    return jnp.concatenate(pieces, axis=concat_axis)


def forward_dft(signal, dft):
    return jnp.dot(signal.astype(jnp.float32), dft, precision=TRANSFORM_PRECISION)


def inverse_dft(spec, dft):
    length = dft.shape[0]
    total = 2 * length
    col = np.arange(total)[None, :]
    weight = np.where(col % length == 0, 1.0 / total, 2.0 / total).astype(np.float32)
    return lax.dot_general(
        spec * weight, dft, (((1,), (1,)), ((), ())), precision=TRANSFORM_PRECISION
    )


def halves(spec):
    length = spec.shape[1] // 2
    return spec[:, :length], spec[:, length:]


def first_col(shape):
    return np.arange(shape[1])[None, :] == 0


def cmul(ga, gb, xa, xb, conj_g):
    edge = first_col(ga.shape)
    sign = -1.0 if conj_g else 1.0
    ya = ga * xa - sign * (gb * xb)
    yb = ga * xb + sign * (gb * xa)
    ya = jnp.where(edge, ga * xa, ya)
    yb = jnp.where(edge, gb * xb, yb)
    return jnp.concatenate([ya, yb], axis=1)


def pair_flip(values):
    even = (np.arange(values.shape[0]) % 2 == 0)[:, None]
    up = jnp.roll(values, -1, axis=0)
    down = jnp.roll(values, 1, axis=0)
    return jnp.where(even, up, down)


def add_conj_flip(spec):
    a, b = halves(spec)
    fa, fb = halves(pair_flip(spec))
    edge = first_col(a.shape)
    return jnp.concatenate([a + fa, jnp.where(edge, b + fb, b - fb)], axis=1)


def norm_gain_local(norm_gain, group_index, local_width):
    return lax.dynamic_slice_in_dim(norm_gain, group_index * local_width, local_width, 0)


def per_device(tokens, kmer_table, norm_gain, in_proj, long_filter, out_proj, cotangent):
    row_count = tokens.shape[0]
    kmer_len, letter_count, model_width = kmer_table.shape
    local_width = in_proj.shape[2]
    length = row_count * lax.axis_size("seq")
    group_index = lax.axis_index(("chan", "pair"))
    rim_width = kmer_len - 1
    seq_count = lax.axis_size("seq")
    before = lax.ppermute(
        tokens[row_count - rim_width :], "seq", [(i, (i + 1) % seq_count) for i in range(seq_count)]
    )
    before = jnp.where(lax.axis_index("seq") == 0, -1, before)
    extended = jnp.concatenate([before, tokens])
    letters = jnp.arange(letter_count, dtype=jnp.int32)
    columns = []
    for shift_back in range(kmer_len):
        window = extended[rim_width - shift_back : rim_width - shift_back + row_count]
        columns.append(window[:, None] == letters[None, :])
    onehot_t = jnp.concatenate(columns, axis=1).T.astype(jnp.bfloat16)
    table_t = kmer_table.reshape(kmer_len * letter_count, model_width).T
    embedded = jnp.dot(table_t, onehot_t, preferred_element_type=jnp.float32)
    inv_rms = lax.rsqrt(jnp.mean(embedded * embedded, axis=0, keepdims=True) + NORM_EPSILON)
    normed = embedded * inv_rms
    scaled_normed = normed * norm_gain[:, None]
    hidden = scaled_normed.astype(jnp.bfloat16)
    projected = jnp.einsum("dr,dmc->mcr", hidden, in_proj, preferred_element_type=jnp.float32)
    residual = (scaled_normed - hidden.astype(jnp.float32)).astype(jnp.bfloat16)
    unrounded = projected + jnp.einsum(
        "dr,dmc->mcr", residual, in_proj, preferred_element_type=jnp.float32
    )
    query_part = projected[0]
    key_part = projected[1]
    value_part = projected[2]
    mixed_in = (key_part * value_part).astype(jnp.bfloat16)
    grad_scale = 1.0 / math.sqrt(length)
    groups = lax.axis_size("chan") * lax.axis_size("pair")
    gated_partial = jnp.einsum("rd,cd->rc", cotangent, out_proj, preferred_element_type=jnp.float32)
    d_gated = reduce_blocks_cp(gated_partial, local_width).T * grad_scale
    dft = dft_matrix(length)
    filter_rows = long_filter.reshape(long_filter.shape[2], long_filter.shape[3])
    spec_g = add_conj_flip(forward_dft(filter_rows, dft))
    d_conv = (d_gated * query_part).astype(jnp.bfloat16)
    both_cols = all_to_all_seq(jnp.stack([mixed_in, d_conv]), 1, 2)
    both_cols, (spec_g, dft, unrounded) = lax.optimization_barrier(
        (both_cols, (spec_g, dft, unrounded))
    )
    mixed_cols, d_cols = both_cols[0], both_cols[1]
    ga, gb = halves(spec_g)
    spec_s = forward_dft(mixed_cols, dft)
    sa, sb = halves(spec_s)
    conv_cols = inverse_dft(cmul(ga, gb, sa, sb, False), dft).astype(jnp.bfloat16)
    spec_d = forward_dft(d_cols, dft)
    da, db = halves(spec_d)
    d_mixed_cols = inverse_dft(cmul(ga, gb, da, db, True), dft).astype(jnp.bfloat16)
    both_rows = all_to_all_seq(jnp.stack([conv_cols, d_mixed_cols]), 2, 1)
    conv_rows, d_mixed = both_rows[0], both_rows[1]
    gated_rows = (query_part * conv_rows.astype(jnp.float32)).astype(jnp.bfloat16)
    weight_rows = out_proj
    gathered, sources = all_gather_cp(gated_rows)
    mixed_out = None
    offsets = [0]
    for size, stride in ((lax.axis_size("chan"), lax.axis_size("pair")), (lax.axis_size("pair"), 1)):
        step = 1
        while step < size:
            offsets = offsets + [o ^ (step * stride) for o in offsets]
            step *= 2
    position = np.zeros(len(offsets), np.int32)
    position[np.array(offsets)] = np.arange(len(offsets))
    for slot in range(len(sources)):
        piece = lax.dynamic_index_in_dim(
            gathered, jnp.asarray(position)[sources[0] ^ slot], 0, keepdims=False
        )
        term = jnp.einsum(
            "cr,cd->rd",
            piece,
            weight_rows[slot * local_width : (slot + 1) * local_width],
            preferred_element_type=jnp.float32,
        )
        mixed_out = term if mixed_out is None else mixed_out + term
    own_rows = lax.dynamic_slice_in_dim(embedded, group_index * local_width, local_width, 0)
    block_out = (mixed_out + own_rows.T).astype(jnp.bfloat16)
    d_query = d_gated * conv_rows.astype(jnp.float32)
    cross = cmul(sa, sb, da, db, True)
    filter_grad = inverse_dft(add_conj_flip(cross), dft)
    d_key = d_mixed.astype(jnp.float32) * value_part
    d_value = d_mixed.astype(jnp.float32) * key_part
    d_proj = jnp.stack([d_query, d_key, d_value]).astype(jnp.bfloat16)
    d_full = jnp.einsum("mcr,dmc->rd", d_proj, in_proj, preferred_element_type=jnp.float32)
    stat_part = jnp.sum(d_proj.astype(jnp.float32) * unrounded, axis=(0, 1))
    onehot_rows = onehot_t.T.astype(jnp.float32)
    weights = onehot_rows * inv_rms.T
    direct = jnp.einsum("rk,rd->kd", weights, d_full, precision=PRECISE)
    centred = jnp.einsum("rk,dr->kd", weights * stat_part[:, None], normed, precision=PRECISE)
    table_all = norm_gain[None, :] * direct - centred / model_width
    gain_all = jnp.einsum("rd,dr->d", d_full, normed, precision=PRECISE)
    partial = jnp.concatenate([table_all, gain_all[None, :]], axis=0)
    own_block = reduce_blocks_cp(partial, local_width)
    cot_table = jnp.einsum(
        "rk,rc->kc", onehot_rows, cotangent.astype(jnp.float32) * grad_scale, precision=PRECISE
    )
    own_block = own_block + jnp.concatenate(
        [cot_table, jnp.zeros((1, local_width), jnp.float32)], axis=0
    )
    summed, (block_out, filter_grad) = sum_over_seq(own_block, (block_out, filter_grad))
    kmer_grad = summed[: kmer_len * letter_count]
    gain_grad = summed[kmer_len * letter_count]
    return (
        block_out,
        filter_grad.reshape(long_filter.shape),
        kmer_grad.reshape(kmer_len, letter_count, local_width),
        gain_grad,
    )


def solution(mesh):
    in_specs = (
        P(("groups", "seq")),
        P(),
        P(),
        P(None, None, ("chan", "pair")),
        P(("chan", "pair"), "seq", None, None),
        P(None, ("chan", "pair")),
        P(("groups", "seq"), ("chan", "pair")),
    )
    out_specs = (
        P(("groups", "seq"), ("chan", "pair")),
        P(("groups", "chan", "pair"), "seq", None, None),
        P("groups", None, ("chan", "pair")),
        P(("groups", "chan", "pair")),
    )
    return jax.shard_map(
        per_device, mesh=mesh, in_specs=in_specs, out_specs=out_specs, check_vma=False
    )
```
